128 devices in a mesh: gx: 8 (over z, x_lo), gy: 8 (over y, x_hi), gz: 2 (over core).
Axes of the slice: x: 4 (x_hi: 2, x_lo: 2; x = x_hi * 2 + x_lo), y: 4, z: 4, core: 2. Of those that a mesh axis runs over, the one named last changes fastest.
Arguments:
- populations: float32 [19, 64, 16, 1024], P(None, 'gx', 'gz', 'gy'), may hold values from 0.01 to 0.2
- le_shift: int32 [2], replicated, may hold values from 0 to 1023
- le_frac: int32 [2], replicated, may hold values from 0 to 255
- links: int32 [64, 16, 256], P('gx', 'gz', 'gy'), may hold values from 1 to 19455, as said below
Outputs:
- final_states: float32 [19, 64, 16, 1024], P(None, 'gx', 'gz', 'gy')
- final_density: float32 [64, 16, 1024], P('gx', 'gz', 'gy')
The draws below stay inside these ranges and needn't reach their ends.
Inputs may be any that keep to these rules, and one draw needn't show every extreme that they name: `links`: each entry is y * 19 + m with m from 1 to 18; the entries in columns b * 32 to (b + 1) * 32 - 1 have y from b * 128 to (b + 1) * 128 - 1.
All inputs are finite; a program needn't handle non-finite values.
Results may differ from the reference program's by a relative error of at most 0.00002.
Values sent between devices are 32-bit elements; how exact they have to be, the bound alone decides.
No kernel may reach another device: no remote copies, remote signals or barrier semaphores. Data moves between devices by JAX's collectives and lax.ppermute only.
A program may use at most 64 MiB of HBM per device.

```python
import jax
import jax.numpy as jnp
import numpy as np
from jax import lax

CX = 8
CY = 128
LROW = 32
STEPS = 2
NX = 64
NY = 1024
NZ = 16
LINKS_ROW = 256
N_GX = 8


def draw_links(key, part):
    key_cell, key_member = jax.random.split(jax.random.fold_in(key, 11))
    column = lax.broadcasted_iota(jnp.int32, (NX, NZ, LINKS_ROW), 2)
    block = column // LROW
    cell = jax.random.randint(key_cell, (NX, NZ, LINKS_ROW), 0, CY)
    member = jax.random.randint(key_member, (NX, NZ, LINKS_ROW), 1, 19)
    return ((block * CY + cell) * 19 + member).astype(jnp.int32)


def steps_of(key, dims, cuts, least, largest):
    factor_of = 1.0
    for axis_at, blocks in cuts:
        steps = jax.random.uniform(jax.random.fold_in(jax.random.fold_in(key, 6), axis_at), (blocks,), jnp.float32, least / len(cuts), largest / len(cuts))
        factor_of = factor_of * jnp.repeat(jnp.exp(steps), dims[axis_at] // blocks).reshape((-1,) + (1,) * (len(dims) - 1 - axis_at))
    return factor_of


def setup_inputs(seed: int = 0) -> dict:
    splits = jax.random.split(jax.random.key(seed), 5)
    return {
        "populations": jnp.clip(0.01 + 0.19 * jax.random.uniform(splits[0], (19, NX, NZ, NY), jnp.float32) ** steps_of(splits[0], (19, NX, NZ, NY), ((1, 8), (2, 2), (3, 8)), -0.2, 0.2), 0.01, 0.2),
        "le_shift": jax.random.randint(splits[1], (STEPS,), 0, NY).astype(jnp.int32),
        "le_frac": jax.random.randint(splits[2], (STEPS,), 0, 256).astype(jnp.int32),
        "links": draw_links(jax.random.fold_in(splits[4], 71), 0),
    }


velocity_table = ((0, 0, 0), (1, 0, 0), (-1, 0, 0), (0, 1, 0), (0, -1, 0), (0, 0, 1), (0, 0, -1), (1, 1, 0), (-1, -1, 0), (1, -1, 0), (-1, 1, 0), (1, 0, 1), (-1, 0, -1), (1, 0, -1), (-1, 0, 1), (0, 1, 1), (0, -1, -1), (0, 1, -1), (0, -1, 1))
weight_table = (1.0 / 3.0,) + (1.0 / 18.0,) * 6 + (1.0 / 36.0,) * 12
upward = (1, 7, 9, 11, 13)
downward = (2, 8, 10, 12, 14)
relax_rate = 1.25
plane_speed = 0.08


def total_density(states):
    density = states[0]
    for member in range(1, 19):
        density = density + states[member]
    return density


def moments(states):
    density = total_density(states)
    velocity = []
    for dim_index in range(3):
        momentum = None
        for member in range(19):
            sign_part = velocity_table[member][dim_index]
            if sign_part == 1:
                momentum = states[member] if momentum is None else momentum + states[member]
            elif sign_part == -1:
                momentum = -states[member] if momentum is None else momentum - states[member]
        velocity.append(momentum / density)
    return density, velocity


def speed_square(velocity):
    return velocity[0] * velocity[0] + velocity[1] * velocity[1] + velocity[2] * velocity[2]


def equilibrium(member, density, velocity, speed_sq):
    projected = None
    for dim_index in range(3):
        sign_part = velocity_table[member][dim_index]
        if sign_part != 0:
            summand = velocity[dim_index] if sign_part > 0 else -velocity[dim_index]
            projected = summand if projected is None else projected + summand
    if projected is None:
        return weight_table[member] * density * (1.0 - 1.5 * speed_sq)
    return weight_table[member] * density * (1.0 + 3.0 * projected + 4.5 * projected * projected - 1.5 * speed_sq)


def relax(states):
    density, velocity = moments(states)
    speed_sq = speed_square(velocity)
    return jnp.stack([states[member] + relax_rate * (equilibrium(member, density, velocity, speed_sq) - states[member]) for member in range(19)])


def corrected(plane, members, sign_part):
    density, velocity = moments(plane)
    speed_sq = speed_square(velocity)
    moved = [velocity[0], velocity[1] + sign_part * plane_speed, velocity[2]]
    moved_sq = speed_square(moved)
    return jnp.stack([plane[member] + equilibrium(member, density, moved, moved_sq) - equilibrium(member, density, velocity, speed_sq) for member in members])


def reference(populations, le_shift, le_frac, links):
    states = populations
    x_index = lax.broadcasted_iota(jnp.int32, links.shape, 0)
    z_index = lax.broadcasted_iota(jnp.int32, links.shape, 1)
    cell_y = (links // 19).astype(jnp.int32)
    direction = (links % 19).astype(jnp.int32)
    reverse = direction - 1 + 2 * (direction % 2)
    for section in range(STEPS):
        relaxed = relax(states)
        offset = le_shift[section]
        fraction = le_frac[section].astype(jnp.float32) / 256.0
        keep = 1.0 - fraction
        slab_view = relaxed.reshape(19, N_GX, CX, NZ, NY)
        top_out = corrected(slab_view[:, :, CX - 1], upward, -1.0)
        bottom = corrected(slab_view[:, :, 0], downward, 1.0)
        low_ghost = keep * jnp.roll(top_out, offset, axis=3) + fraction * jnp.roll(top_out, offset + 1, axis=3)
        high_ghost = fraction * jnp.roll(bottom, -(offset + 1), axis=3) + keep * jnp.roll(bottom, -offset, axis=3)
        low_ghost = jnp.roll(low_ghost, 1, axis=1)
        high_ghost = jnp.roll(high_ghost, -1, axis=1)
        empty = jnp.zeros((19, N_GX, NZ, NY), jnp.float32)
        low_plane = empty.at[np.array(upward)].set(low_ghost)
        high_plane = empty.at[np.array(downward)].set(high_ghost)
        extended = jnp.concatenate([low_plane[:, :, None], slab_view, high_plane[:, :, None]], axis=2)
        pulled = []
        for member in range(19):
            step_x, step_y, step_z = velocity_table[member]
            moved = jnp.roll(extended[member], (step_z, step_y), axis=(2, 3))
            pulled.append(moved[:, 1 - step_x:1 - step_x + CX].reshape(NX, NZ, NY))
        read = jnp.stack(pulled)
        states = read.at[reverse, x_index, z_index, cell_y].set(relaxed[direction, x_index, z_index, cell_y])
    return states, total_density(states)
```

```python
import jax
import jax.numpy as jnp
import numpy as np
from jax import lax
from jax.sharding import PartitionSpec as P

STEPS = 2


velocity_table = (
    (0, 0, 0),
    (1, 0, 0),
    (-1, 0, 0),
    (0, 1, 0),
    (0, -1, 0),
    (0, 0, 1),
    (0, 0, -1),
    (1, 1, 0),
    (-1, -1, 0),
    (1, -1, 0),
    (-1, 1, 0),
    (1, 0, 1),
    (-1, 0, -1),
    (1, 0, -1),
    (-1, 0, 1),
    (0, 1, 1),
    (0, -1, -1),
    (0, 1, -1),
    (0, -1, 1),
)
weight_table = (1.0 / 3.0,) + (1.0 / 18.0,) * 6 + (1.0 / 36.0,) * 12
upward = (1, 7, 9, 11, 13)
downward = (2, 8, 10, 12, 14)
y_plus = tuple(m for m in range(19) if velocity_table[m][1] == 1)
y_minus = tuple(m for m in range(19) if velocity_table[m][1] == -1)
relax_rate = 1.25
plane_speed = 0.08


def total_density(states):
    density = states[0]
    for member in range(1, 19):
        density = density + states[member]
    return density


def moments(states):
    density = total_density(states)
    velocity = []
    for dim_index in range(3):
        momentum = None
        for member in range(19):
            sign_part = velocity_table[member][dim_index]
            if sign_part == 1:
                momentum = states[member] if momentum is None else momentum + states[member]
            elif sign_part == -1:
                momentum = momentum - states[member]
        velocity.append(momentum / density)
    return (density, velocity)


def speed_square(velocity):
    return velocity[0] * velocity[0] + velocity[1] * velocity[1] + velocity[2] * velocity[2]


def equilibrium(member, density, velocity, speed_sq):
    projected = None
    for dim_index in range(3):
        sign_part = velocity_table[member][dim_index]
        if sign_part != 0:
            summand = velocity[dim_index] if sign_part > 0 else -velocity[dim_index]
            projected = summand if projected is None else projected + summand
    if projected is None:
        return weight_table[member] * density * (1.0 - 1.5 * speed_sq)
    return (
        weight_table[member]
        * density
        * (1.0 + 3.0 * projected + 4.5 * projected * projected - 1.5 * speed_sq)
    )


def relax(states):
    density, velocity = moments(states)
    speed_sq = speed_square(velocity)
    return [
        states[member]
        + relax_rate * (equilibrium(member, density, velocity, speed_sq) - states[member])
        for member in range(19)
    ]


def corrected(plane, members, sign_part):
    density, velocity = moments(plane)
    speed_sq = speed_square(velocity)
    moved = [velocity[0], velocity[1] + sign_part * plane_speed, velocity[2]]
    moved_sq = speed_square(moved)
    return jnp.stack(
        [
            plane[member]
            + equilibrium(member, density, moved, moved_sq)
            - equilibrium(member, density, velocity, speed_sq)
            for member in members
        ]
    )


def link_hits(links, anchor, row_span):
    cell_y = links // 19 - anchor
    member = links % 19
    by_member = (member[:, :, None, :] == jnp.arange(19, dtype=jnp.int32)[:, None]).astype(jnp.bfloat16)
    by_cell = (cell_y[:, :, :, None] == jnp.arange(row_span, dtype=jnp.int32)).astype(jnp.bfloat16)
    counts = jnp.einsum("xzml,xzly->mxzy", by_member, by_cell, preferred_element_type=jnp.float32)
    return counts > 0.5


def per_device(populations, le_shift, le_frac, links):
    n_members, slab_width, half_depth, row_span = populations.shape
    flow_cycle = lax.axis_size("gy")
    slab_cycle = lax.axis_size("gx")
    flow_cells = row_span * flow_cycle
    me_y = lax.axis_index("gy")
    me_z = lax.axis_index("gz")
    anchor = me_y * row_span

    size = populations.size
    packed = jnp.concatenate([populations.reshape(-1), links.astype(jnp.float32).reshape(-1)])
    other = lax.ppermute(packed, "gz", [(0, 1), (1, 0)])
    other_states = other[:size].reshape(populations.shape)
    other_links = other[size:].reshape(links.shape).astype(jnp.int32)
    first = me_z == 0
    states = jnp.where(
        first,
        jnp.concatenate([populations, other_states], axis=2),
        jnp.concatenate([other_states, populations], axis=2),
    )
    all_links = jnp.where(
        first, jnp.concatenate([links, other_links], axis=1), jnp.concatenate([other_links, links], axis=1)
    )
    depth = 2 * half_depth
    hits = link_hits(all_links, anchor, row_span)

    peer = lax.broadcasted_iota(jnp.int32, (flow_cycle, 1), 0)
    to_next = peer == (me_y + 1) % flow_cycle
    to_prev = peer == (me_y - 1 + flow_cycle) % flow_cycle
    face_size = 2 * 5 * depth * row_span
    span = row_span + 2

    for section in range(STEPS):
        relaxed = relax([states[m] for m in range(n_members)])
        offset = le_shift[section]
        fraction = le_frac[section].astype(jnp.float32) / 256.0
        keep = 1.0 - fraction
        top = corrected([r[slab_width - 1] for r in relaxed], upward, -1.0)
        bottom = corrected([r[0] for r in relaxed], downward, 1.0)
        faces = jnp.stack([top, bottom]).reshape(1, -1)
        up_rim = jnp.stack([relaxed[m][:, :, row_span - 1] for m in y_plus]).reshape(1, -1)
        down_rim = jnp.stack([relaxed[m][:, :, 0] for m in y_minus]).reshape(1, -1)
        rim = jnp.where(to_next, up_rim, jnp.where(to_prev, down_rim, 0.0))
        chunks = jnp.concatenate([jnp.broadcast_to(faces, (flow_cycle, face_size)), rim], axis=1)
        got = lax.all_to_all(chunks, "gy", 0, 0, tiled=True)
        rim_low = lax.dynamic_index_in_dim(got, (me_y - 1 + flow_cycle) % flow_cycle, 0, keepdims=False)
        rim_high = lax.dynamic_index_in_dim(got, (me_y + 1) % flow_cycle, 0, keepdims=False)
        rim_low = rim_low[face_size:].reshape(5, slab_width, depth)
        rim_high = rim_high[face_size:].reshape(5, slab_width, depth)
        whole = got[:, :face_size].reshape(flow_cycle, 2, 5, depth, row_span)
        whole = jnp.moveaxis(whole, 0, 3).reshape(2, 5, depth, flow_cells)
        whole = jnp.concatenate([whole, whole[..., : span + 1]], axis=3)
        low_start = (anchor - offset - 2 + 2 * flow_cells) % flow_cells
        high_start = (anchor + offset - 1 + flow_cells) % flow_cells
        low_window = lax.dynamic_slice_in_dim(whole[0], low_start, span + 1, 2)
        high_window = lax.dynamic_slice_in_dim(whole[1], high_start, span + 1, 2)
        low_send = keep * low_window[:, :, 1:] + fraction * low_window[:, :, :-1]
        high_send = fraction * high_window[:, :, 1:] + keep * high_window[:, :, :-1]
        low_ghost = lax.ppermute(low_send, "gx", [(i, (i + 1) % slab_cycle) for i in range(slab_cycle)])
        high_ghost = lax.ppermute(high_send, "gx", [(i, (i - 1) % slab_cycle) for i in range(slab_cycle)])

        result = []
        for member in range(n_members):
            step_x, step_y, step_z = velocity_table[member]
            cells = relaxed[member]
            if step_y == 1:
                cells = jnp.concatenate([rim_low[y_plus.index(member)][:, :, None], cells[:, :, : row_span - 1]], axis=2)
            elif step_y == -1:
                cells = jnp.concatenate([cells[:, :, 1:], rim_high[y_minus.index(member)][:, :, None]], axis=2)
            if step_x == 1:
                ghost = low_ghost[upward.index(member), :, 1 - step_y : 1 - step_y + row_span]
                cells = jnp.concatenate([ghost[None], cells[: slab_width - 1]], axis=0)
            elif step_x == -1:
                ghost = high_ghost[downward.index(member), :, 1 - step_y : 1 - step_y + row_span]
                cells = jnp.concatenate([cells[1:], ghost[None]], axis=0)
            if step_z != 0:
                cells = jnp.roll(cells, step_z, axis=1)
            result.append(cells)
        bounced = [result[0]]
        for member in range(1, n_members):
            source = member - 1 + 2 * (member % 2)
            bounced.append(jnp.where(hits[source], relaxed[source], result[member]))
        states = jnp.stack(bounced)

    final = lax.dynamic_slice_in_dim(states, me_z * half_depth, half_depth, axis=2)
    return (final, total_density(final))


def solution(mesh):
    in_specs = (P(None, "gx", "gz", "gy"), P(), P(), P("gx", "gz", "gy"))
    out_specs = (P(None, "gx", "gz", "gy"), P("gx", "gz", "gy"))
    return jax.shard_map(
        per_device, mesh=mesh, in_specs=in_specs, out_specs=out_specs, check_vma=False
    )
```

```python
import jax
import jax.numpy as jnp
import numpy as np
from jax import lax
from jax.sharding import PartitionSpec as P
from jax.experimental import pallas as pl
from jax.experimental.pallas import tpu as pltpu

STEPS = 2


velocity_table = (
    (0, 0, 0),
    (1, 0, 0),
    (-1, 0, 0),
    (0, 1, 0),
    (0, -1, 0),
    (0, 0, 1),
    (0, 0, -1),
    (1, 1, 0),
    (-1, -1, 0),
    (1, -1, 0),
    (-1, 1, 0),
    (1, 0, 1),
    (-1, 0, -1),
    (1, 0, -1),
    (-1, 0, 1),
    (0, 1, 1),
    (0, -1, -1),
    (0, 1, -1),
    (0, -1, 1),
)
weight_table = (1.0 / 3.0,) + (1.0 / 18.0,) * 6 + (1.0 / 36.0,) * 12
upward = (1, 7, 9, 11, 13)
downward = (2, 8, 10, 12, 14)
y_plus = tuple(m for m in range(19) if velocity_table[m][1] == 1)
y_minus = tuple(m for m in range(19) if velocity_table[m][1] == -1)
relax_rate = 1.25
plane_speed = 0.08


def total_density(states):
    density = states[0]
    for member in range(1, 19):
        density = density + states[member]
    return density


def moments(states):
    density = total_density(states)
    velocity = []
    for dim_index in range(3):
        momentum = None
        for member in range(19):
            sign_part = velocity_table[member][dim_index]
            if sign_part == 1:
                momentum = states[member] if momentum is None else momentum + states[member]
            elif sign_part == -1:
                momentum = momentum - states[member]
        velocity.append(momentum / density)
    return (density, velocity)


def speed_square(velocity):
    return velocity[0] * velocity[0] + velocity[1] * velocity[1] + velocity[2] * velocity[2]


def equilibrium(member, density, velocity, speed_sq):
    projected = None
    for dim_index in range(3):
        sign_part = velocity_table[member][dim_index]
        if sign_part != 0:
            summand = velocity[dim_index] if sign_part > 0 else -velocity[dim_index]
            projected = summand if projected is None else projected + summand
    if projected is None:
        return weight_table[member] * density * (1.0 - 1.5 * speed_sq)
    return (
        weight_table[member]
        * density
        * (1.0 + 3.0 * projected + 4.5 * projected * projected - 1.5 * speed_sq)
    )


def relax(states):
    density, velocity = moments(states)
    speed_sq = speed_square(velocity)
    return [
        states[member]
        + relax_rate * (equilibrium(member, density, velocity, speed_sq) - states[member])
        for member in range(19)
    ]


def corrected(plane, members, sign_part):
    density, velocity = moments(plane)
    speed_sq = speed_square(velocity)
    moved = [velocity[0], velocity[1] + sign_part * plane_speed, velocity[2]]
    moved_sq = speed_square(moved)
    return jnp.stack(
        [
            plane[member]
            + equilibrium(member, density, moved, moved_sq)
            - equilibrium(member, density, velocity, speed_sq)
            for member in members
        ]
    )


def link_hits(links, anchor, row_span):
    cell_y = links // 19 - anchor
    member = links % 19
    by_member = (member[:, :, None, :] == jnp.arange(19, dtype=jnp.int32)[:, None]).astype(jnp.bfloat16)
    by_cell = (cell_y[:, :, :, None] == jnp.arange(row_span, dtype=jnp.int32)).astype(jnp.bfloat16)
    return jnp.einsum("xzml,xzly->mxzy", by_member, by_cell, preferred_element_type=jnp.float32)


LANES = 128
FACE_ROWS = 2 * 5


def _roll(t, shift, axis):
    if isinstance(shift, int):
        shift = shift % t.shape[axis]
        if shift == 0:
            return t
    return pltpu.roll(t, shift, axis)


def _z_roll(t, step):
    half = t.shape[0] // 2
    a, b = t[:half], t[half:]
    row = lax.broadcasted_iota(jnp.int32, a.shape, 0)
    if step == 1:
        ra, rb = _roll(a, 1, 0), _roll(b, 1, 0)
        edge = row == 0
    else:
        ra, rb = _roll(a, half - 1, 0), _roll(b, half - 1, 0)
        edge = row == half - 1
    return jnp.concatenate([jnp.where(edge, rb, ra), jnp.where(edge, ra, rb)], axis=0)


def _emit_relax(cells_of_x, slab_width, relaxed_ref, chunk_ref, sc_ref, depth):
    lane = lax.broadcasted_iota(jnp.int32, (depth, LANES), 1)
    up_pack = jnp.zeros((depth, LANES), jnp.float32)
    down_pack = jnp.zeros((depth, LANES), jnp.float32)
    top = bottom = None
    for x in range(slab_width):
        r = relax(cells_of_x(x))
        for m in range(19):
            relaxed_ref[m, x] = r[m]
        if x == slab_width - 1:
            top = corrected(r, upward, -1.0)
        if x == 0:
            bottom = corrected(r, downward, 1.0)
        for i, m in enumerate(y_plus):
            k = i * slab_width + x
            up_pack = jnp.where(lane == k, _roll(r[m], k + 1, 1), up_pack)
        for i, m in enumerate(y_minus):
            k = i * slab_width + x
            down_pack = jnp.where(lane == k, _roll(r[m], k, 1), down_pack)
    faces = jnp.concatenate([top.reshape(5 * depth, LANES), bottom.reshape(5 * depth, LANES)], axis=0)
    to_next = jnp.full((depth, LANES), sc_ref[1], jnp.int32)
    to_prev = jnp.full((depth, LANES), sc_ref[2], jnp.int32)
    peers = chunk_ref.shape[0]
    for p in range(peers):
        chunk_ref[p, : FACE_ROWS * depth] = faces
        chunk_ref[p, FACE_ROWS * depth :] = jnp.where(to_next == p, up_pack, jnp.where(to_prev == p, down_pack, 0.0))


def _streamed(x, slab_width, relaxed_ref, rims_ref, low_ref, high_ref, hits_ref, depth):
    lane = lax.broadcasted_iota(jnp.int32, (depth, LANES), 1)
    out = []
    for n in range(19):
        step_x, step_y, step_z = velocity_table[n]
        xs = x - step_x
        if xs < 0:
            t = low_ref[upward.index(n)]
        elif xs >= slab_width:
            t = high_ref[downward.index(n)]
        else:
            t = relaxed_ref[n, xs]
            if step_y == 1:
                k = y_plus.index(n) * slab_width + xs
                t = jnp.where(lane == 0, _roll(rims_ref[0], LANES - k, 1), _roll(t, 1, 1))
            elif step_y == -1:
                k = y_minus.index(n) * slab_width + xs
                t = jnp.where(lane == LANES - 1, _roll(rims_ref[1], LANES - 1 - k, 1), _roll(t, LANES - 1, 1))
        if step_z != 0:
            t = _z_roll(t, step_z)
        out.append(t)
    result = [out[0]]
    for n in range(1, 19):
        source = n - 1 + 2 * (n % 2)
        result.append(jnp.where(hits_ref[source, x] > 0.5, relaxed_ref[source, x], out[n]))
    return result


def _first_kernel(sc_ref, states_ref, relaxed_ref, chunk_ref):
    slab_width, depth = states_ref.shape[1], states_ref.shape[2]
    _emit_relax(lambda x: [states_ref[m, x] for m in range(19)], slab_width, relaxed_ref, chunk_ref, sc_ref, depth)


def _middle_kernel(sc_ref, relaxed_ref, rims_ref, low_ref, high_ref, hits_ref, next_ref, chunk_ref):
    slab_width, depth = relaxed_ref.shape[1], relaxed_ref.shape[2]
    cells = lambda x: _streamed(x, slab_width, relaxed_ref, rims_ref, low_ref, high_ref, hits_ref, depth)
    _emit_relax(cells, slab_width, next_ref, chunk_ref, sc_ref, depth)


def _last_kernel(sc_ref, relaxed_ref, rims_ref, low_ref, high_ref, hits_ref, out_ref, density_ref):
    slab_width, depth = relaxed_ref.shape[1], relaxed_ref.shape[2]
    half = depth // 2
    lower = jnp.full((half, LANES), sc_ref[3], jnp.int32) == 0
    for x in range(slab_width):
        cells = _streamed(x, slab_width, relaxed_ref, rims_ref, low_ref, high_ref, hits_ref, depth)
        mine = [jnp.where(lower, c[:half], c[half:]) for c in cells]
        for m in range(19):
            out_ref[m, x] = mine[m]
        density_ref[x] = total_density(mine)


def _window_kernel(sc_ref, mix_ref, got_ref, send_ref, rims_ref):
    peers, _, lanes = got_ref.shape
    depth = send_ref.shape[2]
    me_y, offset = sc_ref[0], sc_ref[4]
    fraction, keep = mix_ref[0], mix_ref[1]
    flow_cells = peers * lanes
    anchor = me_y * lanes
    lane = lax.broadcasted_iota(jnp.int32, (depth, lanes), 1)

    def window(row0, start):
        start = (start + 2 * flow_cells) % flow_cells
        block = start // lanes
        off = start % lanes
        after = (block + 1) % peers
        shift = (lanes - off) % lanes
        first = pltpu.roll(got_ref[block, pl.ds(row0, depth), :], shift, 1)
        second = pltpu.roll(got_ref[after, pl.ds(row0, depth), :], shift, 1)
        return jnp.where(lane < lanes - off, first, second)

    for i, m in enumerate(upward):
        step_y = velocity_table[m][1]
        row0 = i * depth
        a = anchor - offset - step_y
        send_ref[0, i] = keep * window(row0, a) + fraction * window(row0, a - 1)
    for i, m in enumerate(downward):
        step_y = velocity_table[m][1]
        row0 = (5 + i) * depth
        c = anchor + offset - step_y
        send_ref[1, i] = fraction * window(row0, c + 1) + keep * window(row0, c)
    rims_ref[0] = got_ref[sc_ref[2], pl.ds(FACE_ROWS * depth, depth), :]
    rims_ref[1] = got_ref[sc_ref[1], pl.ds(FACE_ROWS * depth, depth), :]


def _vmem():
    return pl.BlockSpec(memory_space=pltpu.VMEM)


def _smem():
    return pl.BlockSpec(memory_space=pltpu.SMEM)


def _call(kernel, n_smem, n_vmem, out_shapes):
    return pl.pallas_call(
        kernel,
        out_shape=out_shapes,
        in_specs=[_smem()] * n_smem + [_vmem()] * n_vmem,
        out_specs=tuple(_vmem() for _ in out_shapes),
    )


def per_device(populations, le_shift, le_frac, links):
    n_members, slab_width, half_depth, row_span = populations.shape
    flow_cycle = lax.axis_size("gy")
    slab_cycle = lax.axis_size("gx")
    me_y = lax.axis_index("gy")
    me_z = lax.axis_index("gz")
    anchor = me_y * row_span

    size = populations.size
    packed = jnp.concatenate([populations.reshape(-1), links.astype(jnp.float32).reshape(-1)])
    other = lax.ppermute(packed, "gz", [(0, 1), (1, 0)])
    other_states = other[:size].reshape(populations.shape)
    other_links = other[size:].reshape(links.shape).astype(jnp.int32)
    first = me_z == 0
    states = jnp.where(
        first,
        jnp.concatenate([populations, other_states], axis=2),
        jnp.concatenate([other_states, populations], axis=2),
    )
    all_links = jnp.where(
        first, jnp.concatenate([links, other_links], axis=1), jnp.concatenate([other_links, links], axis=1)
    )
    depth = 2 * half_depth
    hits = link_hits(all_links, anchor, row_span)

    f32 = jnp.float32
    full = jax.ShapeDtypeStruct((n_members, slab_width, depth, row_span), f32)
    chunk = jax.ShapeDtypeStruct((flow_cycle, (FACE_ROWS + 1) * depth, row_span), f32)
    send = jax.ShapeDtypeStruct((2, 5, depth, row_span), f32)
    rims = jax.ShapeDtypeStruct((2, depth, row_span), f32)
    own = jax.ShapeDtypeStruct((n_members, slab_width, half_depth, row_span), f32)
    density = jax.ShapeDtypeStruct((slab_width, half_depth, row_span), f32)

    relaxed, chunks = None, None
    for section in range(STEPS):
        scalars = jnp.stack(
            [me_y, (me_y + 1) % flow_cycle, (me_y - 1 + flow_cycle) % flow_cycle, me_z, le_shift[section]]
        ).astype(jnp.int32)
        fraction = le_frac[section].astype(f32) / 256.0
        mix = jnp.stack([fraction, 1.0 - fraction])
        if section == 0:
            relaxed, chunks = _call(_first_kernel, 1, 1, (full, chunk))(scalars, states)
        got = lax.all_to_all(chunks, "gy", 0, 0, tiled=True)
        sends, rim_pair = _call(_window_kernel, 2, 1, (send, rims))(scalars, mix, got)
        low_ghost = lax.ppermute(sends[0], "gx", [(i, (i + 1) % slab_cycle) for i in range(slab_cycle)])
        high_ghost = lax.ppermute(sends[1], "gx", [(i, (i - 1) % slab_cycle) for i in range(slab_cycle)])
        if section + 1 < STEPS:
            relaxed, chunks = _call(_middle_kernel, 1, 5, (full, chunk))(
                scalars, relaxed, rim_pair, low_ghost, high_ghost, hits
            )
        else:
            final, dens = _call(_last_kernel, 1, 5, (own, density))(
                scalars, relaxed, rim_pair, low_ghost, high_ghost, hits
            )
    return (final, dens)


def solution(mesh):
    in_specs = (P(None, "gx", "gz", "gy"), P(), P(), P("gx", "gz", "gy"))
    out_specs = (P(None, "gx", "gz", "gy"), P("gx", "gz", "gy"))
    return jax.shard_map(
        per_device, mesh=mesh, in_specs=in_specs, out_specs=out_specs, check_vma=False
    )
```

```python
import functools

import jax
import jax.numpy as jnp
import numpy as np
from jax import lax
from jax.sharding import PartitionSpec as P
from jax.experimental import pallas as pl
from jax.experimental.pallas import tpu as pltpu

STEPS = 2


velocity_table = (
    (0, 0, 0),
    (1, 0, 0),
    (-1, 0, 0),
    (0, 1, 0),
    (0, -1, 0),
    (0, 0, 1),
    (0, 0, -1),
    (1, 1, 0),
    (-1, -1, 0),
    (1, -1, 0),
    (-1, 1, 0),
    (1, 0, 1),
    (-1, 0, -1),
    (1, 0, -1),
    (-1, 0, 1),
    (0, 1, 1),
    (0, -1, -1),
    (0, 1, -1),
    (0, -1, 1),
)
weight_table = (1.0 / 3.0,) + (1.0 / 18.0,) * 6 + (1.0 / 36.0,) * 12
upward = (1, 7, 9, 11, 13)
downward = (2, 8, 10, 12, 14)
y_plus = tuple(m for m in range(19) if velocity_table[m][1] == 1)
y_minus = tuple(m for m in range(19) if velocity_table[m][1] == -1)
relax_rate = 1.25
plane_speed = 0.08


def total_density(states):
    density = states[0]
    for member in range(1, 19):
        density = density + states[member]
    return density


def moments(states):
    density = total_density(states)
    velocity = []
    for dim_index in range(3):
        momentum = None
        for member in range(19):
            sign_part = velocity_table[member][dim_index]
            if sign_part == 1:
                momentum = states[member] if momentum is None else momentum + states[member]
            elif sign_part == -1:
                momentum = momentum - states[member]
        velocity.append(momentum / density)
    return (density, velocity)


def speed_square(velocity):
    return velocity[0] * velocity[0] + velocity[1] * velocity[1] + velocity[2] * velocity[2]


def equilibrium(member, density, velocity, speed_sq):
    projected = None
    for dim_index in range(3):
        sign_part = velocity_table[member][dim_index]
        if sign_part != 0:
            summand = velocity[dim_index] if sign_part > 0 else -velocity[dim_index]
            projected = summand if projected is None else projected + summand
    if projected is None:
        return weight_table[member] * density * (1.0 - 1.5 * speed_sq)
    return (
        weight_table[member]
        * density
        * (1.0 + 3.0 * projected + 4.5 * projected * projected - 1.5 * speed_sq)
    )


def relax(states):
    density, velocity = moments(states)
    speed_sq = speed_square(velocity)
    return [
        states[member]
        + relax_rate * (equilibrium(member, density, velocity, speed_sq) - states[member])
        for member in range(19)
    ]


def corrected(plane, members, sign_part):
    density, velocity = moments(plane)
    speed_sq = speed_square(velocity)
    moved = [velocity[0], velocity[1] + sign_part * plane_speed, velocity[2]]
    moved_sq = speed_square(moved)
    return jnp.stack(
        [
            plane[member]
            + equilibrium(member, density, moved, moved_sq)
            - equilibrium(member, density, velocity, speed_sq)
            for member in members
        ]
    )


def link_hits(links, anchor, row_span):
    cell_y = links // 19 - anchor
    member = links % 19
    by_member = (member[:, :, None, :] == jnp.arange(19, dtype=jnp.int32)[:, None]).astype(jnp.bfloat16)
    by_cell = (cell_y[:, :, :, None] == jnp.arange(row_span, dtype=jnp.int32)).astype(jnp.bfloat16)
    return jnp.einsum("xzml,xzly->mxzy", by_member, by_cell, preferred_element_type=jnp.float32)


LANES = 128
FACE_ROWS = 2 * 5


def _roll(t, shift, axis):
    if isinstance(shift, int):
        shift = shift % t.shape[axis]
        if shift == 0:
            return t
    return pltpu.roll(t, shift, axis)


def _z_roll(t, step):
    half = t.shape[0] // 2
    a, b = t[:half], t[half:]
    row = lax.broadcasted_iota(jnp.int32, a.shape, 0)
    if step == 1:
        ra, rb = _roll(a, 1, 0), _roll(b, 1, 0)
        edge = row == 0
    else:
        ra, rb = _roll(a, half - 1, 0), _roll(b, half - 1, 0)
        edge = row == half - 1
    return jnp.concatenate([jnp.where(edge, rb, ra), jnp.where(edge, ra, rb)], axis=0)


def _positions():
    flow_cycle = lax.axis_size("gy")
    me_y = lax.axis_index("gy")
    return me_y, (me_y + 1) % flow_cycle, (me_y - 1 + flow_cycle) % flow_cycle, lax.axis_index("gz")


def _emit_relax(cells_of_x, slab_width, relaxed_ref, chunk_ref, depth):
    lane = lax.broadcasted_iota(jnp.int32, (depth, LANES), 1)
    up_pack = jnp.zeros((depth, LANES), jnp.float32)
    down_pack = jnp.zeros((depth, LANES), jnp.float32)
    top = bottom = None
    for x in range(slab_width):
        r = relax(cells_of_x(x))
        for m in range(19):
            relaxed_ref[m, x] = r[m]
        if x == slab_width - 1:
            top = corrected(r, upward, -1.0)
        if x == 0:
            bottom = corrected(r, downward, 1.0)
        for i, m in enumerate(y_plus):
            k = i * slab_width + x
            up_pack = jnp.where(lane == k, _roll(r[m], k + 1, 1), up_pack)
        for i, m in enumerate(y_minus):
            k = i * slab_width + x
            down_pack = jnp.where(lane == k, _roll(r[m], k, 1), down_pack)
    faces = jnp.concatenate([top.reshape(5 * depth, LANES), bottom.reshape(5 * depth, LANES)], axis=0)
    _, after, before, _ = _positions()
    to_next = jnp.full((depth, LANES), after, jnp.int32)
    to_prev = jnp.full((depth, LANES), before, jnp.int32)
    peers = chunk_ref.shape[0]
    for p in range(peers):
        chunk_ref[p, : FACE_ROWS * depth] = faces
        chunk_ref[p, FACE_ROWS * depth :] = jnp.where(to_next == p, up_pack, jnp.where(to_prev == p, down_pack, 0.0))


def _streamed(x, slab_width, relaxed_ref, rims_ref, low_ref, high_ref, hits_ref, depth):
    lane = lax.broadcasted_iota(jnp.int32, (depth, LANES), 1)
    out = []
    for n in range(19):
        step_x, step_y, step_z = velocity_table[n]
        xs = x - step_x
        if xs < 0:
            t = low_ref[upward.index(n)]
        elif xs >= slab_width:
            t = high_ref[downward.index(n)]
        else:
            t = relaxed_ref[n, xs]
            if step_y == 1:
                k = y_plus.index(n) * slab_width + xs
                t = jnp.where(lane == 0, _roll(rims_ref[0], LANES - k, 1), _roll(t, 1, 1))
            elif step_y == -1:
                k = y_minus.index(n) * slab_width + xs
                t = jnp.where(lane == LANES - 1, _roll(rims_ref[1], LANES - 1 - k, 1), _roll(t, LANES - 1, 1))
        if step_z != 0:
            t = _z_roll(t, step_z)
        out.append(t)
    result = [out[0]]
    for n in range(1, 19):
        source = n - 1 + 2 * (n % 2)
        result.append(jnp.where(hits_ref[source, x] > 0.5, relaxed_ref[source, x], out[n]))
    return result


def _first_kernel(mine_ref, other_ref, relaxed_ref, chunk_ref):
    slab_width, half = mine_ref.shape[1], mine_ref.shape[2]
    depth = 2 * half
    lower = jnp.full((half, LANES), _positions()[3], jnp.int32) == 0

    def cells(x):
        out = []
        for m in range(19):
            a, b = mine_ref[m, x], other_ref[m, x]
            out.append(jnp.concatenate([jnp.where(lower, a, b), jnp.where(lower, b, a)], axis=0))
        return out

    _emit_relax(cells, slab_width, relaxed_ref, chunk_ref, depth)


def _middle_kernel(relaxed_ref, rims_ref, low_ref, high_ref, hits_ref, next_ref, chunk_ref):
    slab_width, depth = relaxed_ref.shape[1], relaxed_ref.shape[2]
    cells = lambda x: _streamed(x, slab_width, relaxed_ref, rims_ref, low_ref, high_ref, hits_ref, depth)
    _emit_relax(cells, slab_width, next_ref, chunk_ref, depth)


def _last_kernel(relaxed_ref, rims_ref, low_ref, high_ref, hits_ref, out_ref, density_ref):
    slab_width, depth = relaxed_ref.shape[1], relaxed_ref.shape[2]
    half = depth // 2
    lower = jnp.full((half, LANES), _positions()[3], jnp.int32) == 0
    for x in range(slab_width):
        cells = _streamed(x, slab_width, relaxed_ref, rims_ref, low_ref, high_ref, hits_ref, depth)
        mine = [jnp.where(lower, c[:half], c[half:]) for c in cells]
        for m in range(19):
            out_ref[m, x] = mine[m]
        density_ref[x] = total_density(mine)


def _window_kernel(section, shift_ref, frac_ref, got_ref, low_ref, high_ref, rims_ref):
    peers, _, lanes = got_ref.shape
    depth = low_ref.shape[1]
    me_y, after, before, _ = _positions()
    offset = shift_ref[section]
    fraction = jnp.full((depth, lanes), frac_ref[section], jnp.int32).astype(jnp.float32) / 256.0
    keep = 1.0 - fraction
    flow_cells = peers * lanes
    anchor = me_y * lanes
    lane = lax.broadcasted_iota(jnp.int32, (depth, lanes), 1)

    def window(row0, start):
        start = (start + 2 * flow_cells) % flow_cells
        block = start // lanes
        off = start % lanes
        after = (block + 1) % peers
        shift = (lanes - off) % lanes
        first = pltpu.roll(got_ref[block, pl.ds(row0, depth), :], shift, 1)
        second = pltpu.roll(got_ref[after, pl.ds(row0, depth), :], shift, 1)
        return jnp.where(lane < lanes - off, first, second)

    for i, m in enumerate(upward):
        step_y = velocity_table[m][1]
        row0 = i * depth
        a = anchor - offset - step_y
        low_ref[i] = keep * window(row0, a) + fraction * window(row0, a - 1)
    for i, m in enumerate(downward):
        step_y = velocity_table[m][1]
        row0 = (5 + i) * depth
        c = anchor + offset - step_y
        high_ref[i] = fraction * window(row0, c + 1) + keep * window(row0, c)
    rims_ref[0] = got_ref[before, pl.ds(FACE_ROWS * depth, depth), :]
    rims_ref[1] = got_ref[after, pl.ds(FACE_ROWS * depth, depth), :]


def _vmem():
    return pl.BlockSpec(memory_space=pltpu.VMEM)


def _smem():
    return pl.BlockSpec(memory_space=pltpu.SMEM)


def _call(kernel, n_smem, n_vmem, out_shapes):
    return pl.pallas_call(
        kernel,
        out_shape=out_shapes,
        in_specs=[_smem()] * n_smem + [_vmem()] * n_vmem,
        out_specs=tuple(_vmem() for _ in out_shapes),
    )


def per_device(populations, le_shift, le_frac, links):
    n_members, slab_width, half_depth, row_span = populations.shape
    flow_cycle = lax.axis_size("gy")
    slab_cycle = lax.axis_size("gx")
    me_y = lax.axis_index("gy")
    me_z = lax.axis_index("gz")
    anchor = me_y * row_span

    other_states = lax.ppermute(populations, "gz", [(0, 1), (1, 0)])
    other_links = lax.ppermute(links, "gz", [(0, 1), (1, 0)])
    all_links = jnp.where(
        me_z == 0, jnp.concatenate([links, other_links], axis=1), jnp.concatenate([other_links, links], axis=1)
    )
    depth = 2 * half_depth
    hits = link_hits(all_links, anchor, row_span)

    f32 = jnp.float32
    full = jax.ShapeDtypeStruct((n_members, slab_width, depth, row_span), f32)
    chunk = jax.ShapeDtypeStruct((flow_cycle, (FACE_ROWS + 1) * depth, row_span), f32)
    ghost = jax.ShapeDtypeStruct((5, depth, row_span), f32)
    rims = jax.ShapeDtypeStruct((2, depth, row_span), f32)
    own = jax.ShapeDtypeStruct((n_members, slab_width, half_depth, row_span), f32)
    density = jax.ShapeDtypeStruct((slab_width, half_depth, row_span), f32)

    relaxed, chunks = _call(_first_kernel, 0, 2, (full, chunk))(populations, other_states)
    for section in range(STEPS):
        got = lax.all_to_all(chunks, "gy", 0, 0, tiled=True)
        low_send, high_send, rim_pair = _call(functools.partial(_window_kernel, section), 2, 1, (ghost, ghost, rims))(
            le_shift, le_frac, got
        )
        low_ghost = lax.ppermute(low_send, "gx", [(i, (i + 1) % slab_cycle) for i in range(slab_cycle)])
        high_ghost = lax.ppermute(high_send, "gx", [(i, (i - 1) % slab_cycle) for i in range(slab_cycle)])
        if section + 1 < STEPS:
            relaxed, chunks = _call(_middle_kernel, 0, 5, (full, chunk))(relaxed, rim_pair, low_ghost, high_ghost, hits)
        else:
            final, dens = _call(_last_kernel, 0, 5, (own, density))(relaxed, rim_pair, low_ghost, high_ghost, hits)
    return (final, dens)


def solution(mesh):
    in_specs = (P(None, "gx", "gz", "gy"), P(), P(), P("gx", "gz", "gy"))
    out_specs = (P(None, "gx", "gz", "gy"), P("gx", "gz", "gy"))
    return jax.shard_map(
        per_device, mesh=mesh, in_specs=in_specs, out_specs=out_specs, check_vma=False
    )
```

```python
import functools

import jax
import jax.numpy as jnp
from jax import lax
from jax.sharding import PartitionSpec as P
from jax.experimental import pallas as pl
from jax.experimental.pallas import tpu as pltpu


STEPS = 2


velocity_table = (
    (0, 0, 0),
    (1, 0, 0),
    (-1, 0, 0),
    (0, 1, 0),
    (0, -1, 0),
    (0, 0, 1),
    (0, 0, -1),
    (1, 1, 0),
    (-1, -1, 0),
    (1, -1, 0),
    (-1, 1, 0),
    (1, 0, 1),
    (-1, 0, -1),
    (1, 0, -1),
    (-1, 0, 1),
    (0, 1, 1),
    (0, -1, -1),
    (0, 1, -1),
    (0, -1, 1),
)
weight_table = (1.0 / 3.0,) + (1.0 / 18.0,) * 6 + (1.0 / 36.0,) * 12
upward = (1, 7, 9, 11, 13)
downward = (2, 8, 10, 12, 14)
y_plus = tuple(m for m in range(19) if velocity_table[m][1] == 1)
y_minus = tuple(m for m in range(19) if velocity_table[m][1] == -1)
relax_rate = 1.25
plane_speed = 0.08


def total_density(states):
    density = states[0]
    for member in range(1, 19):
        density = density + states[member]
    return density


def moments(states):
    density = total_density(states)
    velocity = []
    for dim_index in range(3):
        momentum = None
        for member in range(19):
            sign_part = velocity_table[member][dim_index]
            if sign_part == 1:
                momentum = states[member] if momentum is None else momentum + states[member]
            elif sign_part == -1:
                momentum = momentum - states[member]
        velocity.append(momentum / density)
    return (density, velocity)


def speed_square(velocity):
    return velocity[0] * velocity[0] + velocity[1] * velocity[1] + velocity[2] * velocity[2]


def equilibrium(member, density, velocity, speed_sq):
    projected = None
    for dim_index in range(3):
        sign_part = velocity_table[member][dim_index]
        if sign_part != 0:
            summand = velocity[dim_index] if sign_part > 0 else -velocity[dim_index]
            projected = summand if projected is None else projected + summand
    if projected is None:
        return weight_table[member] * density * (1.0 - 1.5 * speed_sq)
    return (
        weight_table[member]
        * density
        * (1.0 + 3.0 * projected + 4.5 * projected * projected - 1.5 * speed_sq)
    )


def relax(states):
    density, velocity = moments(states)
    speed_sq = speed_square(velocity)
    return [
        states[member]
        + relax_rate * (equilibrium(member, density, velocity, speed_sq) - states[member])
        for member in range(19)
    ]


def corrected(plane, members, sign_part):
    density, velocity = moments(plane)
    speed_sq = speed_square(velocity)
    moved = [velocity[0], velocity[1] + sign_part * plane_speed, velocity[2]]
    moved_sq = speed_square(moved)
    return jnp.stack(
        [
            plane[member]
            + equilibrium(member, density, moved, moved_sq)
            - equilibrium(member, density, velocity, speed_sq)
            for member in members
        ]
    )


def link_hits(links, anchor, row_span):
    cell_y = links // 19 - anchor
    member = links % 19
    by_member = (member[:, :, None, :] == jnp.arange(19, dtype=jnp.int32)[:, None]).astype(jnp.bfloat16)
    by_cell = (cell_y[:, :, :, None] == jnp.arange(row_span, dtype=jnp.int32)).astype(jnp.bfloat16)
    return jnp.einsum("xzml,xzly->mxzy", by_member, by_cell, preferred_element_type=jnp.float32)


LANES = 128
FACE_ROWS = 2 * 5


def _roll(t, shift, axis):
    if isinstance(shift, int):
        shift = shift % t.shape[axis]
        if shift == 0:
            return t
    return pltpu.roll(t, shift, axis)


def _z_roll(t, step):
    half = t.shape[0] // 2
    a, b = t[:half], t[half:]
    row = lax.broadcasted_iota(jnp.int32, a.shape, 0)
    if step == 1:
        ra, rb = _roll(a, 1, 0), _roll(b, 1, 0)
        edge = row == 0
    else:
        ra, rb = _roll(a, half - 1, 0), _roll(b, half - 1, 0)
        edge = row == half - 1
    return jnp.concatenate([jnp.where(edge, rb, ra), jnp.where(edge, ra, rb)], axis=0)


def _positions():
    flow_cycle = lax.axis_size("gy")
    me_y = lax.axis_index("gy")
    return me_y, (me_y + 1) % flow_cycle, (me_y - 1 + flow_cycle) % flow_cycle, lax.axis_index("gz")


def _emit_relax(cells_of_x, slab_width, relaxed_ref, chunk_ref, depth):
    lane = lax.broadcasted_iota(jnp.int32, (depth, LANES), 1)
    up_pack = jnp.zeros((depth, LANES), jnp.float32)
    down_pack = jnp.zeros((depth, LANES), jnp.float32)
    top = bottom = None
    for x in range(slab_width):
        r = relax(cells_of_x(x))
        for m in range(19):
            relaxed_ref[m, x] = r[m]
        if x == slab_width - 1:
            top = corrected(r, upward, -1.0)
        if x == 0:
            bottom = corrected(r, downward, 1.0)
        for i, m in enumerate(y_plus):
            k = i * slab_width + x
            up_pack = jnp.where(lane == k, _roll(r[m], k + 1, 1), up_pack)
        for i, m in enumerate(y_minus):
            k = i * slab_width + x
            down_pack = jnp.where(lane == k, _roll(r[m], k, 1), down_pack)
    faces = jnp.concatenate([top.reshape(5 * depth, LANES), bottom.reshape(5 * depth, LANES)], axis=0)
    _, after, before, _ = _positions()
    to_next = jnp.full((depth, LANES), after, jnp.int32)
    to_prev = jnp.full((depth, LANES), before, jnp.int32)
    peers = chunk_ref.shape[0]
    for p in range(peers):
        chunk_ref[p, : FACE_ROWS * depth] = faces
        chunk_ref[p, FACE_ROWS * depth :] = jnp.where(to_next == p, up_pack, jnp.where(to_prev == p, down_pack, 0.0))


def _streamed(x, slab_width, relaxed_ref, rims_ref, low_ref, high_ref, hits_ref, depth):
    lane = lax.broadcasted_iota(jnp.int32, (depth, LANES), 1)
    out = []
    for n in range(19):
        step_x, step_y, step_z = velocity_table[n]
        xs = x - step_x
        if xs < 0:
            t = low_ref[upward.index(n)]
        elif xs >= slab_width:
            t = high_ref[downward.index(n)]
        else:
            t = relaxed_ref[n, xs]
            if step_y == 1:
                k = y_plus.index(n) * slab_width + xs
                t = jnp.where(lane == 0, _roll(rims_ref[0], LANES - k, 1), _roll(t, 1, 1))
            elif step_y == -1:
                k = y_minus.index(n) * slab_width + xs
                t = jnp.where(lane == LANES - 1, _roll(rims_ref[1], LANES - 1 - k, 1), _roll(t, LANES - 1, 1))
        if step_z != 0:
            t = _z_roll(t, step_z)
        out.append(t)
    result = [out[0]]
    for n in range(1, 19):
        source = n - 1 + 2 * (n % 2)
        result.append(jnp.where(hits_ref[source, x] > 0.5, relaxed_ref[source, x], out[n]))
    return result


def _first_kernel(mine_ref, other_ref, relaxed_ref, chunk_ref):
    slab_width, half = mine_ref.shape[1], mine_ref.shape[2]
    depth = 2 * half
    lower = jnp.full((half, LANES), _positions()[3], jnp.int32) == 0

    def cells(x):
        out = []
        for m in range(19):
            a, b = mine_ref[m, x], other_ref[m, x]
            out.append(jnp.concatenate([jnp.where(lower, a, b), jnp.where(lower, b, a)], axis=0))
        return out

    _emit_relax(cells, slab_width, relaxed_ref, chunk_ref, depth)


def _middle_kernel(relaxed_ref, rims_ref, low_ref, high_ref, hits_ref, next_ref, chunk_ref):
    slab_width, depth = relaxed_ref.shape[1], relaxed_ref.shape[2]
    cells = lambda x: _streamed(x, slab_width, relaxed_ref, rims_ref, low_ref, high_ref, hits_ref, depth)
    _emit_relax(cells, slab_width, next_ref, chunk_ref, depth)


def _last_kernel(relaxed_ref, rims_ref, low_ref, high_ref, hits_ref, out_ref, density_ref):
    slab_width, depth = relaxed_ref.shape[1], relaxed_ref.shape[2]
    half = depth // 2
    lower = jnp.full((half, LANES), _positions()[3], jnp.int32) == 0
    for x in range(slab_width):
        cells = _streamed(x, slab_width, relaxed_ref, rims_ref, low_ref, high_ref, hits_ref, depth)
        mine = [jnp.where(lower, c[:half], c[half:]) for c in cells]
        for m in range(19):
            out_ref[m, x] = mine[m]
        density_ref[x] = total_density(mine)


def _window_kernel(section, shift_ref, frac_ref, got_ref, low_ref, high_ref, rims_ref):
    peers, _, lanes = got_ref.shape
    depth = low_ref.shape[1]
    me_y, after, before, _ = _positions()
    offset = shift_ref[section]
    fraction = jnp.full((depth, lanes), frac_ref[section], jnp.int32).astype(jnp.float32) / 256.0
    keep = 1.0 - fraction
    flow_cells = peers * lanes
    anchor = me_y * lanes
    lane = lax.broadcasted_iota(jnp.int32, (depth, lanes), 1)

    def window(row0, start):
        start = (start + 2 * flow_cells) % flow_cells
        block = start // lanes
        off = start % lanes
        after = (block + 1) % peers
        shift = (lanes - off) % lanes
        first = pltpu.roll(got_ref[block, pl.ds(row0, depth), :], shift, 1)
        second = pltpu.roll(got_ref[after, pl.ds(row0, depth), :], shift, 1)
        return jnp.where(lane < lanes - off, first, second)

    for i, m in enumerate(upward):
        step_y = velocity_table[m][1]
        row0 = i * depth
        a = anchor - offset - step_y
        low_ref[i] = keep * window(row0, a) + fraction * window(row0, a - 1)
    for i, m in enumerate(downward):
        step_y = velocity_table[m][1]
        row0 = (5 + i) * depth
        c = anchor + offset - step_y
        high_ref[i] = fraction * window(row0, c + 1) + keep * window(row0, c)
    rims_ref[0] = got_ref[before, pl.ds(FACE_ROWS * depth, depth), :]
    rims_ref[1] = got_ref[after, pl.ds(FACE_ROWS * depth, depth), :]


def _vmem():
    return pl.BlockSpec(memory_space=pltpu.VMEM)


def _smem():
    return pl.BlockSpec(memory_space=pltpu.SMEM)


def _call(kernel, n_smem, n_vmem, out_shapes):
    return pl.pallas_call(
        kernel,
        out_shape=out_shapes,
        in_specs=[_smem()] * n_smem + [_vmem()] * n_vmem,
        out_specs=tuple(_vmem() for _ in out_shapes),
    )


def _per_device(populations, le_shift, le_frac, links):
    n_members, slab_width, half_depth, row_span = populations.shape
    flow_cycle = lax.axis_size("gy")
    slab_cycle = lax.axis_size("gx")
    me_y = lax.axis_index("gy")
    me_z = lax.axis_index("gz")
    anchor = me_y * row_span

    other_states = lax.ppermute(populations, "gz", [(0, 1), (1, 0)])
    other_links = lax.ppermute(links, "gz", [(0, 1), (1, 0)])
    all_links = jnp.where(
        me_z == 0, jnp.concatenate([links, other_links], axis=1), jnp.concatenate([other_links, links], axis=1)
    )
    depth = 2 * half_depth
    hits = link_hits(all_links, anchor, row_span)

    f32 = jnp.float32
    full = jax.ShapeDtypeStruct((n_members, slab_width, depth, row_span), f32)
    chunk = jax.ShapeDtypeStruct((flow_cycle, (FACE_ROWS + 1) * depth, row_span), f32)
    ghost = jax.ShapeDtypeStruct((5, depth, row_span), f32)
    rims = jax.ShapeDtypeStruct((2, depth, row_span), f32)
    own = jax.ShapeDtypeStruct((n_members, slab_width, half_depth, row_span), f32)
    density = jax.ShapeDtypeStruct((slab_width, half_depth, row_span), f32)

    relaxed, chunks = _call(_first_kernel, 0, 2, (full, chunk))(populations, other_states)
    for section in range(STEPS):
        got = lax.all_to_all(chunks, "gy", 0, 0, tiled=True)
        low_send, high_send, rim_pair = _call(functools.partial(_window_kernel, section), 2, 1, (ghost, ghost, rims))(
            le_shift, le_frac, got
        )
        low_ghost = lax.ppermute(low_send, "gx", [(i, (i + 1) % slab_cycle) for i in range(slab_cycle)])
        high_ghost = lax.ppermute(high_send, "gx", [(i, (i - 1) % slab_cycle) for i in range(slab_cycle)])
        if section + 1 < STEPS:
            relaxed, chunks = _call(_middle_kernel, 0, 5, (full, chunk))(relaxed, rim_pair, low_ghost, high_ghost, hits)
        else:
            final, dens = _call(_last_kernel, 0, 5, (own, density))(relaxed, rim_pair, low_ghost, high_ghost, hits)
    return (final, dens)


def solution(mesh):
    in_specs = (P(None, "gx", "gz", "gy"), P(), P(), P("gx", "gz", "gy"))
    out_specs = (P(None, "gx", "gz", "gy"), P("gx", "gz", "gy"))
    return jax.shard_map(_per_device, mesh=mesh, in_specs=in_specs, out_specs=out_specs, check_vma=False)
```

```python
import functools

import jax
import jax.numpy as jnp
from jax import lax
from jax.sharding import PartitionSpec as P
from jax.experimental import pallas as pl
from jax.experimental.pallas import tpu as pltpu


STEPS = 2


velocity_table = (
    (0, 0, 0),
    (1, 0, 0),
    (-1, 0, 0),
    (0, 1, 0),
    (0, -1, 0),
    (0, 0, 1),
    (0, 0, -1),
    (1, 1, 0),
    (-1, -1, 0),
    (1, -1, 0),
    (-1, 1, 0),
    (1, 0, 1),
    (-1, 0, -1),
    (1, 0, -1),
    (-1, 0, 1),
    (0, 1, 1),
    (0, -1, -1),
    (0, 1, -1),
    (0, -1, 1),
)
weight_table = (1.0 / 3.0,) + (1.0 / 18.0,) * 6 + (1.0 / 36.0,) * 12
upward = (1, 7, 9, 11, 13)
downward = (2, 8, 10, 12, 14)
y_plus = tuple(m for m in range(19) if velocity_table[m][1] == 1)
y_minus = tuple(m for m in range(19) if velocity_table[m][1] == -1)
relax_rate = 1.25
plane_speed = 0.08


def total_density(states):
    density = states[0]
    for member in range(1, 19):
        density = density + states[member]
    return density


def moments(states):
    density = total_density(states)
    velocity = []
    for dim_index in range(3):
        momentum = None
        for member in range(19):
            sign_part = velocity_table[member][dim_index]
            if sign_part == 1:
                momentum = states[member] if momentum is None else momentum + states[member]
            elif sign_part == -1:
                momentum = momentum - states[member]
        velocity.append(momentum / density)
    return (density, velocity)


def speed_square(velocity):
    return velocity[0] * velocity[0] + velocity[1] * velocity[1] + velocity[2] * velocity[2]


def equilibrium(member, density, velocity, speed_sq):
    projected = None
    for dim_index in range(3):
        sign_part = velocity_table[member][dim_index]
        if sign_part != 0:
            summand = velocity[dim_index] if sign_part > 0 else -velocity[dim_index]
            projected = summand if projected is None else projected + summand
    if projected is None:
        return weight_table[member] * density * (1.0 - 1.5 * speed_sq)
    return (
        weight_table[member]
        * density
        * (1.0 + 3.0 * projected + 4.5 * projected * projected - 1.5 * speed_sq)
    )


def relax(states):
    density, velocity = moments(states)
    speed_sq = speed_square(velocity)
    return [
        states[member]
        + relax_rate * (equilibrium(member, density, velocity, speed_sq) - states[member])
        for member in range(19)
    ]


def corrected(plane, members, sign_part):
    density, velocity = moments(plane)
    speed_sq = speed_square(velocity)
    moved = [velocity[0], velocity[1] + sign_part * plane_speed, velocity[2]]
    moved_sq = speed_square(moved)
    return jnp.stack(
        [
            plane[member]
            + equilibrium(member, density, moved, moved_sq)
            - equilibrium(member, density, velocity, speed_sq)
            for member in members
        ]
    )


def link_hits(links, anchor, row_span):
    cell_y = links // 19 - anchor
    member = links % 19
    by_member = (member[:, :, None, :] == jnp.arange(19, dtype=jnp.int32)[:, None]).astype(jnp.bfloat16)
    by_cell = (cell_y[:, :, :, None] == jnp.arange(row_span, dtype=jnp.int32)).astype(jnp.bfloat16)
    return jnp.einsum("xzml,xzly->mxzy", by_member, by_cell, preferred_element_type=jnp.float32)


LANES = 128
FACE_ROWS = 2 * 5


def _roll(t, shift, axis):
    if isinstance(shift, int):
        shift = shift % t.shape[axis]
        if shift == 0:
            return t
    return pltpu.roll(t, shift, axis)


def _z_roll(t, step):
    half = t.shape[0] // 2
    a, b = t[:half], t[half:]
    row = lax.broadcasted_iota(jnp.int32, a.shape, 0)
    if step == 1:
        ra, rb = _roll(a, 1, 0), _roll(b, 1, 0)
        edge = row == 0
    else:
        ra, rb = _roll(a, half - 1, 0), _roll(b, half - 1, 0)
        edge = row == half - 1
    return jnp.concatenate([jnp.where(edge, rb, ra), jnp.where(edge, ra, rb)], axis=0)


def _positions():
    flow_cycle = lax.axis_size("gy")
    me_y = lax.axis_index("gy")
    return me_y, (me_y + 1) % flow_cycle, (me_y - 1 + flow_cycle) % flow_cycle, lax.axis_index("gz")


def _emit_relax(cells_of_x, slab_width, relaxed_ref, chunk_ref, depth):
    lane = lax.broadcasted_iota(jnp.int32, (depth, LANES), 1)
    up_pack = jnp.zeros((depth, LANES), jnp.float32)
    down_pack = jnp.zeros((depth, LANES), jnp.float32)
    top = bottom = None
    for x in range(slab_width):
        r = relax(cells_of_x(x))
        for m in range(19):
            relaxed_ref[m, x] = r[m]
        if x == slab_width - 1:
            top = corrected(r, upward, -1.0)
        if x == 0:
            bottom = corrected(r, downward, 1.0)
        for i, m in enumerate(y_plus):
            k = i * slab_width + x
            up_pack = jnp.where(lane == k, _roll(r[m], k + 1, 1), up_pack)
        for i, m in enumerate(y_minus):
            k = i * slab_width + x
            down_pack = jnp.where(lane == k, _roll(r[m], k, 1), down_pack)
    faces = jnp.concatenate([top.reshape(5 * depth, LANES), bottom.reshape(5 * depth, LANES)], axis=0)
    _, after, before, _ = _positions()
    to_next = jnp.full((depth, LANES), after, jnp.int32)
    to_prev = jnp.full((depth, LANES), before, jnp.int32)
    peers = chunk_ref.shape[0]
    for p in range(peers):
        chunk_ref[p, : FACE_ROWS * depth] = faces
        chunk_ref[p, FACE_ROWS * depth :] = jnp.where(to_next == p, up_pack, jnp.where(to_prev == p, down_pack, 0.0))


def _streamed(x, slab_width, relaxed_ref, rims_ref, low_ref, high_ref, hits_ref, depth):
    lane = lax.broadcasted_iota(jnp.int32, (depth, LANES), 1)
    out = []
    for n in range(19):
        step_x, step_y, step_z = velocity_table[n]
        xs = x - step_x
        if xs < 0:
            t = low_ref(upward.index(n))
        elif xs >= slab_width:
            t = high_ref(downward.index(n))
        else:
            t = relaxed_ref[n, xs]
            if step_y == 1:
                k = y_plus.index(n) * slab_width + xs
                t = jnp.where(lane == 0, _roll(rims_ref[0], LANES - k, 1), _roll(t, 1, 1))
            elif step_y == -1:
                k = y_minus.index(n) * slab_width + xs
                t = jnp.where(lane == LANES - 1, _roll(rims_ref[1], LANES - 1 - k, 1), _roll(t, LANES - 1, 1))
        if step_z != 0:
            t = _z_roll(t, step_z)
        out.append(t)
    result = [out[0]]
    for n in range(1, 19):
        source = n - 1 + 2 * (n % 2)
        result.append(jnp.where(hits_ref[source, x] > 0.5, relaxed_ref[source, x], out[n]))
    return result


def _first_kernel(mine_ref, other_ref, relaxed_ref, chunk_ref):
    slab_width, half = mine_ref.shape[1], mine_ref.shape[2]
    depth = 2 * half
    lower = jnp.full((half, LANES), _positions()[3], jnp.int32) == 0

    def cells(x):
        out = []
        for m in range(19):
            a, b = mine_ref[m, x], other_ref[m, x]
            out.append(jnp.concatenate([jnp.where(lower, a, b), jnp.where(lower, b, a)], axis=0))
        return out

    _emit_relax(cells, slab_width, relaxed_ref, chunk_ref, depth)


def _ghost_pair(cross_ref, swap_ref):
    lower = _positions()[3] == 0
    low = lambda i: jnp.where(lower, cross_ref[i], swap_ref[i])
    high = lambda i: jnp.where(lower, swap_ref[i], cross_ref[i])
    return low, high


def _middle_kernel(relaxed_ref, rims_ref, cross_ref, swap_ref, hits_ref, next_ref, chunk_ref):
    slab_width, depth = relaxed_ref.shape[1], relaxed_ref.shape[2]
    low_ref, high_ref = _ghost_pair(cross_ref, swap_ref)
    cells = lambda x: _streamed(x, slab_width, relaxed_ref, rims_ref, low_ref, high_ref, hits_ref, depth)
    _emit_relax(cells, slab_width, next_ref, chunk_ref, depth)


def _last_kernel(relaxed_ref, rims_ref, cross_ref, swap_ref, hits_ref, out_ref, density_ref):
    slab_width, depth = relaxed_ref.shape[1], relaxed_ref.shape[2]
    low_ref, high_ref = _ghost_pair(cross_ref, swap_ref)
    half = depth // 2
    lower = jnp.full((half, LANES), _positions()[3], jnp.int32) == 0
    for x in range(slab_width):
        cells = _streamed(x, slab_width, relaxed_ref, rims_ref, low_ref, high_ref, hits_ref, depth)
        mine = [jnp.where(lower, c[:half], c[half:]) for c in cells]
        for m in range(19):
            out_ref[m, x] = mine[m]
        density_ref[x] = total_density(mine)


def _window_kernel(section, shift_ref, frac_ref, got_ref, ghost_ref, rims_ref):
    peers, _, lanes = got_ref.shape
    depth = ghost_ref.shape[1]
    me_y, after, before, me_z = _positions()
    offset = shift_ref[section]
    fraction = jnp.full((depth, lanes), frac_ref[section], jnp.int32).astype(jnp.float32) / 256.0
    keep = 1.0 - fraction
    flow_cells = peers * lanes
    anchor = me_y * lanes
    lane = lax.broadcasted_iota(jnp.int32, (depth, lanes), 1)

    def window(row0, start):
        start = (start + 2 * flow_cells) % flow_cells
        block = start // lanes
        off = start % lanes
        after = (block + 1) % peers
        shift = (lanes - off) % lanes
        first = pltpu.roll(got_ref[block, pl.ds(row0, depth), :], shift, 1)
        second = pltpu.roll(got_ref[after, pl.ds(row0, depth), :], shift, 1)
        return jnp.where(lane < lanes - off, first, second)

    @pl.when(me_z == 0)
    def _():
        for i, m in enumerate(upward):
            step_y = velocity_table[m][1]
            row0 = i * depth
            a = anchor - offset - step_y
            ghost_ref[i] = keep * window(row0, a) + fraction * window(row0, a - 1)

    @pl.when(me_z != 0)
    def _():
        for i, m in enumerate(downward):
            step_y = velocity_table[m][1]
            row0 = (5 + i) * depth
            c = anchor + offset - step_y
            ghost_ref[i] = fraction * window(row0, c + 1) + keep * window(row0, c)

    rims_ref[0] = got_ref[before, pl.ds(FACE_ROWS * depth, depth), :]
    rims_ref[1] = got_ref[after, pl.ds(FACE_ROWS * depth, depth), :]


def _vmem():
    return pl.BlockSpec(memory_space=pltpu.VMEM)


def _smem():
    return pl.BlockSpec(memory_space=pltpu.SMEM)


def _call(kernel, n_smem, n_vmem, out_shapes):
    return pl.pallas_call(
        kernel,
        out_shape=out_shapes,
        in_specs=[_smem()] * n_smem + [_vmem()] * n_vmem,
        out_specs=tuple(_vmem() for _ in out_shapes),
    )


def _per_device(populations, le_shift, le_frac, links):
    n_members, slab_width, half_depth, row_span = populations.shape
    flow_cycle = lax.axis_size("gy")
    slab_cycle = lax.axis_size("gx")
    me_y = lax.axis_index("gy")
    me_z = lax.axis_index("gz")
    anchor = me_y * row_span

    other_states = lax.ppermute(populations, "gz", [(0, 1), (1, 0)])
    other_links = lax.ppermute(links, "gz", [(0, 1), (1, 0)])
    all_links = jnp.where(
        me_z == 0, jnp.concatenate([links, other_links], axis=1), jnp.concatenate([other_links, links], axis=1)
    )
    depth = 2 * half_depth
    hits = link_hits(all_links, anchor, row_span)

    f32 = jnp.float32
    full = jax.ShapeDtypeStruct((n_members, slab_width, depth, row_span), f32)
    chunk = jax.ShapeDtypeStruct((flow_cycle, (FACE_ROWS + 1) * depth, row_span), f32)
    ghost = jax.ShapeDtypeStruct((5, depth, row_span), f32)
    rims = jax.ShapeDtypeStruct((2, depth, row_span), f32)
    own = jax.ShapeDtypeStruct((n_members, slab_width, half_depth, row_span), f32)
    density = jax.ShapeDtypeStruct((slab_width, half_depth, row_span), f32)

    cores = lax.axis_size("gz")
    slab_pairs = []
    for a in range(slab_cycle):
        for b in range(flow_cycle):
            slab_pairs.append(((a * flow_cycle + b) * cores, (((a + 1) % slab_cycle) * flow_cycle + b) * cores))
            slab_pairs.append(
                ((a * flow_cycle + b) * cores + 1, (((a - 1) % slab_cycle) * flow_cycle + b) * cores + 1)
            )
    relaxed, chunks = _call(_first_kernel, 0, 2, (full, chunk))(populations, other_states)
    for section in range(STEPS):
        got = lax.all_to_all(chunks, "gy", 0, 0, tiled=True)
        ghost_send, rim_pair = _call(functools.partial(_window_kernel, section), 2, 1, (ghost, rims))(
            le_shift, le_frac, got
        )
        cross = lax.ppermute(ghost_send, ("gx", "gy", "gz"), slab_pairs)
        low_ghost = cross
        high_ghost = lax.ppermute(cross, "gz", [(0, 1), (1, 0)])
        if section + 1 < STEPS:
            relaxed, chunks = _call(_middle_kernel, 0, 5, (full, chunk))(relaxed, rim_pair, low_ghost, high_ghost, hits)
        else:
            final, dens = _call(_last_kernel, 0, 5, (own, density))(relaxed, rim_pair, low_ghost, high_ghost, hits)
    return (final, dens)


def solution(mesh):
    in_specs = (P(None, "gx", "gz", "gy"), P(), P(), P("gx", "gz", "gy"))
    out_specs = (P(None, "gx", "gz", "gy"), P("gx", "gz", "gy"))
    return jax.shard_map(_per_device, mesh=mesh, in_specs=in_specs, out_specs=out_specs, check_vma=False)
```

```python
import functools

import jax
import jax.numpy as jnp
from jax import lax
from jax.sharding import PartitionSpec as P
from jax.experimental import pallas as pl
from jax.experimental.pallas import tpu as pltpu


STEPS = 2


velocity_table = (
    (0, 0, 0),
    (1, 0, 0),
    (-1, 0, 0),
    (0, 1, 0),
    (0, -1, 0),
    (0, 0, 1),
    (0, 0, -1),
    (1, 1, 0),
    (-1, -1, 0),
    (1, -1, 0),
    (-1, 1, 0),
    (1, 0, 1),
    (-1, 0, -1),
    (1, 0, -1),
    (-1, 0, 1),
    (0, 1, 1),
    (0, -1, -1),
    (0, 1, -1),
    (0, -1, 1),
)
weight_table = (1.0 / 3.0,) + (1.0 / 18.0,) * 6 + (1.0 / 36.0,) * 12
upward = (1, 7, 9, 11, 13)
downward = (2, 8, 10, 12, 14)
y_plus = tuple(m for m in range(19) if velocity_table[m][1] == 1)
y_minus = tuple(m for m in range(19) if velocity_table[m][1] == -1)
relax_rate = 1.25
plane_speed = 0.08


def total_density(states):
    density = states[0]
    for member in range(1, 19):
        density = density + states[member]
    return density


def moments(states):
    density = total_density(states)
    velocity = []
    for dim_index in range(3):
        momentum = None
        for member in range(19):
            sign_part = velocity_table[member][dim_index]
            if sign_part == 1:
                momentum = states[member] if momentum is None else momentum + states[member]
            elif sign_part == -1:
                momentum = momentum - states[member]
        velocity.append(momentum / density)
    return (density, velocity)


def speed_square(velocity):
    return velocity[0] * velocity[0] + velocity[1] * velocity[1] + velocity[2] * velocity[2]


def equilibrium(member, density, velocity, speed_sq):
    projected = None
    for dim_index in range(3):
        sign_part = velocity_table[member][dim_index]
        if sign_part != 0:
            summand = velocity[dim_index] if sign_part > 0 else -velocity[dim_index]
            projected = summand if projected is None else projected + summand
    if projected is None:
        return weight_table[member] * density * (1.0 - 1.5 * speed_sq)
    return (
        weight_table[member]
        * density
        * (1.0 + 3.0 * projected + 4.5 * projected * projected - 1.5 * speed_sq)
    )


def relax(states):
    density, velocity = moments(states)
    speed_sq = speed_square(velocity)
    return [
        states[member]
        + relax_rate * (equilibrium(member, density, velocity, speed_sq) - states[member])
        for member in range(19)
    ]


def corrected(plane, members, sign_part):
    density, velocity = moments(plane)
    speed_sq = speed_square(velocity)
    moved = [velocity[0], velocity[1] + sign_part * plane_speed, velocity[2]]
    moved_sq = speed_square(moved)
    return jnp.stack(
        [
            plane[member]
            + equilibrium(member, density, moved, moved_sq)
            - equilibrium(member, density, velocity, speed_sq)
            for member in members
        ]
    )


def link_hits(links, anchor, row_span):
    cell_y = links // 19 - anchor
    member = links % 19
    by_member = (member[:, :, None, :] == jnp.arange(19, dtype=jnp.int32)[:, None]).astype(jnp.bfloat16)
    by_cell = (cell_y[:, :, :, None] == jnp.arange(row_span, dtype=jnp.int32)).astype(jnp.bfloat16)
    return jnp.einsum("xzml,xzly->mxzy", by_member, by_cell, preferred_element_type=jnp.float32)


LANES = 128
FACE_ROWS = 2 * 5


def _roll(t, shift, axis):
    if isinstance(shift, int):
        shift = shift % t.shape[axis]
        if shift == 0:
            return t
    return pltpu.roll(t, shift, axis)


def _z_roll(t, step):
    half = t.shape[0] // 2
    a, b = t[:half], t[half:]
    row = lax.broadcasted_iota(jnp.int32, a.shape, 0)
    if step == 1:
        ra, rb = _roll(a, 1, 0), _roll(b, 1, 0)
        edge = row == 0
    else:
        ra, rb = _roll(a, half - 1, 0), _roll(b, half - 1, 0)
        edge = row == half - 1
    return jnp.concatenate([jnp.where(edge, rb, ra), jnp.where(edge, ra, rb)], axis=0)


def _positions():
    flow_cycle = lax.axis_size("gy")
    me_y = lax.axis_index("gy")
    return me_y, (me_y + 1) % flow_cycle, (me_y - 1 + flow_cycle) % flow_cycle, lax.axis_index("gz")


def _emit_relax(cells_of_x, slab_width, relaxed_ref, chunk_ref, depth):
    lane = lax.broadcasted_iota(jnp.int32, (depth, LANES), 1)
    up_pack = jnp.zeros((depth, LANES), jnp.float32)
    down_pack = jnp.zeros((depth, LANES), jnp.float32)
    top = bottom = None
    half = depth // 2
    for x in range(slab_width):
        cells = cells_of_x(x)
        lower = relax([c[:half] for c in cells])
        upper = relax([c[half:] for c in cells])
        r = [jnp.concatenate([a, b], axis=0) for a, b in zip(lower, upper)]
        for m in range(19):
            relaxed_ref[m, x] = r[m]
        if x == slab_width - 1:
            top = corrected(r, upward, -1.0)
        if x == 0:
            bottom = corrected(r, downward, 1.0)
        for i, m in enumerate(y_plus):
            k = i * slab_width + x
            up_pack = jnp.where(lane == k, _roll(r[m], k + 1, 1), up_pack)
        for i, m in enumerate(y_minus):
            k = i * slab_width + x
            down_pack = jnp.where(lane == k, _roll(r[m], k, 1), down_pack)
    faces = jnp.concatenate([top.reshape(5 * depth, LANES), bottom.reshape(5 * depth, LANES)], axis=0)
    _, after, before, _ = _positions()
    to_next = jnp.full((depth, LANES), after, jnp.int32)
    to_prev = jnp.full((depth, LANES), before, jnp.int32)
    peers = chunk_ref.shape[0]
    for p in range(peers):
        chunk_ref[p, : FACE_ROWS * depth] = faces
        chunk_ref[p, FACE_ROWS * depth :] = jnp.where(to_next == p, up_pack, jnp.where(to_prev == p, down_pack, 0.0))


def _streamed(x, slab_width, relaxed_ref, rims_ref, low_ref, high_ref, hits_ref, depth):
    lane = lax.broadcasted_iota(jnp.int32, (depth, LANES), 1)
    out = []
    for n in range(19):
        step_x, step_y, step_z = velocity_table[n]
        xs = x - step_x
        if xs < 0:
            t = low_ref[upward.index(n)]
        elif xs >= slab_width:
            t = high_ref[downward.index(n)]
        else:
            t = relaxed_ref[n, xs]
            if step_y == 1:
                k = y_plus.index(n) * slab_width + xs
                t = jnp.where(lane == 0, _roll(rims_ref[0], LANES - k, 1), _roll(t, 1, 1))
            elif step_y == -1:
                k = y_minus.index(n) * slab_width + xs
                t = jnp.where(lane == LANES - 1, _roll(rims_ref[1], LANES - 1 - k, 1), _roll(t, LANES - 1, 1))
        if step_z != 0:
            t = _z_roll(t, step_z)
        out.append(t)
    result = [out[0]]
    for n in range(1, 19):
        source = n - 1 + 2 * (n % 2)
        result.append(jnp.where(hits_ref[source, x] > 0.5, relaxed_ref[source, x], out[n]))
    return result


def _first_kernel(mine_ref, other_ref, relaxed_ref, chunk_ref):
    slab_width, half = mine_ref.shape[1], mine_ref.shape[2]
    depth = 2 * half
    lower = jnp.full((half, LANES), _positions()[3], jnp.int32) == 0

    def cells(x):
        out = []
        for m in range(19):
            a, b = mine_ref[m, x], other_ref[m, x]
            out.append(jnp.concatenate([jnp.where(lower, a, b), jnp.where(lower, b, a)], axis=0))
        return out

    _emit_relax(cells, slab_width, relaxed_ref, chunk_ref, depth)


def _middle_kernel(relaxed_ref, rims_ref, low_ref, high_ref, hits_ref, next_ref, chunk_ref):
    slab_width, depth = relaxed_ref.shape[1], relaxed_ref.shape[2]
    cells = lambda x: _streamed(x, slab_width, relaxed_ref, rims_ref, low_ref, high_ref, hits_ref, depth)
    _emit_relax(cells, slab_width, next_ref, chunk_ref, depth)


def _last_kernel(relaxed_ref, rims_ref, low_ref, high_ref, hits_ref, out_ref, density_ref):
    slab_width, depth = relaxed_ref.shape[1], relaxed_ref.shape[2]
    half = depth // 2
    lower = jnp.full((half, LANES), _positions()[3], jnp.int32) == 0
    for x in range(slab_width):
        cells = _streamed(x, slab_width, relaxed_ref, rims_ref, low_ref, high_ref, hits_ref, depth)
        mine = [jnp.where(lower, c[:half], c[half:]) for c in cells]
        for m in range(19):
            out_ref[m, x] = mine[m]
        density_ref[x] = total_density(mine)


def _window_kernel(section, shift_ref, frac_ref, got_ref, low_ref, high_ref, rims_ref):
    peers, _, lanes = got_ref.shape
    depth = low_ref.shape[1]
    me_y, after, before, _ = _positions()
    offset = shift_ref[section]
    fraction = jnp.full((depth, lanes), frac_ref[section], jnp.int32).astype(jnp.float32) / 256.0
    keep = 1.0 - fraction
    flow_cells = peers * lanes
    anchor = me_y * lanes
    lane = lax.broadcasted_iota(jnp.int32, (depth, lanes), 1)

    def window(row0, start):
        start = (start + 2 * flow_cells) % flow_cells
        block = start // lanes
        off = start % lanes
        after = (block + 1) % peers
        shift = (lanes - off) % lanes
        first = pltpu.roll(got_ref[block, pl.ds(row0, depth), :], shift, 1)
        second = pltpu.roll(got_ref[after, pl.ds(row0, depth), :], shift, 1)
        return jnp.where(lane < lanes - off, first, second)

    for i, m in enumerate(upward):
        step_y = velocity_table[m][1]
        row0 = i * depth
        a = anchor - offset - step_y
        low_ref[i] = keep * window(row0, a) + fraction * window(row0, a - 1)
    for i, m in enumerate(downward):
        step_y = velocity_table[m][1]
        row0 = (5 + i) * depth
        c = anchor + offset - step_y
        high_ref[i] = fraction * window(row0, c + 1) + keep * window(row0, c)
    rims_ref[0] = got_ref[before, pl.ds(FACE_ROWS * depth, depth), :]
    rims_ref[1] = got_ref[after, pl.ds(FACE_ROWS * depth, depth), :]


def _vmem():
    return pl.BlockSpec(memory_space=pltpu.VMEM)


def _smem():
    return pl.BlockSpec(memory_space=pltpu.SMEM)


def _call(kernel, n_smem, n_vmem, out_shapes):
    return pl.pallas_call(
        kernel,
        out_shape=out_shapes,
        in_specs=[_smem()] * n_smem + [_vmem()] * n_vmem,
        out_specs=tuple(_vmem() for _ in out_shapes),
    )


def _per_device(populations, le_shift, le_frac, links):
    n_members, slab_width, half_depth, row_span = populations.shape
    flow_cycle = lax.axis_size("gy")
    slab_cycle = lax.axis_size("gx")
    me_y = lax.axis_index("gy")
    me_z = lax.axis_index("gz")
    anchor = me_y * row_span

    other_states = lax.ppermute(populations, "gz", [(0, 1), (1, 0)])
    other_links = lax.ppermute(links, "gz", [(0, 1), (1, 0)])
    all_links = jnp.where(
        me_z == 0, jnp.concatenate([links, other_links], axis=1), jnp.concatenate([other_links, links], axis=1)
    )
    depth = 2 * half_depth
    hits = link_hits(all_links, anchor, row_span)

    f32 = jnp.float32
    full = jax.ShapeDtypeStruct((n_members, slab_width, depth, row_span), f32)
    chunk = jax.ShapeDtypeStruct((flow_cycle, (FACE_ROWS + 1) * depth, row_span), f32)
    ghost = jax.ShapeDtypeStruct((5, depth, row_span), f32)
    rims = jax.ShapeDtypeStruct((2, depth, row_span), f32)
    own = jax.ShapeDtypeStruct((n_members, slab_width, half_depth, row_span), f32)
    density = jax.ShapeDtypeStruct((slab_width, half_depth, row_span), f32)

    relaxed, chunks = _call(_first_kernel, 0, 2, (full, chunk))(populations, other_states)
    for section in range(STEPS):
        got = lax.all_to_all(chunks, "gy", 0, 0, tiled=True)
        low_send, high_send, rim_pair = _call(functools.partial(_window_kernel, section), 2, 1, (ghost, ghost, rims))(
            le_shift, le_frac, got
        )
        low_ghost = lax.ppermute(low_send, "gx", [(i, (i + 1) % slab_cycle) for i in range(slab_cycle)])
        high_ghost = lax.ppermute(high_send, "gx", [(i, (i - 1) % slab_cycle) for i in range(slab_cycle)])
        if section + 1 < STEPS:
            relaxed, chunks = _call(_middle_kernel, 0, 5, (full, chunk))(relaxed, rim_pair, low_ghost, high_ghost, hits)
        else:
            final, dens = _call(_last_kernel, 0, 5, (own, density))(relaxed, rim_pair, low_ghost, high_ghost, hits)
    return (final, dens)


def solution(mesh):
    in_specs = (P(None, "gx", "gz", "gy"), P(), P(), P("gx", "gz", "gy"))
    out_specs = (P(None, "gx", "gz", "gy"), P("gx", "gz", "gy"))
    return jax.shard_map(_per_device, mesh=mesh, in_specs=in_specs, out_specs=out_specs, check_vma=False)
```

```python
import functools

import jax
import jax.numpy as jnp
from jax import lax
from jax.sharding import PartitionSpec as P
from jax.experimental import pallas as pl
from jax.experimental.pallas import tpu as pltpu


STEPS = 2


velocity_table = (
    (0, 0, 0),
    (1, 0, 0),
    (-1, 0, 0),
    (0, 1, 0),
    (0, -1, 0),
    (0, 0, 1),
    (0, 0, -1),
    (1, 1, 0),
    (-1, -1, 0),
    (1, -1, 0),
    (-1, 1, 0),
    (1, 0, 1),
    (-1, 0, -1),
    (1, 0, -1),
    (-1, 0, 1),
    (0, 1, 1),
    (0, -1, -1),
    (0, 1, -1),
    (0, -1, 1),
)
weight_table = (1.0 / 3.0,) + (1.0 / 18.0,) * 6 + (1.0 / 36.0,) * 12
upward = (1, 7, 9, 11, 13)
downward = (2, 8, 10, 12, 14)
y_plus = tuple(m for m in range(19) if velocity_table[m][1] == 1)
y_minus = tuple(m for m in range(19) if velocity_table[m][1] == -1)
relax_rate = 1.25
plane_speed = 0.08


def total_density(states):
    density = states[0]
    for member in range(1, 19):
        density = density + states[member]
    return density


def moments(states):
    density = total_density(states)
    velocity = []
    for dim_index in range(3):
        momentum = None
        for member in range(19):
            sign_part = velocity_table[member][dim_index]
            if sign_part == 1:
                momentum = states[member] if momentum is None else momentum + states[member]
            elif sign_part == -1:
                momentum = momentum - states[member]
        velocity.append(momentum / density)
    return (density, velocity)


def speed_square(velocity):
    return velocity[0] * velocity[0] + velocity[1] * velocity[1] + velocity[2] * velocity[2]


def equilibrium(member, density, velocity, speed_sq):
    projected = None
    for dim_index in range(3):
        sign_part = velocity_table[member][dim_index]
        if sign_part != 0:
            summand = velocity[dim_index] if sign_part > 0 else -velocity[dim_index]
            projected = summand if projected is None else projected + summand
    if projected is None:
        return weight_table[member] * density * (1.0 - 1.5 * speed_sq)
    return (
        weight_table[member]
        * density
        * (1.0 + 3.0 * projected + 4.5 * projected * projected - 1.5 * speed_sq)
    )


def relax(states):
    density, velocity = moments(states)
    speed_sq = speed_square(velocity)
    return [
        states[member]
        + relax_rate * (equilibrium(member, density, velocity, speed_sq) - states[member])
        for member in range(19)
    ]


def corrected(plane, members, sign_part):
    density, velocity = moments(plane)
    speed_sq = speed_square(velocity)
    moved = [velocity[0], velocity[1] + sign_part * plane_speed, velocity[2]]
    moved_sq = speed_square(moved)
    return jnp.stack(
        [
            plane[member]
            + equilibrium(member, density, moved, moved_sq)
            - equilibrium(member, density, velocity, speed_sq)
            for member in members
        ]
    )


def link_hits(links, anchor, row_span):
    cell_y = links // 19 - anchor
    member = links % 19
    by_member = (member[:, :, None, :] == jnp.arange(19, dtype=jnp.int32)[:, None]).astype(jnp.bfloat16)
    by_cell = (cell_y[:, :, :, None] == jnp.arange(row_span, dtype=jnp.int32)).astype(jnp.bfloat16)
    counts = jnp.einsum("xzml,xzly->mxzy", by_member, by_cell, preferred_element_type=jnp.float32)
    return (counts > 0.5).astype(jnp.bfloat16)


LANES = 128
FACE_ROWS = 2 * 5


def _roll(t, shift, axis):
    if isinstance(shift, int):
        shift = shift % t.shape[axis]
        if shift == 0:
            return t
    return pltpu.roll(t, shift, axis)


def _z_roll(t, step):
    half = t.shape[0] // 2
    a, b = t[:half], t[half:]
    row = lax.broadcasted_iota(jnp.int32, a.shape, 0)
    if step == 1:
        ra, rb = _roll(a, 1, 0), _roll(b, 1, 0)
        edge = row == 0
    else:
        ra, rb = _roll(a, half - 1, 0), _roll(b, half - 1, 0)
        edge = row == half - 1
    return jnp.concatenate([jnp.where(edge, rb, ra), jnp.where(edge, ra, rb)], axis=0)


def _positions():
    flow_cycle = lax.axis_size("gy")
    me_y = lax.axis_index("gy")
    return me_y, (me_y + 1) % flow_cycle, (me_y - 1 + flow_cycle) % flow_cycle, lax.axis_index("gz")


def _emit_relax(cells_of_x, slab_width, relaxed_ref, chunk_ref, depth, plane_done=None):
    lane = lax.broadcasted_iota(jnp.int32, (depth, LANES), 1)
    up_pack = jnp.zeros((depth, LANES), jnp.float32)
    down_pack = jnp.zeros((depth, LANES), jnp.float32)
    top = bottom = None
    for x in range(slab_width):
        r = relax(cells_of_x(x))
        for m in range(19):
            relaxed_ref[m, x] = r[m]
        if plane_done is not None:
            plane_done(x)
        if x == slab_width - 1:
            top = corrected(r, upward, -1.0)
        if x == 0:
            bottom = corrected(r, downward, 1.0)
        for i, m in enumerate(y_plus):
            k = i * slab_width + x
            up_pack = jnp.where(lane == k, _roll(r[m], k + 1, 1), up_pack)
        for i, m in enumerate(y_minus):
            k = i * slab_width + x
            down_pack = jnp.where(lane == k, _roll(r[m], k, 1), down_pack)
    faces = jnp.concatenate([top.reshape(5 * depth, LANES), bottom.reshape(5 * depth, LANES)], axis=0)
    _, after, before, _ = _positions()
    to_next = jnp.full((depth, LANES), after, jnp.int32)
    to_prev = jnp.full((depth, LANES), before, jnp.int32)
    peers = chunk_ref.shape[0]
    for p in range(peers):
        chunk_ref[p, : FACE_ROWS * depth] = faces
        chunk_ref[p, FACE_ROWS * depth :] = jnp.where(to_next == p, up_pack, jnp.where(to_prev == p, down_pack, 0.0))


def _streamed(x, slab_width, relaxed_ref, rims_ref, low_ref, high_ref, hits_ref, depth):
    lane = lax.broadcasted_iota(jnp.int32, (depth, LANES), 1)
    out = []
    for n in range(19):
        step_x, step_y, step_z = velocity_table[n]
        xs = x - step_x
        if xs < 0:
            t = low_ref[upward.index(n)]
        elif xs >= slab_width:
            t = high_ref[downward.index(n)]
        else:
            t = relaxed_ref[n, xs]
            if step_y == 1:
                k = y_plus.index(n) * slab_width + xs
                t = jnp.where(lane == 0, _roll(rims_ref[0], LANES - k, 1), _roll(t, 1, 1))
            elif step_y == -1:
                k = y_minus.index(n) * slab_width + xs
                t = jnp.where(lane == LANES - 1, _roll(rims_ref[1], LANES - 1 - k, 1), _roll(t, LANES - 1, 1))
        if step_z != 0:
            t = _z_roll(t, step_z)
        out.append(t)
    result = [out[0]]
    for n in range(1, 19):
        source = n - 1 + 2 * (n % 2)
        result.append(jnp.where(hits_ref[source, x].astype(jnp.float32) > 0.5, relaxed_ref[source, x], out[n]))
    return result


class _Planes:
    def __init__(self, src, dst, sems):
        self.copies = [pltpu.make_async_copy(src.at[:, x], dst.at[:, x], sems.at[x]) for x in range(src.shape[1])]
        self.waited = set()

    def start(self, x=None):
        for i, c in enumerate(self.copies):
            if x is None or i == x:
                c.start()

    def need(self, *planes):
        for x in planes:
            if 0 <= x < len(self.copies) and x not in self.waited:
                self.copies[x].wait()
                self.waited.add(x)

    def finish(self):
        self.need(*range(len(self.copies)))


def _first_kernel(mine_hbm, other_hbm, relaxed_hbm, chunk_ref, mine_v, other_v, rel_v, sems):
    slab_width, half = mine_v.shape[1], mine_v.shape[2]
    depth = 2 * half
    lower = jnp.full((half, LANES), _positions()[3], jnp.int32) == 0
    mine = _Planes(mine_hbm, mine_v, sems.at[0])
    other = _Planes(other_hbm, other_v, sems.at[1])
    out = _Planes(rel_v, relaxed_hbm, sems.at[2])
    mine.start()
    other.start()

    def cells(x):
        mine.need(x)
        other.need(x)
        res = []
        for m in range(19):
            a, b = mine_v[m, x], other_v[m, x]
            res.append(jnp.concatenate([jnp.where(lower, a, b), jnp.where(lower, b, a)], axis=0))
        return res

    _emit_relax(cells, slab_width, rel_v, chunk_ref, depth, plane_done=out.start)
    out.finish()


def _middle_kernel(relaxed_hbm, hits_hbm, rims_ref, low_ref, high_ref, next_hbm, chunk_ref, rel_v, hits_v, out_v, sems):
    slab_width, depth = rel_v.shape[1], rel_v.shape[2]
    rel = _Planes(relaxed_hbm, rel_v, sems.at[0])
    hit = _Planes(hits_hbm, hits_v, sems.at[1])
    out = _Planes(out_v, next_hbm, sems.at[2])
    rel.start()
    hit.start()

    def cells(x):
        rel.need(x - 1, x, x + 1)
        hit.need(x)
        return _streamed(x, slab_width, rel_v, rims_ref, low_ref, high_ref, hits_v, depth)

    _emit_relax(cells, slab_width, out_v, chunk_ref, depth, plane_done=out.start)
    out.finish()


def _last_kernel(relaxed_hbm, hits_hbm, rims_ref, low_ref, high_ref, out_hbm, density_ref, rel_v, hits_v, out_v, sems):
    slab_width, depth = rel_v.shape[1], rel_v.shape[2]
    half = depth // 2
    lower = jnp.full((half, LANES), _positions()[3], jnp.int32) == 0
    rel = _Planes(relaxed_hbm, rel_v, sems.at[0])
    hit = _Planes(hits_hbm, hits_v, sems.at[1])
    out = _Planes(out_v, out_hbm, sems.at[2])
    rel.start()
    hit.start()
    for x in range(slab_width):
        rel.need(x - 1, x, x + 1)
        hit.need(x)
        cells = _streamed(x, slab_width, rel_v, rims_ref, low_ref, high_ref, hits_v, depth)
        mine = [jnp.where(lower, c[:half], c[half:]) for c in cells]
        for m in range(19):
            out_v[m, x] = mine[m]
        out.start(x)
        density_ref[x] = total_density(mine)
    out.finish()


def _window_kernel(section, shift_ref, frac_ref, got_ref, low_ref, high_ref, rims_ref):
    peers, _, lanes = got_ref.shape
    depth = low_ref.shape[1]
    me_y, after, before, _ = _positions()
    offset = shift_ref[section]
    fraction = jnp.full((depth, lanes), frac_ref[section], jnp.int32).astype(jnp.float32) / 256.0
    keep = 1.0 - fraction
    flow_cells = peers * lanes
    anchor = me_y * lanes
    lane = lax.broadcasted_iota(jnp.int32, (depth, lanes), 1)

    def window(row0, start):
        start = (start + 2 * flow_cells) % flow_cells
        block = start // lanes
        off = start % lanes
        after = (block + 1) % peers
        shift = (lanes - off) % lanes
        first = pltpu.roll(got_ref[block, pl.ds(row0, depth), :], shift, 1)
        second = pltpu.roll(got_ref[after, pl.ds(row0, depth), :], shift, 1)
        return jnp.where(lane < lanes - off, first, second)

    for i, m in enumerate(upward):
        step_y = velocity_table[m][1]
        row0 = i * depth
        a = anchor - offset - step_y
        low_ref[i] = keep * window(row0, a) + fraction * window(row0, a - 1)
    for i, m in enumerate(downward):
        step_y = velocity_table[m][1]
        row0 = (5 + i) * depth
        c = anchor + offset - step_y
        high_ref[i] = fraction * window(row0, c + 1) + keep * window(row0, c)
    rims_ref[0] = got_ref[before, pl.ds(FACE_ROWS * depth, depth), :]
    rims_ref[1] = got_ref[after, pl.ds(FACE_ROWS * depth, depth), :]


def _vmem():
    return pl.BlockSpec(memory_space=pltpu.VMEM)


def _smem():
    return pl.BlockSpec(memory_space=pltpu.SMEM)


def _any():
    return pl.BlockSpec(memory_space=pl.ANY)


def _call(kernel, in_kinds, out_shapes, out_kinds=None, scratch=()):
    kinds = {"s": _smem, "v": _vmem, "a": _any}
    out_kinds = out_kinds or "v" * len(out_shapes)
    return pl.pallas_call(
        kernel,
        out_shape=out_shapes,
        in_specs=[kinds[k]() for k in in_kinds],
        out_specs=tuple(kinds[k]() for k in out_kinds),
        scratch_shapes=list(scratch),
    )


def _per_device(populations, le_shift, le_frac, links):
    n_members, slab_width, half_depth, row_span = populations.shape
    flow_cycle = lax.axis_size("gy")
    slab_cycle = lax.axis_size("gx")
    me_y = lax.axis_index("gy")
    me_z = lax.axis_index("gz")
    anchor = me_y * row_span

    other_states = lax.ppermute(populations, "gz", [(0, 1), (1, 0)])
    other_links = lax.ppermute(links, "gz", [(0, 1), (1, 0)])
    all_links = jnp.where(
        me_z == 0, jnp.concatenate([links, other_links], axis=1), jnp.concatenate([other_links, links], axis=1)
    )
    depth = 2 * half_depth
    hits = link_hits(all_links, anchor, row_span)

    f32 = jnp.float32
    full = jax.ShapeDtypeStruct((n_members, slab_width, depth, row_span), f32)
    chunk = jax.ShapeDtypeStruct((flow_cycle, (FACE_ROWS + 1) * depth, row_span), f32)
    ghost = jax.ShapeDtypeStruct((5, depth, row_span), f32)
    rims = jax.ShapeDtypeStruct((2, depth, row_span), f32)
    own = jax.ShapeDtypeStruct((n_members, slab_width, half_depth, row_span), f32)
    density = jax.ShapeDtypeStruct((slab_width, half_depth, row_span), f32)

    half_full = (n_members, slab_width, half_depth, row_span)
    dma = pltpu.SemaphoreType.DMA((3, slab_width))
    relaxed, chunks = _call(
        _first_kernel, "aa", (full, chunk), "av",
        (pltpu.VMEM(half_full, f32), pltpu.VMEM(half_full, f32), pltpu.VMEM(full.shape, f32), dma),
    )(populations, other_states)
    stream_scratch = (
        pltpu.VMEM(full.shape, f32), pltpu.VMEM(full.shape, jnp.bfloat16), pltpu.VMEM(full.shape, f32), dma
    )
    for section in range(STEPS):
        got = lax.all_to_all(chunks, "gy", 0, 0, tiled=True)
        low_send, high_send, rim_pair = _call(functools.partial(_window_kernel, section), "ssv", (ghost, ghost, rims))(
            le_shift, le_frac, got
        )
        low_ghost = lax.ppermute(low_send, "gx", [(i, (i + 1) % slab_cycle) for i in range(slab_cycle)])
        high_ghost = lax.ppermute(high_send, "gx", [(i, (i - 1) % slab_cycle) for i in range(slab_cycle)])
        if section + 1 < STEPS:
            relaxed, chunks = _call(_middle_kernel, "aavvv", (full, chunk), "av", stream_scratch)(
                relaxed, hits, rim_pair, low_ghost, high_ghost
            )
        else:
            last_scratch = stream_scratch[:2] + (pltpu.VMEM(own.shape, f32), dma)
            final, dens = _call(_last_kernel, "aavvv", (own, density), "av", last_scratch)(
                relaxed, hits, rim_pair, low_ghost, high_ghost
            )
    return (final, dens)


def solution(mesh):
    in_specs = (P(None, "gx", "gz", "gy"), P(), P(), P("gx", "gz", "gy"))
    out_specs = (P(None, "gx", "gz", "gy"), P("gx", "gz", "gy"))
    return jax.shard_map(_per_device, mesh=mesh, in_specs=in_specs, out_specs=out_specs, check_vma=False)
```

```python
import functools

import jax
import jax.numpy as jnp
from jax import lax
from jax.sharding import PartitionSpec as P
from jax.experimental import pallas as pl
from jax.experimental.pallas import tpu as pltpu


STEPS = 2


velocity_table = (
    (0, 0, 0),
    (1, 0, 0),
    (-1, 0, 0),
    (0, 1, 0),
    (0, -1, 0),
    (0, 0, 1),
    (0, 0, -1),
    (1, 1, 0),
    (-1, -1, 0),
    (1, -1, 0),
    (-1, 1, 0),
    (1, 0, 1),
    (-1, 0, -1),
    (1, 0, -1),
    (-1, 0, 1),
    (0, 1, 1),
    (0, -1, -1),
    (0, 1, -1),
    (0, -1, 1),
)
weight_table = (1.0 / 3.0,) + (1.0 / 18.0,) * 6 + (1.0 / 36.0,) * 12
upward = (1, 7, 9, 11, 13)
downward = (2, 8, 10, 12, 14)
y_plus = tuple(m for m in range(19) if velocity_table[m][1] == 1)
y_minus = tuple(m for m in range(19) if velocity_table[m][1] == -1)
relax_rate = 1.25
plane_speed = 0.08


def total_density(states):
    density = states[0]
    for member in range(1, 19):
        density = density + states[member]
    return density


def moments(states):
    density = total_density(states)
    velocity = []
    for dim_index in range(3):
        momentum = None
        for member in range(19):
            sign_part = velocity_table[member][dim_index]
            if sign_part == 1:
                momentum = states[member] if momentum is None else momentum + states[member]
            elif sign_part == -1:
                momentum = momentum - states[member]
        velocity.append(momentum / density)
    return (density, velocity)


def speed_square(velocity):
    return velocity[0] * velocity[0] + velocity[1] * velocity[1] + velocity[2] * velocity[2]


def equilibrium(member, density, velocity, speed_sq):
    projected = None
    for dim_index in range(3):
        sign_part = velocity_table[member][dim_index]
        if sign_part != 0:
            summand = velocity[dim_index] if sign_part > 0 else -velocity[dim_index]
            projected = summand if projected is None else projected + summand
    if projected is None:
        return weight_table[member] * density * (1.0 - 1.5 * speed_sq)
    return (
        weight_table[member]
        * density
        * (1.0 + 3.0 * projected + 4.5 * projected * projected - 1.5 * speed_sq)
    )


def relax(states):
    density, velocity = moments(states)
    speed_sq = speed_square(velocity)
    return [
        states[member]
        + relax_rate * (equilibrium(member, density, velocity, speed_sq) - states[member])
        for member in range(19)
    ]


def corrected(plane, members, sign_part):
    density, velocity = moments(plane)
    speed_sq = speed_square(velocity)
    moved = [velocity[0], velocity[1] + sign_part * plane_speed, velocity[2]]
    moved_sq = speed_square(moved)
    return jnp.stack(
        [
            plane[member]
            + equilibrium(member, density, moved, moved_sq)
            - equilibrium(member, density, velocity, speed_sq)
            for member in members
        ]
    )


def link_hits(links, anchor, row_span):
    cell_y = links // 19 - anchor
    member = links % 19
    by_member = (member[:, :, None, :] == jnp.arange(19, dtype=jnp.int32)[:, None]).astype(jnp.bfloat16)
    by_cell = (cell_y[:, :, :, None] == jnp.arange(row_span, dtype=jnp.int32)).astype(jnp.bfloat16)
    return jnp.einsum("xzml,xzly->mxzy", by_member, by_cell, preferred_element_type=jnp.float32)


LANES = 128
FACE_ROWS = 2 * 5


def _roll(t, shift, axis):
    if isinstance(shift, int):
        shift = shift % t.shape[axis]
        if shift == 0:
            return t
    return pltpu.roll(t, shift, axis)


def _z_roll(t, step):
    half = t.shape[0] // 2
    a, b = t[:half], t[half:]
    row = lax.broadcasted_iota(jnp.int32, a.shape, 0)
    if step == 1:
        ra, rb = _roll(a, 1, 0), _roll(b, 1, 0)
        edge = row == 0
    else:
        ra, rb = _roll(a, half - 1, 0), _roll(b, half - 1, 0)
        edge = row == half - 1
    return jnp.concatenate([jnp.where(edge, rb, ra), jnp.where(edge, ra, rb)], axis=0)


def _positions():
    flow_cycle = lax.axis_size("gy")
    me_y = lax.axis_index("gy")
    return me_y, (me_y + 1) % flow_cycle, (me_y - 1 + flow_cycle) % flow_cycle, lax.axis_index("gz")


def _emit_relax(cells_of_x, slab_width, relaxed_ref, chunk_ref, depth):
    lane = lax.broadcasted_iota(jnp.int32, (depth, LANES), 1)
    up_pack = jnp.zeros((depth, LANES), jnp.float32)
    down_pack = jnp.zeros((depth, LANES), jnp.float32)
    top = bottom = None
    for x in range(slab_width):
        r = relax(cells_of_x(x))
        if relaxed_ref is not None:
            for m in range(19):
                relaxed_ref[m, x] = r[m]
        if chunk_ref is None:
            continue
        if x == slab_width - 1:
            top = corrected(r, upward, -1.0)
        if x == 0:
            bottom = corrected(r, downward, 1.0)
        for i, m in enumerate(y_plus):
            k = i * slab_width + x
            up_pack = jnp.where(lane == k, _roll(r[m], k + 1, 1), up_pack)
        for i, m in enumerate(y_minus):
            k = i * slab_width + x
            down_pack = jnp.where(lane == k, _roll(r[m], k, 1), down_pack)
    if chunk_ref is None:
        return
    faces = jnp.concatenate([top.reshape(5 * depth, LANES), bottom.reshape(5 * depth, LANES)], axis=0)
    _, after, before, _ = _positions()
    to_next = jnp.full((depth, LANES), after, jnp.int32)
    to_prev = jnp.full((depth, LANES), before, jnp.int32)
    peers = chunk_ref.shape[0]
    for p in range(peers):
        chunk_ref[p, : FACE_ROWS * depth] = faces
        chunk_ref[p, FACE_ROWS * depth :] = jnp.where(to_next == p, up_pack, jnp.where(to_prev == p, down_pack, 0.0))


def _streamed(x, slab_width, relaxed_ref, rims_ref, low_ref, high_ref, hits_ref, depth):
    lane = lax.broadcasted_iota(jnp.int32, (depth, LANES), 1)
    out = []
    for n in range(19):
        step_x, step_y, step_z = velocity_table[n]
        xs = x - step_x
        if xs < 0:
            t = low_ref[upward.index(n)]
        elif xs >= slab_width:
            t = high_ref[downward.index(n)]
        else:
            t = relaxed_ref[n, xs]
            if step_y == 1:
                k = y_plus.index(n) * slab_width + xs
                t = jnp.where(lane == 0, _roll(rims_ref[0], LANES - k, 1), _roll(t, 1, 1))
            elif step_y == -1:
                k = y_minus.index(n) * slab_width + xs
                t = jnp.where(lane == LANES - 1, _roll(rims_ref[1], LANES - 1 - k, 1), _roll(t, LANES - 1, 1))
        if step_z != 0:
            t = _z_roll(t, step_z)
        out.append(t)
    result = [out[0]]
    for n in range(1, 19):
        source = n - 1 + 2 * (n % 2)
        result.append(jnp.where(hits_ref[source, x] > 0.5, relaxed_ref[source, x], out[n]))
    return result


def _first_kernel(mine_ref, other_ref, *outs):
    relaxed_ref, chunk_ref = (outs[0], None) if outs[0].shape[0] == 19 else (None, outs[0])
    slab_width, half = mine_ref.shape[1], mine_ref.shape[2]
    depth = 2 * half
    lower = jnp.full((half, LANES), _positions()[3], jnp.int32) == 0

    def cells(x):
        out = []
        for m in range(19):
            a, b = mine_ref[m, x], other_ref[m, x]
            out.append(jnp.concatenate([jnp.where(lower, a, b), jnp.where(lower, b, a)], axis=0))
        return out

    _emit_relax(cells, slab_width, relaxed_ref, chunk_ref, depth)


def _middle_kernel(relaxed_ref, rims_ref, low_ref, high_ref, hits_ref, *outs):
    next_ref, chunk_ref = (outs[0], None) if outs[0].shape[0] == 19 else (None, outs[0])
    slab_width, depth = relaxed_ref.shape[1], relaxed_ref.shape[2]
    cells = lambda x: _streamed(x, slab_width, relaxed_ref, rims_ref, low_ref, high_ref, hits_ref, depth)
    _emit_relax(cells, slab_width, next_ref, chunk_ref, depth)


def _last_kernel(relaxed_ref, rims_ref, low_ref, high_ref, hits_ref, out_ref, density_ref):
    slab_width, depth = relaxed_ref.shape[1], relaxed_ref.shape[2]
    half = depth // 2
    lower = jnp.full((half, LANES), _positions()[3], jnp.int32) == 0
    for x in range(slab_width):
        cells = _streamed(x, slab_width, relaxed_ref, rims_ref, low_ref, high_ref, hits_ref, depth)
        mine = [jnp.where(lower, c[:half], c[half:]) for c in cells]
        for m in range(19):
            out_ref[m, x] = mine[m]
        density_ref[x] = total_density(mine)


def _window_kernel(section, shift_ref, frac_ref, got_ref, low_ref, high_ref, rims_ref):
    peers, _, lanes = got_ref.shape
    depth = low_ref.shape[1]
    me_y, after, before, _ = _positions()
    offset = shift_ref[section]
    fraction = jnp.full((depth, lanes), frac_ref[section], jnp.int32).astype(jnp.float32) / 256.0
    keep = 1.0 - fraction
    flow_cells = peers * lanes
    anchor = me_y * lanes
    lane = lax.broadcasted_iota(jnp.int32, (depth, lanes), 1)

    def window(row0, start):
        start = (start + 2 * flow_cells) % flow_cells
        block = start // lanes
        off = start % lanes
        after = (block + 1) % peers
        shift = (lanes - off) % lanes
        first = pltpu.roll(got_ref[block, pl.ds(row0, depth), :], shift, 1)
        second = pltpu.roll(got_ref[after, pl.ds(row0, depth), :], shift, 1)
        return jnp.where(lane < lanes - off, first, second)

    for i, m in enumerate(upward):
        step_y = velocity_table[m][1]
        row0 = i * depth
        a = anchor - offset - step_y
        low_ref[i] = keep * window(row0, a) + fraction * window(row0, a - 1)
    for i, m in enumerate(downward):
        step_y = velocity_table[m][1]
        row0 = (5 + i) * depth
        c = anchor + offset - step_y
        high_ref[i] = fraction * window(row0, c + 1) + keep * window(row0, c)
    rims_ref[0] = got_ref[before, pl.ds(FACE_ROWS * depth, depth), :]
    rims_ref[1] = got_ref[after, pl.ds(FACE_ROWS * depth, depth), :]


def _vmem():
    return pl.BlockSpec(memory_space=pltpu.VMEM)


def _smem():
    return pl.BlockSpec(memory_space=pltpu.SMEM)


def _call(kernel, n_smem, n_vmem, out_shapes):
    return pl.pallas_call(
        kernel,
        out_shape=out_shapes,
        in_specs=[_smem()] * n_smem + [_vmem()] * n_vmem,
        out_specs=tuple(_vmem() for _ in out_shapes) if isinstance(out_shapes, tuple) else _vmem(),
    )


def _per_device(populations, le_shift, le_frac, links):
    n_members, slab_width, half_depth, row_span = populations.shape
    flow_cycle = lax.axis_size("gy")
    slab_cycle = lax.axis_size("gx")
    me_y = lax.axis_index("gy")
    me_z = lax.axis_index("gz")
    anchor = me_y * row_span

    other_states = lax.ppermute(populations, "gz", [(0, 1), (1, 0)])
    other_links = lax.ppermute(links, "gz", [(0, 1), (1, 0)])
    all_links = jnp.where(
        me_z == 0, jnp.concatenate([links, other_links], axis=1), jnp.concatenate([other_links, links], axis=1)
    )
    depth = 2 * half_depth
    hits = link_hits(all_links, anchor, row_span)

    f32 = jnp.float32
    full = jax.ShapeDtypeStruct((n_members, slab_width, depth, row_span), f32)
    chunk = jax.ShapeDtypeStruct((flow_cycle, (FACE_ROWS + 1) * depth, row_span), f32)
    ghost = jax.ShapeDtypeStruct((5, depth, row_span), f32)
    rims = jax.ShapeDtypeStruct((2, depth, row_span), f32)
    own = jax.ShapeDtypeStruct((n_members, slab_width, half_depth, row_span), f32)
    density = jax.ShapeDtypeStruct((slab_width, half_depth, row_span), f32)

    chunks = _call(_first_kernel, 0, 2, chunk)(populations, other_states)
    relaxed = _call(_first_kernel, 0, 2, full)(populations, other_states)
    for section in range(STEPS):
        got = lax.all_to_all(chunks, "gy", 0, 0, tiled=True)
        low_send, high_send, rim_pair = _call(functools.partial(_window_kernel, section), 2, 1, (ghost, ghost, rims))(
            le_shift, le_frac, got
        )
        low_ghost = lax.ppermute(low_send, "gx", [(i, (i + 1) % slab_cycle) for i in range(slab_cycle)])
        high_ghost = lax.ppermute(high_send, "gx", [(i, (i - 1) % slab_cycle) for i in range(slab_cycle)])
        if section + 1 < STEPS:
            args = (relaxed, rim_pair, low_ghost, high_ghost, hits)
            chunks = _call(_middle_kernel, 0, 5, chunk)(*args)
            relaxed = _call(_middle_kernel, 0, 5, full)(*args)
        else:
            final, dens = _call(_last_kernel, 0, 5, (own, density))(relaxed, rim_pair, low_ghost, high_ghost, hits)
    return (final, dens)


def solution(mesh):
    in_specs = (P(None, "gx", "gz", "gy"), P(), P(), P("gx", "gz", "gy"))
    out_specs = (P(None, "gx", "gz", "gy"), P("gx", "gz", "gy"))
    return jax.shard_map(_per_device, mesh=mesh, in_specs=in_specs, out_specs=out_specs, check_vma=False)
```

```python
import functools

import jax
import jax.numpy as jnp
from jax import lax
from jax.sharding import PartitionSpec as P
from jax.experimental import pallas as pl
from jax.experimental.pallas import tpu as pltpu


STEPS = 2


velocity_table = (
    (0, 0, 0),
    (1, 0, 0),
    (-1, 0, 0),
    (0, 1, 0),
    (0, -1, 0),
    (0, 0, 1),
    (0, 0, -1),
    (1, 1, 0),
    (-1, -1, 0),
    (1, -1, 0),
    (-1, 1, 0),
    (1, 0, 1),
    (-1, 0, -1),
    (1, 0, -1),
    (-1, 0, 1),
    (0, 1, 1),
    (0, -1, -1),
    (0, 1, -1),
    (0, -1, 1),
)
weight_table = (1.0 / 3.0,) + (1.0 / 18.0,) * 6 + (1.0 / 36.0,) * 12
upward = (1, 7, 9, 11, 13)
downward = (2, 8, 10, 12, 14)
y_plus = tuple(m for m in range(19) if velocity_table[m][1] == 1)
y_minus = tuple(m for m in range(19) if velocity_table[m][1] == -1)
relax_rate = 1.25
plane_speed = 0.08


def total_density(states):
    density = states[0]
    for member in range(1, 19):
        density = density + states[member]
    return density


def moments(states):
    density = total_density(states)
    velocity = []
    for dim_index in range(3):
        momentum = None
        for member in range(19):
            sign_part = velocity_table[member][dim_index]
            if sign_part == 1:
                momentum = states[member] if momentum is None else momentum + states[member]
            elif sign_part == -1:
                momentum = momentum - states[member]
        velocity.append(momentum / density)
    return (density, velocity)


def speed_square(velocity):
    return velocity[0] * velocity[0] + velocity[1] * velocity[1] + velocity[2] * velocity[2]


def equilibrium(member, density, velocity, speed_sq):
    projected = None
    for dim_index in range(3):
        sign_part = velocity_table[member][dim_index]
        if sign_part != 0:
            summand = velocity[dim_index] if sign_part > 0 else -velocity[dim_index]
            projected = summand if projected is None else projected + summand
    if projected is None:
        return weight_table[member] * density * (1.0 - 1.5 * speed_sq)
    return (
        weight_table[member]
        * density
        * (1.0 + 3.0 * projected + 4.5 * projected * projected - 1.5 * speed_sq)
    )


def relax(states):
    density, velocity = moments(states)
    speed_sq = speed_square(velocity)
    return [
        states[member]
        + relax_rate * (equilibrium(member, density, velocity, speed_sq) - states[member])
        for member in range(19)
    ]


def corrected(plane, members, sign_part):
    density, velocity = moments(plane)
    speed_sq = speed_square(velocity)
    moved = [velocity[0], velocity[1] + sign_part * plane_speed, velocity[2]]
    moved_sq = speed_square(moved)
    return jnp.stack(
        [
            plane[member]
            + equilibrium(member, density, moved, moved_sq)
            - equilibrium(member, density, velocity, speed_sq)
            for member in members
        ]
    )


def link_hits(links, anchor, row_span):
    cell_y = links // 19 - anchor
    member = links % 19
    by_member = (member[:, :, None, :] == jnp.arange(19, dtype=jnp.int32)[:, None]).astype(jnp.bfloat16)
    by_cell = (cell_y[:, :, :, None] == jnp.arange(row_span, dtype=jnp.int32)).astype(jnp.bfloat16)
    counts = jnp.einsum("xzml,xzly->mxzy", by_member, by_cell, preferred_element_type=jnp.float32)
    return (counts > 0.5).astype(jnp.bfloat16)


LANES = 128
FACE_ROWS = 2 * 5


def _roll(t, shift, axis):
    if isinstance(shift, int):
        shift = shift % t.shape[axis]
        if shift == 0:
            return t
    return pltpu.roll(t, shift, axis)


def _z_roll(t, step):
    half = t.shape[0] // 2
    a, b = t[:half], t[half:]
    row = lax.broadcasted_iota(jnp.int32, a.shape, 0)
    if step == 1:
        ra, rb = _roll(a, 1, 0), _roll(b, 1, 0)
        edge = row == 0
    else:
        ra, rb = _roll(a, half - 1, 0), _roll(b, half - 1, 0)
        edge = row == half - 1
    return jnp.concatenate([jnp.where(edge, rb, ra), jnp.where(edge, ra, rb)], axis=0)


def _positions():
    flow_cycle = lax.axis_size("gy")
    me_y = lax.axis_index("gy")
    return me_y, (me_y + 1) % flow_cycle, (me_y - 1 + flow_cycle) % flow_cycle, lax.axis_index("gz")


def _emit_relax(cells_of_x, slab_width, relaxed_ref, chunk_ref, depth):
    lane = lax.broadcasted_iota(jnp.int32, (depth, LANES), 1)
    up_pack = jnp.zeros((depth, LANES), jnp.float32)
    down_pack = jnp.zeros((depth, LANES), jnp.float32)
    top = bottom = None
    for x in range(slab_width):
        r = relax(cells_of_x(x))
        if relaxed_ref is not None:
            for m in range(19):
                relaxed_ref[m, x] = r[m]
        if chunk_ref is None:
            continue
        if x == slab_width - 1:
            top = corrected(r, upward, -1.0)
        if x == 0:
            bottom = corrected(r, downward, 1.0)
        for i, m in enumerate(y_plus):
            k = i * slab_width + x
            up_pack = jnp.where(lane == k, _roll(r[m], k + 1, 1), up_pack)
        for i, m in enumerate(y_minus):
            k = i * slab_width + x
            down_pack = jnp.where(lane == k, _roll(r[m], k, 1), down_pack)
    if chunk_ref is None:
        return
    faces = jnp.concatenate([top.reshape(5 * depth, LANES), bottom.reshape(5 * depth, LANES)], axis=0)
    _, after, before, _ = _positions()
    to_next = jnp.full((depth, LANES), after, jnp.int32)
    to_prev = jnp.full((depth, LANES), before, jnp.int32)
    peers = chunk_ref.shape[0]
    for p in range(peers):
        chunk_ref[p, : FACE_ROWS * depth] = faces
        chunk_ref[p, FACE_ROWS * depth :] = jnp.where(to_next == p, up_pack, jnp.where(to_prev == p, down_pack, 0.0))


def _streamed(x, slab_width, relaxed_ref, rims_ref, low_ref, high_ref, hits_ref, depth, own=None):
    rows = depth if own is None else depth // 2
    part = (lambda ref, *idx: ref[idx]) if own is None else (lambda ref, *idx: ref[idx + (pl.ds(own, rows),)])
    lower = None if own is None else jnp.full((rows, LANES), own, jnp.int32) == 0

    def source(n, full):
        step_x, step_y, _ = velocity_table[n]
        get = (lambda ref, *idx: ref[idx]) if full else part
        width = depth if full else rows
        lane = lax.broadcasted_iota(jnp.int32, (width, LANES), 1)
        xs = x - step_x
        if xs < 0:
            return get(low_ref, upward.index(n))
        if xs >= slab_width:
            return get(high_ref, downward.index(n))
        t = get(relaxed_ref, n, xs)
        if step_y == 1:
            k = y_plus.index(n) * slab_width + xs
            t = jnp.where(lane == 0, _roll(get(rims_ref, 0), LANES - k, 1), _roll(t, 1, 1))
        elif step_y == -1:
            k = y_minus.index(n) * slab_width + xs
            t = jnp.where(lane == LANES - 1, _roll(get(rims_ref, 1), LANES - 1 - k, 1), _roll(t, LANES - 1, 1))
        return t

    out = []
    for n in range(19):
        step_z = velocity_table[n][2]
        if step_z == 0:
            out.append(source(n, own is None))
            continue
        t = _z_roll(source(n, True), step_z)
        if own is not None:
            t = jnp.where(lower, t[:rows], t[rows:])
        out.append(t)
    result = [out[0]]
    for n in range(1, 19):
        src = n - 1 + 2 * (n % 2)
        hit = part(hits_ref, src, x).astype(jnp.float32) > 0.5
        result.append(jnp.where(hit, part(relaxed_ref, src, x), out[n]))
    return result


def _first_kernel(mine_ref, other_ref, *outs):
    relaxed_ref, chunk_ref = (outs[0], None) if outs[0].shape[0] == 19 else (None, outs[0])
    slab_width, half = mine_ref.shape[1], mine_ref.shape[2]
    depth = 2 * half
    lower = jnp.full((half, LANES), _positions()[3], jnp.int32) == 0

    def cells(x):
        out = []
        for m in range(19):
            a, b = mine_ref[m, x], other_ref[m, x]
            out.append(jnp.concatenate([jnp.where(lower, a, b), jnp.where(lower, b, a)], axis=0))
        return out

    _emit_relax(cells, slab_width, relaxed_ref, chunk_ref, depth)


def _middle_kernel(relaxed_ref, rims_ref, low_ref, high_ref, hits_ref, *outs):
    next_ref, chunk_ref = (outs[0], None) if outs[0].shape[0] == 19 else (None, outs[0])
    slab_width, depth = relaxed_ref.shape[1], relaxed_ref.shape[2]
    cells = lambda x: _streamed(x, slab_width, relaxed_ref, rims_ref, low_ref, high_ref, hits_ref, depth)
    _emit_relax(cells, slab_width, next_ref, chunk_ref, depth)


def _last_kernel(relaxed_ref, rims_ref, low_ref, high_ref, hits_ref, out_ref, density_ref):
    slab_width, depth = relaxed_ref.shape[1], relaxed_ref.shape[2]
    half = depth // 2
    lower = jnp.full((half, LANES), _positions()[3], jnp.int32) == 0
    own = pl.multiple_of(_positions()[3] * half, half)
    for x in range(slab_width):
        mine = _streamed(x, slab_width, relaxed_ref, rims_ref, low_ref, high_ref, hits_ref, depth, own=own)
        for m in range(19):
            out_ref[m, x] = mine[m]
        density_ref[x] = total_density(mine)


def _window_kernel(section, shift_ref, frac_ref, got_ref, low_ref, high_ref, rims_ref):
    peers, _, lanes = got_ref.shape
    depth = low_ref.shape[1]
    me_y, after, before, _ = _positions()
    offset = shift_ref[section]
    fraction = jnp.full((depth, lanes), frac_ref[section], jnp.int32).astype(jnp.float32) / 256.0
    keep = 1.0 - fraction
    flow_cells = peers * lanes
    anchor = me_y * lanes
    lane = lax.broadcasted_iota(jnp.int32, (depth, lanes), 1)

    def window(row0, start):
        start = (start + 2 * flow_cells) % flow_cells
        block = start // lanes
        off = start % lanes
        after = (block + 1) % peers
        shift = (lanes - off) % lanes
        first = pltpu.roll(got_ref[block, pl.ds(row0, depth), :], shift, 1)
        second = pltpu.roll(got_ref[after, pl.ds(row0, depth), :], shift, 1)
        return jnp.where(lane < lanes - off, first, second)

    for i, m in enumerate(upward):
        step_y = velocity_table[m][1]
        row0 = i * depth
        a = anchor - offset - step_y
        low_ref[i] = keep * window(row0, a) + fraction * window(row0, a - 1)
    for i, m in enumerate(downward):
        step_y = velocity_table[m][1]
        row0 = (5 + i) * depth
        c = anchor + offset - step_y
        high_ref[i] = fraction * window(row0, c + 1) + keep * window(row0, c)
    rims_ref[0] = got_ref[before, pl.ds(FACE_ROWS * depth, depth), :]
    rims_ref[1] = got_ref[after, pl.ds(FACE_ROWS * depth, depth), :]


def _vmem():
    return pl.BlockSpec(memory_space=pltpu.VMEM)


def _smem():
    return pl.BlockSpec(memory_space=pltpu.SMEM)


def _call(kernel, n_smem, n_vmem, out_shapes):
    return pl.pallas_call(
        kernel,
        out_shape=out_shapes,
        in_specs=[_smem()] * n_smem + [_vmem()] * n_vmem,
        out_specs=tuple(_vmem() for _ in out_shapes) if isinstance(out_shapes, tuple) else _vmem(),
    )


def _per_device(populations, le_shift, le_frac, links):
    n_members, slab_width, half_depth, row_span = populations.shape
    flow_cycle = lax.axis_size("gy")
    slab_cycle = lax.axis_size("gx")
    me_y = lax.axis_index("gy")
    me_z = lax.axis_index("gz")
    anchor = me_y * row_span

    other_states = lax.ppermute(populations, "gz", [(0, 1), (1, 0)])
    other_links = lax.ppermute(links, "gz", [(0, 1), (1, 0)])
    all_links = jnp.where(
        me_z == 0, jnp.concatenate([links, other_links], axis=1), jnp.concatenate([other_links, links], axis=1)
    )
    depth = 2 * half_depth
    hits = link_hits(all_links, anchor, row_span)

    f32 = jnp.float32
    full = jax.ShapeDtypeStruct((n_members, slab_width, depth, row_span), f32)
    chunk = jax.ShapeDtypeStruct((flow_cycle, (FACE_ROWS + 1) * depth, row_span), f32)
    ghost = jax.ShapeDtypeStruct((5, depth, row_span), f32)
    rims = jax.ShapeDtypeStruct((2, depth, row_span), f32)
    own = jax.ShapeDtypeStruct((n_members, slab_width, half_depth, row_span), f32)
    density = jax.ShapeDtypeStruct((slab_width, half_depth, row_span), f32)

    chunks = _call(_first_kernel, 0, 2, chunk)(populations, other_states)
    relaxed = _call(_first_kernel, 0, 2, full)(populations, other_states)
    for section in range(STEPS):
        got = lax.all_to_all(chunks, "gy", 0, 0, tiled=True)
        low_send, high_send, rim_pair = _call(functools.partial(_window_kernel, section), 2, 1, (ghost, ghost, rims))(
            le_shift, le_frac, got
        )
        low_ghost = lax.ppermute(low_send, "gx", [(i, (i + 1) % slab_cycle) for i in range(slab_cycle)])
        high_ghost = lax.ppermute(high_send, "gx", [(i, (i - 1) % slab_cycle) for i in range(slab_cycle)])
        if section + 1 < STEPS:
            args = (relaxed, rim_pair, low_ghost, high_ghost, hits)
            chunks = _call(_middle_kernel, 0, 5, chunk)(*args)
            relaxed = _call(_middle_kernel, 0, 5, full)(*args)
        else:
            final, dens = _call(_last_kernel, 0, 5, (own, density))(relaxed, rim_pair, low_ghost, high_ghost, hits)
    return (final, dens)


def solution(mesh):
    in_specs = (P(None, "gx", "gz", "gy"), P(), P(), P("gx", "gz", "gy"))
    out_specs = (P(None, "gx", "gz", "gy"), P("gx", "gz", "gy"))
    return jax.shard_map(_per_device, mesh=mesh, in_specs=in_specs, out_specs=out_specs, check_vma=False)
```

```python
import functools

import jax
import jax.numpy as jnp
from jax import lax
from jax.sharding import PartitionSpec as P
from jax.experimental import pallas as pl
from jax.experimental.pallas import tpu as pltpu


STEPS = 2


velocity_table = (
    (0, 0, 0),
    (1, 0, 0),
    (-1, 0, 0),
    (0, 1, 0),
    (0, -1, 0),
    (0, 0, 1),
    (0, 0, -1),
    (1, 1, 0),
    (-1, -1, 0),
    (1, -1, 0),
    (-1, 1, 0),
    (1, 0, 1),
    (-1, 0, -1),
    (1, 0, -1),
    (-1, 0, 1),
    (0, 1, 1),
    (0, -1, -1),
    (0, 1, -1),
    (0, -1, 1),
)
weight_table = (1.0 / 3.0,) + (1.0 / 18.0,) * 6 + (1.0 / 36.0,) * 12
upward = (1, 7, 9, 11, 13)
downward = (2, 8, 10, 12, 14)
y_plus = tuple(m for m in range(19) if velocity_table[m][1] == 1)
y_minus = tuple(m for m in range(19) if velocity_table[m][1] == -1)
relax_rate = 1.25
plane_speed = 0.08


def total_density(states):
    density = states[0]
    for member in range(1, 19):
        density = density + states[member]
    return density


def moments(states):
    density = total_density(states)
    velocity = []
    for dim_index in range(3):
        momentum = None
        for member in range(19):
            sign_part = velocity_table[member][dim_index]
            if sign_part == 1:
                momentum = states[member] if momentum is None else momentum + states[member]
            elif sign_part == -1:
                momentum = momentum - states[member]
        velocity.append(momentum / density)
    return (density, velocity)


def speed_square(velocity):
    return velocity[0] * velocity[0] + velocity[1] * velocity[1] + velocity[2] * velocity[2]


def equilibrium(member, density, velocity, speed_sq):
    projected = None
    for dim_index in range(3):
        sign_part = velocity_table[member][dim_index]
        if sign_part != 0:
            summand = velocity[dim_index] if sign_part > 0 else -velocity[dim_index]
            projected = summand if projected is None else projected + summand
    if projected is None:
        return weight_table[member] * density * (1.0 - 1.5 * speed_sq)
    return (
        weight_table[member]
        * density
        * (1.0 + 3.0 * projected + 4.5 * projected * projected - 1.5 * speed_sq)
    )


def relax(states):
    density, velocity = moments(states)
    speed_sq = speed_square(velocity)
    return [
        states[member]
        + relax_rate * (equilibrium(member, density, velocity, speed_sq) - states[member])
        for member in range(19)
    ]


def corrected(plane, members, sign_part):
    density, velocity = moments(plane)
    speed_sq = speed_square(velocity)
    moved = [velocity[0], velocity[1] + sign_part * plane_speed, velocity[2]]
    moved_sq = speed_square(moved)
    return jnp.stack(
        [
            plane[member]
            + equilibrium(member, density, moved, moved_sq)
            - equilibrium(member, density, velocity, speed_sq)
            for member in members
        ]
    )


def link_hits(links, anchor, row_span):
    cell_y = links // 19 - anchor
    member = links % 19
    by_member = (member[:, :, None, :] == jnp.arange(19, dtype=jnp.int32)[:, None]).astype(jnp.bfloat16)
    by_cell = (cell_y[:, :, :, None] == jnp.arange(row_span, dtype=jnp.int32)).astype(jnp.bfloat16)
    counts = jnp.einsum("xzml,xzly->mxzy", by_member, by_cell, preferred_element_type=jnp.float32)
    return (counts > 0.5).astype(jnp.bfloat16)


LANES = 128
FACE_ROWS = 2 * 5


def _roll(t, shift, axis):
    if isinstance(shift, int):
        shift = shift % t.shape[axis]
        if shift == 0:
            return t
    return pltpu.roll(t, shift, axis)


def _z_roll(t, step):
    half = t.shape[0] // 2
    a, b = t[:half], t[half:]
    row = lax.broadcasted_iota(jnp.int32, a.shape, 0)
    if step == 1:
        ra, rb = _roll(a, 1, 0), _roll(b, 1, 0)
        edge = row == 0
    else:
        ra, rb = _roll(a, half - 1, 0), _roll(b, half - 1, 0)
        edge = row == half - 1
    return jnp.concatenate([jnp.where(edge, rb, ra), jnp.where(edge, ra, rb)], axis=0)


def _positions():
    flow_cycle = lax.axis_size("gy")
    me_y = lax.axis_index("gy")
    return me_y, (me_y + 1) % flow_cycle, (me_y - 1 + flow_cycle) % flow_cycle, lax.axis_index("gz")


def _emit_relax(cells_of_x, slab_width, relaxed_ref, chunk_ref, depth):
    lane = lax.broadcasted_iota(jnp.int32, (depth, LANES), 1)
    up_pack = jnp.zeros((depth, LANES), jnp.float32)
    down_pack = jnp.zeros((depth, LANES), jnp.float32)
    top = bottom = None
    for x in range(slab_width):
        r = relax(cells_of_x(x))
        if relaxed_ref is not None:
            for m in range(19):
                relaxed_ref[m, x] = r[m]
        if chunk_ref is None:
            continue
        if x == slab_width - 1:
            top = corrected(r, upward, -1.0)
        if x == 0:
            bottom = corrected(r, downward, 1.0)
        for i, m in enumerate(y_plus):
            k = i * slab_width + x
            up_pack = jnp.where(lane == k, _roll(r[m], k + 1, 1), up_pack)
        for i, m in enumerate(y_minus):
            k = i * slab_width + x
            down_pack = jnp.where(lane == k, _roll(r[m], k, 1), down_pack)
    if chunk_ref is None:
        return
    half = depth // 2
    peers = chunk_ref.shape[0]
    for h in range(2):
        rows = slice(h * half, (h + 1) * half)
        faces = jnp.concatenate(
            [top[:, rows].reshape(5 * half, LANES), bottom[:, rows].reshape(5 * half, LANES)], axis=0
        )
        for p in range(peers):
            chunk_ref[p, h, : FACE_ROWS * half] = faces
            chunk_ref[p, h, FACE_ROWS * half : (FACE_ROWS + 1) * half] = up_pack[rows]
            chunk_ref[p, h, (FACE_ROWS + 1) * half :] = down_pack[rows]


def _streamed(x, slab_width, relaxed_ref, rims_ref, low_ref, high_ref, hits_ref, depth, own=None):
    rows = depth if own is None else depth // 2
    part = (lambda ref, *idx: ref[idx]) if own is None else (lambda ref, *idx: ref[idx + (pl.ds(own, rows),)])
    lower = None if own is None else jnp.full((rows, LANES), own, jnp.int32) == 0

    def source(n, full):
        step_x, step_y, _ = velocity_table[n]
        get = (lambda ref, *idx: ref[idx]) if full else part
        width = depth if full else rows
        lane = lax.broadcasted_iota(jnp.int32, (width, LANES), 1)
        xs = x - step_x
        if xs < 0:
            return get(low_ref, upward.index(n))
        if xs >= slab_width:
            return get(high_ref, downward.index(n))
        t = get(relaxed_ref, n, xs)
        if step_y == 1:
            k = y_plus.index(n) * slab_width + xs
            t = jnp.where(lane == 0, _roll(get(rims_ref, 0), LANES - k, 1), _roll(t, 1, 1))
        elif step_y == -1:
            k = y_minus.index(n) * slab_width + xs
            t = jnp.where(lane == LANES - 1, _roll(get(rims_ref, 1), LANES - 1 - k, 1), _roll(t, LANES - 1, 1))
        return t

    out = []
    for n in range(19):
        step_z = velocity_table[n][2]
        if step_z == 0:
            out.append(source(n, own is None))
            continue
        t = _z_roll(source(n, True), step_z)
        if own is not None:
            t = jnp.where(lower, t[:rows], t[rows:])
        out.append(t)
    result = [out[0]]
    for n in range(1, 19):
        src = n - 1 + 2 * (n % 2)
        hit = part(hits_ref, src, x).astype(jnp.float32) > 0.5
        result.append(jnp.where(hit, part(relaxed_ref, src, x), out[n]))
    return result


def _first_kernel(mine_ref, other_ref, *outs):
    relaxed_ref, chunk_ref = (outs[0], None) if outs[0].shape[0] == 19 else (None, outs[0])
    slab_width, half = mine_ref.shape[1], mine_ref.shape[2]
    depth = 2 * half
    lower = jnp.full((half, LANES), _positions()[3], jnp.int32) == 0

    def cells(x):
        out = []
        for m in range(19):
            a, b = mine_ref[m, x], other_ref[m, x]
            out.append(jnp.concatenate([jnp.where(lower, a, b), jnp.where(lower, b, a)], axis=0))
        return out

    _emit_relax(cells, slab_width, relaxed_ref, chunk_ref, depth)


def _half_kernel(mine_ref, half_ref):
    slab_width, half = mine_ref.shape[1], mine_ref.shape[2]
    lane = lax.broadcasted_iota(jnp.int32, (half, LANES), 1)
    up_pack = jnp.zeros((half, LANES), jnp.float32)
    down_pack = jnp.zeros((half, LANES), jnp.float32)
    for x in range(slab_width):
        r = relax([mine_ref[m, x] for m in range(19)])
        if x == slab_width - 1:
            half_ref[: 5 * half] = corrected(r, upward, -1.0).reshape(5 * half, LANES)
        if x == 0:
            half_ref[5 * half : FACE_ROWS * half] = corrected(r, downward, 1.0).reshape(5 * half, LANES)
        for i, m in enumerate(y_plus):
            k = i * slab_width + x
            up_pack = jnp.where(lane == k, _roll(r[m], k + 1, 1), up_pack)
        for i, m in enumerate(y_minus):
            k = i * slab_width + x
            down_pack = jnp.where(lane == k, _roll(r[m], k, 1), down_pack)
    half_ref[FACE_ROWS * half : (FACE_ROWS + 1) * half] = up_pack
    half_ref[(FACE_ROWS + 1) * half :] = down_pack


def _middle_kernel(relaxed_ref, rims_ref, low_ref, high_ref, hits_ref, *outs):
    next_ref, chunk_ref = (outs[0], None) if outs[0].shape[0] == 19 else (None, outs[0])
    slab_width, depth = relaxed_ref.shape[1], relaxed_ref.shape[2]
    cells = lambda x: _streamed(x, slab_width, relaxed_ref, rims_ref, low_ref, high_ref, hits_ref, depth)
    _emit_relax(cells, slab_width, next_ref, chunk_ref, depth)


def _last_kernel(relaxed_ref, rims_ref, low_ref, high_ref, hits_ref, out_ref, density_ref):
    slab_width, depth = relaxed_ref.shape[1], relaxed_ref.shape[2]
    half = depth // 2
    lower = jnp.full((half, LANES), _positions()[3], jnp.int32) == 0
    own = pl.multiple_of(_positions()[3] * half, half)
    for x in range(slab_width):
        mine = _streamed(x, slab_width, relaxed_ref, rims_ref, low_ref, high_ref, hits_ref, depth, own=own)
        for m in range(19):
            out_ref[m, x] = mine[m]
        density_ref[x] = total_density(mine)


def _window_kernel(section, shift_ref, frac_ref, got_ref, low_ref, high_ref, rims_ref):
    peers, _, _, lanes = got_ref.shape
    depth = low_ref.shape[1]
    half = depth // 2

    def tile(block, row0):
        return jnp.concatenate([got_ref[block, 0, pl.ds(row0, half), :], got_ref[block, 1, pl.ds(row0, half), :]], axis=0)

    me_y, after, before, _ = _positions()
    offset = shift_ref[section]
    fraction = jnp.full((depth, lanes), frac_ref[section], jnp.int32).astype(jnp.float32) / 256.0
    keep = 1.0 - fraction
    flow_cells = peers * lanes
    anchor = me_y * lanes
    lane = lax.broadcasted_iota(jnp.int32, (depth, lanes), 1)

    def window(row0, start):
        start = (start + 2 * flow_cells) % flow_cells
        block = start // lanes
        off = start % lanes
        after = (block + 1) % peers
        shift = (lanes - off) % lanes
        first = pltpu.roll(tile(block, row0), shift, 1)
        second = pltpu.roll(tile(after, row0), shift, 1)
        return jnp.where(lane < lanes - off, first, second)

    for i, m in enumerate(upward):
        step_y = velocity_table[m][1]
        row0 = i * half
        a = anchor - offset - step_y
        low_ref[i] = keep * window(row0, a) + fraction * window(row0, a - 1)
    for i, m in enumerate(downward):
        step_y = velocity_table[m][1]
        row0 = (5 + i) * half
        c = anchor + offset - step_y
        high_ref[i] = fraction * window(row0, c + 1) + keep * window(row0, c)
    rims_ref[0] = tile(before, FACE_ROWS * half)
    rims_ref[1] = tile(after, (FACE_ROWS + 1) * half)


def _vmem():
    return pl.BlockSpec(memory_space=pltpu.VMEM)


def _smem():
    return pl.BlockSpec(memory_space=pltpu.SMEM)


def _call(kernel, n_smem, n_vmem, out_shapes):
    return pl.pallas_call(
        kernel,
        out_shape=out_shapes,
        in_specs=[_smem()] * n_smem + [_vmem()] * n_vmem,
        out_specs=tuple(_vmem() for _ in out_shapes) if isinstance(out_shapes, tuple) else _vmem(),
    )


def _per_device(populations, le_shift, le_frac, links):
    n_members, slab_width, half_depth, row_span = populations.shape
    flow_cycle = lax.axis_size("gy")
    slab_cycle = lax.axis_size("gx")
    me_y = lax.axis_index("gy")
    me_z = lax.axis_index("gz")
    anchor = me_y * row_span

    other_states = lax.ppermute(populations, "gz", [(0, 1), (1, 0)])
    other_links = lax.ppermute(links, "gz", [(0, 1), (1, 0)])
    all_links = jnp.where(
        me_z == 0, jnp.concatenate([links, other_links], axis=1), jnp.concatenate([other_links, links], axis=1)
    )
    depth = 2 * half_depth
    hits = link_hits(all_links, anchor, row_span)

    f32 = jnp.float32
    full = jax.ShapeDtypeStruct((n_members, slab_width, depth, row_span), f32)
    chunk = jax.ShapeDtypeStruct((flow_cycle, 2, (FACE_ROWS + 2) * half_depth, row_span), f32)
    ghost = jax.ShapeDtypeStruct((5, depth, row_span), f32)
    rims = jax.ShapeDtypeStruct((2, depth, row_span), f32)
    own = jax.ShapeDtypeStruct((n_members, slab_width, half_depth, row_span), f32)
    density = jax.ShapeDtypeStruct((slab_width, half_depth, row_span), f32)

    half_rows = (FACE_ROWS + 2) * half_depth
    mine_half = _call(_half_kernel, 0, 1, jax.ShapeDtypeStruct((half_rows, row_span), f32))(populations)
    other_half = lax.ppermute(mine_half, "gz", [(0, 1), (1, 0)])
    both = jnp.where(me_z == 0, jnp.stack([mine_half, other_half]), jnp.stack([other_half, mine_half]))
    chunks = jnp.broadcast_to(both[None], (flow_cycle,) + both.shape)
    relaxed = _call(_first_kernel, 0, 2, full)(populations, other_states)
    for section in range(STEPS):
        got = lax.all_to_all(chunks, "gy", 0, 0, tiled=True)
        low_send, high_send, rim_pair = _call(functools.partial(_window_kernel, section), 2, 1, (ghost, ghost, rims))(
            le_shift, le_frac, got
        )
        low_ghost = lax.ppermute(low_send, "gx", [(i, (i + 1) % slab_cycle) for i in range(slab_cycle)])
        high_ghost = lax.ppermute(high_send, "gx", [(i, (i - 1) % slab_cycle) for i in range(slab_cycle)])
        if section + 1 < STEPS:
            args = (relaxed, rim_pair, low_ghost, high_ghost, hits)
            chunks = _call(_middle_kernel, 0, 5, chunk)(*args)
            relaxed = _call(_middle_kernel, 0, 5, full)(*args)
        else:
            final, dens = _call(_last_kernel, 0, 5, (own, density))(relaxed, rim_pair, low_ghost, high_ghost, hits)
    return (final, dens)


def solution(mesh):
    in_specs = (P(None, "gx", "gz", "gy"), P(), P(), P("gx", "gz", "gy"))
    out_specs = (P(None, "gx", "gz", "gy"), P("gx", "gz", "gy"))
    return jax.shard_map(_per_device, mesh=mesh, in_specs=in_specs, out_specs=out_specs, check_vma=False)
```

```python
import functools

import jax
import jax.numpy as jnp
from jax import lax
from jax.sharding import PartitionSpec as P
from jax.experimental import pallas as pl
from jax.experimental.pallas import tpu as pltpu


STEPS = 2


velocity_table = (
    (0, 0, 0),
    (1, 0, 0),
    (-1, 0, 0),
    (0, 1, 0),
    (0, -1, 0),
    (0, 0, 1),
    (0, 0, -1),
    (1, 1, 0),
    (-1, -1, 0),
    (1, -1, 0),
    (-1, 1, 0),
    (1, 0, 1),
    (-1, 0, -1),
    (1, 0, -1),
    (-1, 0, 1),
    (0, 1, 1),
    (0, -1, -1),
    (0, 1, -1),
    (0, -1, 1),
)
weight_table = (1.0 / 3.0,) + (1.0 / 18.0,) * 6 + (1.0 / 36.0,) * 12
upward = (1, 7, 9, 11, 13)
downward = (2, 8, 10, 12, 14)
y_plus = tuple(m for m in range(19) if velocity_table[m][1] == 1)
y_minus = tuple(m for m in range(19) if velocity_table[m][1] == -1)
relax_rate = 1.25
plane_speed = 0.08


def total_density(states):
    density = states[0]
    for member in range(1, 19):
        density = density + states[member]
    return density


def moments(states):
    density = total_density(states)
    velocity = []
    for dim_index in range(3):
        momentum = None
        for member in range(19):
            sign_part = velocity_table[member][dim_index]
            if sign_part == 1:
                momentum = states[member] if momentum is None else momentum + states[member]
            elif sign_part == -1:
                momentum = momentum - states[member]
        velocity.append(momentum / density)
    return (density, velocity)


def speed_square(velocity):
    return velocity[0] * velocity[0] + velocity[1] * velocity[1] + velocity[2] * velocity[2]


def equilibrium(member, density, velocity, speed_sq):
    projected = None
    for dim_index in range(3):
        sign_part = velocity_table[member][dim_index]
        if sign_part != 0:
            summand = velocity[dim_index] if sign_part > 0 else -velocity[dim_index]
            projected = summand if projected is None else projected + summand
    if projected is None:
        return weight_table[member] * density * (1.0 - 1.5 * speed_sq)
    return (
        weight_table[member]
        * density
        * (1.0 + 3.0 * projected + 4.5 * projected * projected - 1.5 * speed_sq)
    )


def relax(states):
    density, velocity = moments(states)
    speed_sq = speed_square(velocity)
    return [
        states[member]
        + relax_rate * (equilibrium(member, density, velocity, speed_sq) - states[member])
        for member in range(19)
    ]


def corrected(plane, members, sign_part):
    density, velocity = moments(plane)
    speed_sq = speed_square(velocity)
    moved = [velocity[0], velocity[1] + sign_part * plane_speed, velocity[2]]
    moved_sq = speed_square(moved)
    return jnp.stack(
        [
            plane[member]
            + equilibrium(member, density, moved, moved_sq)
            - equilibrium(member, density, velocity, speed_sq)
            for member in members
        ]
    )


def link_hits(links, anchor, row_span):
    cell_y = links // 19 - anchor
    member = links % 19
    by_member = (member[:, :, None, :] == jnp.arange(19, dtype=jnp.int32)[:, None]).astype(jnp.bfloat16)
    by_cell = (cell_y[:, :, :, None] == jnp.arange(row_span, dtype=jnp.int32)).astype(jnp.bfloat16)
    counts = jnp.einsum("xzml,xzly->mxzy", by_member, by_cell, preferred_element_type=jnp.float32)
    return (counts > 0.5).astype(jnp.bfloat16)


LANES = 128
FACE_ROWS = 2 * 5


def _roll(t, shift, axis):
    if isinstance(shift, int):
        shift = shift % t.shape[axis]
        if shift == 0:
            return t
    return pltpu.roll(t, shift, axis)


def _z_roll(t, step):
    half = t.shape[0] // 2
    a, b = t[:half], t[half:]
    row = lax.broadcasted_iota(jnp.int32, a.shape, 0)
    if step == 1:
        ra, rb = _roll(a, 1, 0), _roll(b, 1, 0)
        edge = row == 0
    else:
        ra, rb = _roll(a, half - 1, 0), _roll(b, half - 1, 0)
        edge = row == half - 1
    return jnp.concatenate([jnp.where(edge, rb, ra), jnp.where(edge, ra, rb)], axis=0)


def _positions():
    flow_cycle = lax.axis_size("gy")
    me_y = lax.axis_index("gy")
    return me_y, (me_y + 1) % flow_cycle, (me_y - 1 + flow_cycle) % flow_cycle, lax.axis_index("gz")


def _emit_relax(cells_of_x, slab_width, relaxed_ref, chunk_ref, depth, planes=None, packs_in=None, packs_ref=None):
    lane = lax.broadcasted_iota(jnp.int32, (depth, LANES), 1)
    if packs_in is None:
        up_pack = jnp.zeros((depth, LANES), jnp.float32)
        down_pack = jnp.zeros((depth, LANES), jnp.float32)
    else:
        up_pack, down_pack = packs_in[0], packs_in[1]
    top = bottom = None
    packing = chunk_ref is not None or packs_ref is not None
    for x in range(slab_width) if planes is None else planes:
        r = relax(cells_of_x(x))
        if relaxed_ref is not None:
            for m in range(19):
                relaxed_ref[m, x] = r[m]
        if not packing:
            continue
        if x == slab_width - 1:
            top = corrected(r, upward, -1.0)
        if x == 0:
            bottom = corrected(r, downward, 1.0)
        for i, m in enumerate(y_plus):
            k = i * slab_width + x
            up_pack = jnp.where(lane == k, _roll(r[m], k + 1, 1), up_pack)
        for i, m in enumerate(y_minus):
            k = i * slab_width + x
            down_pack = jnp.where(lane == k, _roll(r[m], k, 1), down_pack)
    if packs_ref is not None:
        packs_ref[0] = up_pack
        packs_ref[1] = down_pack
    if chunk_ref is None:
        return
    faces = jnp.concatenate([top.reshape(5 * depth, LANES), bottom.reshape(5 * depth, LANES)], axis=0)
    _, after, before, _ = _positions()
    to_next = jnp.full((depth, LANES), after, jnp.int32)
    to_prev = jnp.full((depth, LANES), before, jnp.int32)
    peers = chunk_ref.shape[0]
    for p in range(peers):
        chunk_ref[p, : FACE_ROWS * depth] = faces
        chunk_ref[p, FACE_ROWS * depth :] = jnp.where(to_next == p, up_pack, jnp.where(to_prev == p, down_pack, 0.0))


def _streamed(x, slab_width, relaxed_ref, rims_ref, low_ref, high_ref, hits_ref, depth, own=None):
    rows = depth if own is None else depth // 2
    part = (lambda ref, *idx: ref[idx]) if own is None else (lambda ref, *idx: ref[idx + (pl.ds(own, rows),)])
    lower = None if own is None else jnp.full((rows, LANES), own, jnp.int32) == 0

    def source(n, full):
        step_x, step_y, _ = velocity_table[n]
        get = (lambda ref, *idx: ref[idx]) if full else part
        width = depth if full else rows
        lane = lax.broadcasted_iota(jnp.int32, (width, LANES), 1)
        xs = x - step_x
        if xs < 0:
            return get(low_ref, upward.index(n))
        if xs >= slab_width:
            return get(high_ref, downward.index(n))
        t = get(relaxed_ref, n, xs)
        if step_y == 1:
            k = y_plus.index(n) * slab_width + xs
            t = jnp.where(lane == 0, _roll(get(rims_ref, 0), LANES - k, 1), _roll(t, 1, 1))
        elif step_y == -1:
            k = y_minus.index(n) * slab_width + xs
            t = jnp.where(lane == LANES - 1, _roll(get(rims_ref, 1), LANES - 1 - k, 1), _roll(t, LANES - 1, 1))
        return t

    out = []
    for n in range(19):
        step_z = velocity_table[n][2]
        if step_z == 0:
            out.append(source(n, own is None))
            continue
        t = _z_roll(source(n, True), step_z)
        if own is not None:
            t = jnp.where(lower, t[:rows], t[rows:])
        out.append(t)
    result = [out[0]]
    for n in range(1, 19):
        src = n - 1 + 2 * (n % 2)
        hit = part(hits_ref, src, x).astype(jnp.float32) > 0.5
        result.append(jnp.where(hit, part(relaxed_ref, src, x), out[n]))
    return result


def _first_kernel(mine_ref, other_ref, *outs):
    relaxed_ref, chunk_ref = (outs[0], None) if outs[0].shape[0] == 19 else (None, outs[0])
    slab_width, half = mine_ref.shape[1], mine_ref.shape[2]
    depth = 2 * half
    lower = jnp.full((half, LANES), _positions()[3], jnp.int32) == 0

    def cells(x):
        out = []
        for m in range(19):
            a, b = mine_ref[m, x], other_ref[m, x]
            out.append(jnp.concatenate([jnp.where(lower, a, b), jnp.where(lower, b, a)], axis=0))
        return out

    _emit_relax(cells, slab_width, relaxed_ref, chunk_ref, depth)


def _middle_kernel(relaxed_ref, rims_ref, low_ref, high_ref, hits_ref, *outs):
    next_ref, chunk_ref = (outs[0], None) if outs[0].shape[0] == 19 else (None, outs[0])
    slab_width, depth = relaxed_ref.shape[1], relaxed_ref.shape[2]
    cells = lambda x: _streamed(x, slab_width, relaxed_ref, rims_ref, low_ref, high_ref, hits_ref, depth)
    _emit_relax(cells, slab_width, next_ref, chunk_ref, depth)


def _interior_kernel(relaxed_ref, rims_ref, hits_ref, packs_ref):
    slab_width, depth = relaxed_ref.shape[1], relaxed_ref.shape[2]
    cells = lambda x: _streamed(x, slab_width, relaxed_ref, rims_ref, None, None, hits_ref, depth)
    _emit_relax(cells, slab_width, None, None, depth, planes=range(1, slab_width - 1), packs_ref=packs_ref)


def _boundary_kernel(relaxed_ref, rims_ref, low_ref, high_ref, hits_ref, packs_ref, chunk_ref):
    slab_width, depth = relaxed_ref.shape[1], relaxed_ref.shape[2]
    cells = lambda x: _streamed(x, slab_width, relaxed_ref, rims_ref, low_ref, high_ref, hits_ref, depth)
    _emit_relax(cells, slab_width, None, chunk_ref, depth, planes=(0, slab_width - 1), packs_in=packs_ref)


def _last_planes(planes, relaxed_ref, rims_ref, low_ref, high_ref, hits_ref, put):
    slab_width, depth = relaxed_ref.shape[1], relaxed_ref.shape[2]
    half = depth // 2
    own = pl.multiple_of(_positions()[3] * half, half)
    for slot, x in enumerate(planes):
        mine = _streamed(x, slab_width, relaxed_ref, rims_ref, low_ref, high_ref, hits_ref, depth, own=own)
        put(slot, x, mine)


def _last_interior(relaxed_ref, rims_ref, hits_ref, out_ref, density_ref):
    slab_width = relaxed_ref.shape[1]

    def put(slot, x, mine):
        for m in range(19):
            out_ref[m, x] = mine[m]
        density_ref[x] = total_density(mine)

    _last_planes(range(1, slab_width - 1), relaxed_ref, rims_ref, None, None, hits_ref, put)


def _last_boundary(relaxed_ref, rims_ref, low_ref, high_ref, hits_ref, out_in, dens_in, out_hbm, dens_hbm, out_v, dens_v, sems):
    slab_width = relaxed_ref.shape[1]
    planes = (0, slab_width - 1)

    def put(slot, x, mine):
        for m in range(19):
            out_v[m, slot] = mine[m]
        dens_v[slot] = total_density(mine)

    _last_planes(planes, relaxed_ref, rims_ref, low_ref, high_ref, hits_ref, put)
    copies = []
    for slot, x in enumerate(planes):
        copies.append(pltpu.make_async_copy(out_v.at[:, slot], out_hbm.at[:, x], sems.at[0, slot]))
        copies.append(pltpu.make_async_copy(dens_v.at[slot], dens_hbm.at[x], sems.at[1, slot]))
    for c in copies:
        c.start()
    for c in copies:
        c.wait()


def _window_kernel(section, shift_ref, frac_ref, got_ref, low_ref, high_ref, rims_ref):
    peers, _, lanes = got_ref.shape
    depth = low_ref.shape[1]
    me_y, after, before, _ = _positions()
    offset = shift_ref[section]
    fraction = jnp.full((depth, lanes), frac_ref[section], jnp.int32).astype(jnp.float32) / 256.0
    keep = 1.0 - fraction
    flow_cells = peers * lanes
    anchor = me_y * lanes
    lane = lax.broadcasted_iota(jnp.int32, (depth, lanes), 1)

    def window(row0, start):
        start = (start + 2 * flow_cells) % flow_cells
        block = start // lanes
        off = start % lanes
        after = (block + 1) % peers
        shift = (lanes - off) % lanes
        first = pltpu.roll(got_ref[block, pl.ds(row0, depth), :], shift, 1)
        second = pltpu.roll(got_ref[after, pl.ds(row0, depth), :], shift, 1)
        return jnp.where(lane < lanes - off, first, second)

    for i, m in enumerate(upward):
        step_y = velocity_table[m][1]
        row0 = i * depth
        a = anchor - offset - step_y
        low_ref[i] = keep * window(row0, a) + fraction * window(row0, a - 1)
    for i, m in enumerate(downward):
        step_y = velocity_table[m][1]
        row0 = (5 + i) * depth
        c = anchor + offset - step_y
        high_ref[i] = fraction * window(row0, c + 1) + keep * window(row0, c)
    rims_ref[0] = got_ref[before, pl.ds(FACE_ROWS * depth, depth), :]
    rims_ref[1] = got_ref[after, pl.ds(FACE_ROWS * depth, depth), :]


def _vmem():
    return pl.BlockSpec(memory_space=pltpu.VMEM)


def _smem():
    return pl.BlockSpec(memory_space=pltpu.SMEM)


def _call(kernel, n_smem, n_vmem, out_shapes):
    return pl.pallas_call(
        kernel,
        out_shape=out_shapes,
        in_specs=[_smem()] * n_smem + [_vmem()] * n_vmem,
        out_specs=tuple(_vmem() for _ in out_shapes) if isinstance(out_shapes, tuple) else _vmem(),
    )


def _per_device(populations, le_shift, le_frac, links):
    n_members, slab_width, half_depth, row_span = populations.shape
    flow_cycle = lax.axis_size("gy")
    slab_cycle = lax.axis_size("gx")
    me_y = lax.axis_index("gy")
    me_z = lax.axis_index("gz")
    anchor = me_y * row_span

    other_states = lax.ppermute(populations, "gz", [(0, 1), (1, 0)])
    other_links = lax.ppermute(links, "gz", [(0, 1), (1, 0)])
    all_links = jnp.where(
        me_z == 0, jnp.concatenate([links, other_links], axis=1), jnp.concatenate([other_links, links], axis=1)
    )
    depth = 2 * half_depth
    hits = link_hits(all_links, anchor, row_span)

    f32 = jnp.float32
    full = jax.ShapeDtypeStruct((n_members, slab_width, depth, row_span), f32)
    chunk = jax.ShapeDtypeStruct((flow_cycle, (FACE_ROWS + 1) * depth, row_span), f32)
    ghost = jax.ShapeDtypeStruct((5, depth, row_span), f32)
    rims = jax.ShapeDtypeStruct((2, depth, row_span), f32)
    own = jax.ShapeDtypeStruct((n_members, slab_width, half_depth, row_span), f32)
    density = jax.ShapeDtypeStruct((slab_width, half_depth, row_span), f32)

    chunks = _call(_first_kernel, 0, 2, chunk)(populations, other_states)
    relaxed = _call(_first_kernel, 0, 2, full)(populations, other_states)
    for section in range(STEPS):
        got = lax.all_to_all(chunks, "gy", 0, 0, tiled=True)
        low_send, high_send, rim_pair = _call(functools.partial(_window_kernel, section), 2, 1, (ghost, ghost, rims))(
            le_shift, le_frac, got
        )
        low_ghost = lax.ppermute(low_send, "gx", [(i, (i + 1) % slab_cycle) for i in range(slab_cycle)])
        high_ghost = lax.ppermute(high_send, "gx", [(i, (i - 1) % slab_cycle) for i in range(slab_cycle)])
        if section + 1 < STEPS:
            args = (relaxed, rim_pair, low_ghost, high_ghost, hits)
            packs = _call(_interior_kernel, 0, 3, rims)(relaxed, rim_pair, hits)
            chunks = _call(_boundary_kernel, 0, 6, chunk)(relaxed, rim_pair, low_ghost, high_ghost, hits, packs)
            relaxed = _call(_middle_kernel, 0, 5, full)(*args)
        else:
            part, part_dens = _call(_last_interior, 0, 3, (own, density))(relaxed, rim_pair, hits)
            final, dens = pl.pallas_call(
                _last_boundary,
                out_shape=(own, density),
                in_specs=[_vmem()] * 5 + [pl.BlockSpec(memory_space=pl.ANY)] * 2,
                out_specs=(pl.BlockSpec(memory_space=pl.ANY), pl.BlockSpec(memory_space=pl.ANY)),
                scratch_shapes=[
                    pltpu.VMEM((n_members, 2, half_depth, row_span), f32),
                    pltpu.VMEM((2, half_depth, row_span), f32),
                    pltpu.SemaphoreType.DMA((2, 2)),
                ],
                input_output_aliases={5: 0, 6: 1},
            )(relaxed, rim_pair, low_ghost, high_ghost, hits, part, part_dens)
    return (final, dens)


def solution(mesh):
    in_specs = (P(None, "gx", "gz", "gy"), P(), P(), P("gx", "gz", "gy"))
    out_specs = (P(None, "gx", "gz", "gy"), P("gx", "gz", "gy"))
    return jax.shard_map(_per_device, mesh=mesh, in_specs=in_specs, out_specs=out_specs, check_vma=False)
```

```python
import functools

import jax
import jax.numpy as jnp
from jax import lax
from jax.sharding import PartitionSpec as P
from jax.experimental import pallas as pl
from jax.experimental.pallas import tpu as pltpu


STEPS = 2


velocity_table = (
    (0, 0, 0),
    (1, 0, 0),
    (-1, 0, 0),
    (0, 1, 0),
    (0, -1, 0),
    (0, 0, 1),
    (0, 0, -1),
    (1, 1, 0),
    (-1, -1, 0),
    (1, -1, 0),
    (-1, 1, 0),
    (1, 0, 1),
    (-1, 0, -1),
    (1, 0, -1),
    (-1, 0, 1),
    (0, 1, 1),
    (0, -1, -1),
    (0, 1, -1),
    (0, -1, 1),
)
weight_table = (1.0 / 3.0,) + (1.0 / 18.0,) * 6 + (1.0 / 36.0,) * 12
upward = (1, 7, 9, 11, 13)
downward = (2, 8, 10, 12, 14)
y_plus = tuple(m for m in range(19) if velocity_table[m][1] == 1)
y_minus = tuple(m for m in range(19) if velocity_table[m][1] == -1)
relax_rate = 1.25
plane_speed = 0.08


def total_density(states):
    density = states[0]
    for member in range(1, 19):
        density = density + states[member]
    return density


def moments(states):
    density = total_density(states)
    velocity = []
    for dim_index in range(3):
        momentum = None
        for member in range(19):
            sign_part = velocity_table[member][dim_index]
            if sign_part == 1:
                momentum = states[member] if momentum is None else momentum + states[member]
            elif sign_part == -1:
                momentum = momentum - states[member]
        velocity.append(momentum / density)
    return (density, velocity)


def speed_square(velocity):
    return velocity[0] * velocity[0] + velocity[1] * velocity[1] + velocity[2] * velocity[2]


def equilibrium(member, density, velocity, speed_sq):
    projected = None
    for dim_index in range(3):
        sign_part = velocity_table[member][dim_index]
        if sign_part != 0:
            summand = velocity[dim_index] if sign_part > 0 else -velocity[dim_index]
            projected = summand if projected is None else projected + summand
    if projected is None:
        return weight_table[member] * density * (1.0 - 1.5 * speed_sq)
    return (
        weight_table[member]
        * density
        * (1.0 + 3.0 * projected + 4.5 * projected * projected - 1.5 * speed_sq)
    )


def relax(states):
    density, velocity = moments(states)
    speed_sq = speed_square(velocity)
    return [
        states[member]
        + relax_rate * (equilibrium(member, density, velocity, speed_sq) - states[member])
        for member in range(19)
    ]


def corrected(plane, members, sign_part):
    density, velocity = moments(plane)
    speed_sq = speed_square(velocity)
    moved = [velocity[0], velocity[1] + sign_part * plane_speed, velocity[2]]
    moved_sq = speed_square(moved)
    return jnp.stack(
        [
            plane[member]
            + equilibrium(member, density, moved, moved_sq)
            - equilibrium(member, density, velocity, speed_sq)
            for member in members
        ]
    )


def link_hits(links, anchor, row_span):
    cell_y = links // 19 - anchor
    member = links % 19
    by_member = (member[:, :, None, :] == jnp.arange(19, dtype=jnp.int32)[:, None]).astype(jnp.bfloat16)
    by_cell = (cell_y[:, :, :, None] == jnp.arange(row_span, dtype=jnp.int32)).astype(jnp.bfloat16)
    counts = jnp.einsum("xzml,xzly->xzym", by_member, by_cell, preferred_element_type=jnp.float32)
    bits = jnp.left_shift(1, jnp.arange(19, dtype=jnp.int32))
    return jnp.sum(jnp.where(counts > 0.5, bits, 0), axis=-1, dtype=jnp.int32)


LANES = 128
FACE_ROWS = 2 * 5


def _roll(t, shift, axis):
    if isinstance(shift, int):
        shift = shift % t.shape[axis]
        if shift == 0:
            return t
    return pltpu.roll(t, shift, axis)


def _z_roll(t, step):
    half = t.shape[0] // 2
    a, b = t[:half], t[half:]
    row = lax.broadcasted_iota(jnp.int32, a.shape, 0)
    if step == 1:
        ra, rb = _roll(a, 1, 0), _roll(b, 1, 0)
        edge = row == 0
    else:
        ra, rb = _roll(a, half - 1, 0), _roll(b, half - 1, 0)
        edge = row == half - 1
    return jnp.concatenate([jnp.where(edge, rb, ra), jnp.where(edge, ra, rb)], axis=0)


def _positions():
    flow_cycle = lax.axis_size("gy")
    me_y = lax.axis_index("gy")
    return me_y, (me_y + 1) % flow_cycle, (me_y - 1 + flow_cycle) % flow_cycle, lax.axis_index("gz")


def _emit_relax(cells_of_x, slab_width, relaxed_ref, chunk_ref, depth):
    lane = lax.broadcasted_iota(jnp.int32, (depth, LANES), 1)
    up_pack = jnp.zeros((depth, LANES), jnp.float32)
    down_pack = jnp.zeros((depth, LANES), jnp.float32)
    top = bottom = None
    for x in range(slab_width):
        r = relax(cells_of_x(x))
        if relaxed_ref is not None:
            for m in range(19):
                relaxed_ref[m, x] = r[m]
        if chunk_ref is None:
            continue
        if x == slab_width - 1:
            top = corrected(r, upward, -1.0)
        if x == 0:
            bottom = corrected(r, downward, 1.0)
        for i, m in enumerate(y_plus):
            k = i * slab_width + x
            up_pack = jnp.where(lane == k, _roll(r[m], k + 1, 1), up_pack)
        for i, m in enumerate(y_minus):
            k = i * slab_width + x
            down_pack = jnp.where(lane == k, _roll(r[m], k, 1), down_pack)
    if chunk_ref is None:
        return
    faces = jnp.concatenate([top.reshape(5 * depth, LANES), bottom.reshape(5 * depth, LANES)], axis=0)
    _, after, before, _ = _positions()
    to_next = jnp.full((depth, LANES), after, jnp.int32)
    to_prev = jnp.full((depth, LANES), before, jnp.int32)
    peers = chunk_ref.shape[0]
    for p in range(peers):
        chunk_ref[p, : FACE_ROWS * depth] = faces
        chunk_ref[p, FACE_ROWS * depth :] = jnp.where(to_next == p, up_pack, jnp.where(to_prev == p, down_pack, 0.0))


def _streamed(x, slab_width, relaxed_ref, rims_ref, low_ref, high_ref, hits_ref, depth, own=None):
    rows = depth if own is None else depth // 2
    part = (lambda ref, *idx: ref[idx]) if own is None else (lambda ref, *idx: ref[idx + (pl.ds(own, rows),)])
    lower = None if own is None else jnp.full((rows, LANES), own, jnp.int32) == 0

    def source(n, full):
        step_x, step_y, _ = velocity_table[n]
        get = (lambda ref, *idx: ref[idx]) if full else part
        width = depth if full else rows
        lane = lax.broadcasted_iota(jnp.int32, (width, LANES), 1)
        xs = x - step_x
        if xs < 0:
            return get(low_ref, upward.index(n))
        if xs >= slab_width:
            return get(high_ref, downward.index(n))
        t = get(relaxed_ref, n, xs)
        if step_y == 1:
            k = y_plus.index(n) * slab_width + xs
            t = jnp.where(lane == 0, _roll(get(rims_ref, 0), LANES - k, 1), _roll(t, 1, 1))
        elif step_y == -1:
            k = y_minus.index(n) * slab_width + xs
            t = jnp.where(lane == LANES - 1, _roll(get(rims_ref, 1), LANES - 1 - k, 1), _roll(t, LANES - 1, 1))
        return t

    out = []
    for n in range(19):
        step_z = velocity_table[n][2]
        if step_z == 0:
            out.append(source(n, own is None))
            continue
        t = _z_roll(source(n, True), step_z)
        if own is not None:
            t = jnp.where(lower, t[:rows], t[rows:])
        out.append(t)
    result = [out[0]]
    for n in range(1, 19):
        src = n - 1 + 2 * (n % 2)
        hit = jnp.bitwise_and(jnp.right_shift(part(hits_ref, x), src), 1) != 0
        result.append(jnp.where(hit, part(relaxed_ref, src, x), out[n]))
    return result


def _first_kernel(mine_ref, other_ref, *outs):
    relaxed_ref, chunk_ref = (outs[0], None) if outs[0].shape[0] == 19 else (None, outs[0])
    slab_width, half = mine_ref.shape[1], mine_ref.shape[2]
    depth = 2 * half
    lower = jnp.full((half, LANES), _positions()[3], jnp.int32) == 0

    def cells(x):
        out = []
        for m in range(19):
            a, b = mine_ref[m, x], other_ref[m, x]
            out.append(jnp.concatenate([jnp.where(lower, a, b), jnp.where(lower, b, a)], axis=0))
        return out

    _emit_relax(cells, slab_width, relaxed_ref, chunk_ref, depth)


def _middle_kernel(relaxed_ref, rims_ref, low_ref, high_ref, hits_ref, *outs):
    next_ref, chunk_ref = (outs[0], None) if outs[0].shape[0] == 19 else (None, outs[0])
    slab_width, depth = relaxed_ref.shape[1], relaxed_ref.shape[2]
    cells = lambda x: _streamed(x, slab_width, relaxed_ref, rims_ref, low_ref, high_ref, hits_ref, depth)
    _emit_relax(cells, slab_width, next_ref, chunk_ref, depth)


def _last_kernel(relaxed_ref, rims_ref, low_ref, high_ref, hits_ref, out_ref, density_ref):
    slab_width, depth = relaxed_ref.shape[1], relaxed_ref.shape[2]
    half = depth // 2
    lower = jnp.full((half, LANES), _positions()[3], jnp.int32) == 0
    own = pl.multiple_of(_positions()[3] * half, half)
    for x in range(slab_width):
        mine = _streamed(x, slab_width, relaxed_ref, rims_ref, low_ref, high_ref, hits_ref, depth, own=own)
        for m in range(19):
            out_ref[m, x] = mine[m]
        density_ref[x] = total_density(mine)


def _window_kernel(section, shift_ref, frac_ref, got_hbm, low_ref, high_ref, rims_ref, faces_v, rim_v, sems):
    peers, _, lanes = got_hbm.shape
    depth = low_ref.shape[1]
    me_y, after, before, _ = _positions()
    offset = shift_ref[section]
    fraction = jnp.full((depth, lanes), frac_ref[section], jnp.int32).astype(jnp.float32) / 256.0
    keep = 1.0 - fraction
    flow_cells = peers * lanes
    anchor = me_y * lanes
    lane = lax.broadcasted_iota(jnp.int32, (depth, lanes), 1)
    face_rows = 5 * depth
    firsts = [
        ((anchor - offset - 2 + 2 * flow_cells) % flow_cells) // lanes,
        ((anchor + offset - 1 + flow_cells) % flow_cells) // lanes,
    ]
    copies = []
    for f in range(2):
        for b in range(3):
            block = (firsts[f] + b) % peers
            copies.append(
                pltpu.make_async_copy(
                    got_hbm.at[block, pl.ds(f * face_rows, face_rows)], faces_v.at[f, b], sems.at[f * 3 + b]
                )
            )
    rim_rows = pl.ds(FACE_ROWS * depth, depth)
    copies.append(pltpu.make_async_copy(got_hbm.at[before, rim_rows], rim_v.at[0], sems.at[6]))
    copies.append(pltpu.make_async_copy(got_hbm.at[after, rim_rows], rim_v.at[1], sems.at[7]))
    for c in copies:
        c.start()
    for c in copies:
        c.wait()

    def window(f, row0, start):
        start = (start + 2 * flow_cells) % flow_cells
        block = start // lanes
        off = start % lanes
        near = (block - firsts[f] + peers) % peers
        shift = (lanes - off) % lanes
        first = pltpu.roll(faces_v[f, near, pl.ds(row0, depth), :], shift, 1)
        second = pltpu.roll(faces_v[f, near + 1, pl.ds(row0, depth), :], shift, 1)
        return jnp.where(lane < lanes - off, first, second)

    for i, m in enumerate(upward):
        step_y = velocity_table[m][1]
        a = anchor - offset - step_y
        low_ref[i] = keep * window(0, i * depth, a) + fraction * window(0, i * depth, a - 1)
    for i, m in enumerate(downward):
        step_y = velocity_table[m][1]
        c = anchor + offset - step_y
        high_ref[i] = fraction * window(1, i * depth, c + 1) + keep * window(1, i * depth, c)
    rims_ref[0] = rim_v[0]
    rims_ref[1] = rim_v[1]


def _vmem():
    return pl.BlockSpec(memory_space=pltpu.VMEM)


def _smem():
    return pl.BlockSpec(memory_space=pltpu.SMEM)


def _call(kernel, n_smem, n_vmem, out_shapes):
    return pl.pallas_call(
        kernel,
        out_shape=out_shapes,
        in_specs=[_smem()] * n_smem + [_vmem()] * n_vmem,
        out_specs=tuple(_vmem() for _ in out_shapes) if isinstance(out_shapes, tuple) else _vmem(),
    )


def _per_device(populations, le_shift, le_frac, links):
    n_members, slab_width, half_depth, row_span = populations.shape
    flow_cycle = lax.axis_size("gy")
    slab_cycle = lax.axis_size("gx")
    me_y = lax.axis_index("gy")
    me_z = lax.axis_index("gz")
    anchor = me_y * row_span

    other_states = lax.ppermute(populations, "gz", [(0, 1), (1, 0)])
    other_links = lax.ppermute(links, "gz", [(0, 1), (1, 0)])
    all_links = jnp.where(
        me_z == 0, jnp.concatenate([links, other_links], axis=1), jnp.concatenate([other_links, links], axis=1)
    )
    depth = 2 * half_depth
    hits = link_hits(all_links, anchor, row_span)

    f32 = jnp.float32
    full = jax.ShapeDtypeStruct((n_members, slab_width, depth, row_span), f32)
    chunk = jax.ShapeDtypeStruct((flow_cycle, (FACE_ROWS + 1) * depth, row_span), f32)
    ghost = jax.ShapeDtypeStruct((5, depth, row_span), f32)
    rims = jax.ShapeDtypeStruct((2, depth, row_span), f32)
    own = jax.ShapeDtypeStruct((n_members, slab_width, half_depth, row_span), f32)
    density = jax.ShapeDtypeStruct((slab_width, half_depth, row_span), f32)

    chunks = _call(_first_kernel, 0, 2, chunk)(populations, other_states)
    relaxed = _call(_first_kernel, 0, 2, full)(populations, other_states)
    for section in range(STEPS):
        got = lax.all_to_all(chunks, "gy", 0, 0, tiled=True)
        low_send, high_send, rim_pair = pl.pallas_call(
            functools.partial(_window_kernel, section),
            out_shape=(ghost, ghost, rims),
            in_specs=[_smem(), _smem(), pl.BlockSpec(memory_space=pl.ANY)],
            out_specs=(_vmem(), _vmem(), _vmem()),
            scratch_shapes=[
                pltpu.VMEM((2, 3, 5 * depth, row_span), f32),
                pltpu.VMEM((2, depth, row_span), f32),
                pltpu.SemaphoreType.DMA((8,)),
            ],
        )(le_shift, le_frac, got)
        low_ghost = lax.ppermute(low_send, "gx", [(i, (i + 1) % slab_cycle) for i in range(slab_cycle)])
        high_ghost = lax.ppermute(high_send, "gx", [(i, (i - 1) % slab_cycle) for i in range(slab_cycle)])
        if section + 1 < STEPS:
            args = (relaxed, rim_pair, low_ghost, high_ghost, hits)
            chunks = _call(_middle_kernel, 0, 5, chunk)(*args)
            relaxed = _call(_middle_kernel, 0, 5, full)(*args)
        else:
            final, dens = _call(_last_kernel, 0, 5, (own, density))(relaxed, rim_pair, low_ghost, high_ghost, hits)
    return (final, dens)


def solution(mesh):
    in_specs = (P(None, "gx", "gz", "gy"), P(), P(), P("gx", "gz", "gy"))
    out_specs = (P(None, "gx", "gz", "gy"), P("gx", "gz", "gy"))
    return jax.shard_map(_per_device, mesh=mesh, in_specs=in_specs, out_specs=out_specs, check_vma=False)
```

```python
import functools

import jax
import jax.numpy as jnp
from jax import lax
from jax.sharding import PartitionSpec as P
from jax.experimental import pallas as pl
from jax.experimental.pallas import tpu as pltpu


STEPS = 2


velocity_table = (
    (0, 0, 0),
    (1, 0, 0),
    (-1, 0, 0),
    (0, 1, 0),
    (0, -1, 0),
    (0, 0, 1),
    (0, 0, -1),
    (1, 1, 0),
    (-1, -1, 0),
    (1, -1, 0),
    (-1, 1, 0),
    (1, 0, 1),
    (-1, 0, -1),
    (1, 0, -1),
    (-1, 0, 1),
    (0, 1, 1),
    (0, -1, -1),
    (0, 1, -1),
    (0, -1, 1),
)
weight_table = (1.0 / 3.0,) + (1.0 / 18.0,) * 6 + (1.0 / 36.0,) * 12
upward = (1, 7, 9, 11, 13)
downward = (2, 8, 10, 12, 14)
y_plus = tuple(m for m in range(19) if velocity_table[m][1] == 1)
y_minus = tuple(m for m in range(19) if velocity_table[m][1] == -1)
relax_rate = 1.25
plane_speed = 0.08


def total_density(states):
    density = states[0]
    for member in range(1, 19):
        density = density + states[member]
    return density


def moments(states):
    density = total_density(states)
    velocity = []
    for dim_index in range(3):
        momentum = None
        for member in range(19):
            sign_part = velocity_table[member][dim_index]
            if sign_part == 1:
                momentum = states[member] if momentum is None else momentum + states[member]
            elif sign_part == -1:
                momentum = momentum - states[member]
        velocity.append(momentum / density)
    return (density, velocity)


def speed_square(velocity):
    return velocity[0] * velocity[0] + velocity[1] * velocity[1] + velocity[2] * velocity[2]


def equilibrium(member, density, velocity, speed_sq):
    projected = None
    for dim_index in range(3):
        sign_part = velocity_table[member][dim_index]
        if sign_part != 0:
            summand = velocity[dim_index] if sign_part > 0 else -velocity[dim_index]
            projected = summand if projected is None else projected + summand
    if projected is None:
        return weight_table[member] * density * (1.0 - 1.5 * speed_sq)
    return (
        weight_table[member]
        * density
        * (1.0 + 3.0 * projected + 4.5 * projected * projected - 1.5 * speed_sq)
    )


def relax(states):
    density, velocity = moments(states)
    speed_sq = speed_square(velocity)
    return [
        states[member]
        + relax_rate * (equilibrium(member, density, velocity, speed_sq) - states[member])
        for member in range(19)
    ]


def corrected(plane, members, sign_part):
    density, velocity = moments(plane)
    speed_sq = speed_square(velocity)
    moved = [velocity[0], velocity[1] + sign_part * plane_speed, velocity[2]]
    moved_sq = speed_square(moved)
    return jnp.stack(
        [
            plane[member]
            + equilibrium(member, density, moved, moved_sq)
            - equilibrium(member, density, velocity, speed_sq)
            for member in members
        ]
    )


def link_hits(links, anchor, row_span):
    cell_y = links // 19 - anchor
    member = links % 19
    by_member = (member[:, :, None, :] == jnp.arange(19, dtype=jnp.int32)[:, None]).astype(jnp.bfloat16)
    by_cell = (cell_y[:, :, :, None] == jnp.arange(row_span, dtype=jnp.int32)).astype(jnp.bfloat16)
    counts = jnp.einsum("xzml,xzly->xzym", by_member, by_cell, preferred_element_type=jnp.float32)
    bits = jnp.left_shift(1, jnp.arange(19, dtype=jnp.int32))
    return jnp.sum(jnp.where(counts > 0.5, bits, 0), axis=-1, dtype=jnp.int32)


LANES = 128
FACE_ROWS = 2 * 5


def _roll(t, shift, axis):
    if isinstance(shift, int):
        shift = shift % t.shape[axis]
        if shift == 0:
            return t
    return pltpu.roll(t, shift, axis)


def _z_roll(t, step):
    half = t.shape[0] // 2
    a, b = t[:half], t[half:]
    row = lax.broadcasted_iota(jnp.int32, a.shape, 0)
    if step == 1:
        ra, rb = _roll(a, 1, 0), _roll(b, 1, 0)
        edge = row == 0
    else:
        ra, rb = _roll(a, half - 1, 0), _roll(b, half - 1, 0)
        edge = row == half - 1
    return jnp.concatenate([jnp.where(edge, rb, ra), jnp.where(edge, ra, rb)], axis=0)


def _positions():
    flow_cycle = lax.axis_size("gy")
    me_y = lax.axis_index("gy")
    return me_y, (me_y + 1) % flow_cycle, (me_y - 1 + flow_cycle) % flow_cycle, lax.axis_index("gz")


def _emit_relax(cells_of_x, slab_width, relaxed_ref, chunk_ref, depth):
    lane = lax.broadcasted_iota(jnp.int32, (depth, LANES), 1)
    up_pack = jnp.zeros((depth, LANES), jnp.float32)
    down_pack = jnp.zeros((depth, LANES), jnp.float32)
    top = bottom = None
    for x in range(slab_width):
        r = relax(cells_of_x(x))
        if relaxed_ref is not None:
            for m in range(19):
                relaxed_ref[m, x] = r[m]
        if chunk_ref is None:
            continue
        if x == slab_width - 1:
            top = corrected(r, upward, -1.0)
        if x == 0:
            bottom = corrected(r, downward, 1.0)
        for i, m in enumerate(y_plus):
            k = i * slab_width + x
            up_pack = jnp.where(lane == k, _roll(r[m], k + 1, 1), up_pack)
        for i, m in enumerate(y_minus):
            k = i * slab_width + x
            down_pack = jnp.where(lane == k, _roll(r[m], k, 1), down_pack)
    if chunk_ref is None:
        return
    faces = jnp.concatenate([top.reshape(5 * depth, LANES), bottom.reshape(5 * depth, LANES)], axis=0)
    _, after, before, _ = _positions()
    to_next = jnp.full((depth, LANES), after, jnp.int32)
    to_prev = jnp.full((depth, LANES), before, jnp.int32)
    peers = chunk_ref.shape[0]
    for p in range(peers):
        chunk_ref[p, : FACE_ROWS * depth] = faces
        chunk_ref[p, FACE_ROWS * depth :] = jnp.where(to_next == p, up_pack, jnp.where(to_prev == p, down_pack, 0.0))


def _streamed(x, slab_width, relaxed_ref, rims_ref, low_ref, high_ref, hits_ref, depth, own=None):
    rows = depth if own is None else depth // 2
    part = (lambda ref, *idx: ref[idx]) if own is None else (lambda ref, *idx: ref[idx + (pl.ds(own, rows),)])
    lower = None if own is None else jnp.full((rows, LANES), own, jnp.int32) == 0

    def source(n, full):
        step_x, step_y, _ = velocity_table[n]
        get = (lambda ref, *idx: ref[idx]) if full else part
        width = depth if full else rows
        lane = lax.broadcasted_iota(jnp.int32, (width, LANES), 1)
        xs = x - step_x
        if xs < 0:
            return get(low_ref, upward.index(n))
        if xs >= slab_width:
            return get(high_ref, downward.index(n))
        t = get(relaxed_ref, n, xs)
        if step_y == 1:
            k = y_plus.index(n) * slab_width + xs
            t = jnp.where(lane == 0, _roll(get(rims_ref, 0), LANES - k, 1), _roll(t, 1, 1))
        elif step_y == -1:
            k = y_minus.index(n) * slab_width + xs
            t = jnp.where(lane == LANES - 1, _roll(get(rims_ref, 1), LANES - 1 - k, 1), _roll(t, LANES - 1, 1))
        return t

    out = []
    for n in range(19):
        step_z = velocity_table[n][2]
        if step_z == 0:
            out.append(source(n, own is None))
            continue
        t = _z_roll(source(n, True), step_z)
        if own is not None:
            t = jnp.where(lower, t[:rows], t[rows:])
        out.append(t)
    result = [out[0]]
    for n in range(1, 19):
        src = n - 1 + 2 * (n % 2)
        hit = jnp.bitwise_and(jnp.right_shift(part(hits_ref, x), src), 1) != 0
        result.append(jnp.where(hit, part(relaxed_ref, src, x), out[n]))
    return result


def _first_kernel(mine_ref, other_ref, *outs):
    relaxed_ref, chunk_ref = (outs[0], None) if outs[0].shape[0] == 19 else (None, outs[0])
    slab_width, half = mine_ref.shape[1], mine_ref.shape[2]
    depth = 2 * half
    lower = jnp.full((half, LANES), _positions()[3], jnp.int32) == 0

    def cells(x):
        out = []
        for m in range(19):
            a, b = mine_ref[m, x], other_ref[m, x]
            out.append(jnp.concatenate([jnp.where(lower, a, b), jnp.where(lower, b, a)], axis=0))
        return out

    _emit_relax(cells, slab_width, relaxed_ref, chunk_ref, depth)


def _middle_kernel(relaxed_ref, rims_ref, low_ref, high_ref, hits_ref, *outs):
    next_ref, chunk_ref = (outs[0], None) if outs[0].shape[0] == 19 else (None, outs[0])
    slab_width, depth = relaxed_ref.shape[1], relaxed_ref.shape[2]
    cells = lambda x: _streamed(x, slab_width, relaxed_ref, rims_ref, low_ref, high_ref, hits_ref, depth)
    _emit_relax(cells, slab_width, next_ref, chunk_ref, depth)


def _last_kernel(relaxed_ref, rims_ref, low_ref, high_ref, hits_ref, out_ref, density_ref):
    slab_width, depth = relaxed_ref.shape[1], relaxed_ref.shape[2]
    half = depth // 2
    lower = jnp.full((half, LANES), _positions()[3], jnp.int32) == 0
    own = pl.multiple_of(_positions()[3] * half, half)
    for x in range(slab_width):
        mine = _streamed(x, slab_width, relaxed_ref, rims_ref, low_ref, high_ref, hits_ref, depth, own=own)
        for m in range(19):
            out_ref[m, x] = mine[m]
        density_ref[x] = total_density(mine)


def _window_kernel(section, shift_ref, frac_ref, got_ref, low_ref, high_ref, rims_ref):
    peers, _, lanes = got_ref.shape
    depth = low_ref.shape[1]
    me_y, after, before, _ = _positions()
    offset = shift_ref[section]
    fraction = jnp.full((depth, lanes), frac_ref[section], jnp.int32).astype(jnp.float32) / 256.0
    keep = 1.0 - fraction
    flow_cells = peers * lanes
    anchor = me_y * lanes
    lane = lax.broadcasted_iota(jnp.int32, (depth, lanes), 1)

    def window(row0, start):
        start = (start + 2 * flow_cells) % flow_cells
        block = start // lanes
        off = start % lanes
        after = (block + 1) % peers
        shift = (lanes - off) % lanes
        first = pltpu.roll(got_ref[block, pl.ds(row0, depth), :], shift, 1)
        second = pltpu.roll(got_ref[after, pl.ds(row0, depth), :], shift, 1)
        return jnp.where(lane < lanes - off, first, second)

    for i, m in enumerate(upward):
        step_y = velocity_table[m][1]
        row0 = i * depth
        a = anchor - offset - step_y
        low_ref[i] = keep * window(row0, a) + fraction * window(row0, a - 1)
    for i, m in enumerate(downward):
        step_y = velocity_table[m][1]
        row0 = (5 + i) * depth
        c = anchor + offset - step_y
        high_ref[i] = fraction * window(row0, c + 1) + keep * window(row0, c)
    rims_ref[0] = got_ref[before, pl.ds(FACE_ROWS * depth, depth), :]
    rims_ref[1] = got_ref[after, pl.ds(FACE_ROWS * depth, depth), :]


def _vmem():
    return pl.BlockSpec(memory_space=pltpu.VMEM)


def _smem():
    return pl.BlockSpec(memory_space=pltpu.SMEM)


def _call(kernel, n_smem, n_vmem, out_shapes):
    return pl.pallas_call(
        kernel,
        out_shape=out_shapes,
        in_specs=[_smem()] * n_smem + [_vmem()] * n_vmem,
        out_specs=tuple(_vmem() for _ in out_shapes) if isinstance(out_shapes, tuple) else _vmem(),
    )


def _per_device(populations, le_shift, le_frac, links):
    n_members, slab_width, half_depth, row_span = populations.shape
    flow_cycle = lax.axis_size("gy")
    slab_cycle = lax.axis_size("gx")
    me_y = lax.axis_index("gy")
    me_z = lax.axis_index("gz")
    anchor = me_y * row_span

    other_states = lax.ppermute(populations, "gz", [(0, 1), (1, 0)])
    other_links = lax.ppermute(links, "gz", [(0, 1), (1, 0)])
    all_links = jnp.where(
        me_z == 0, jnp.concatenate([links, other_links], axis=1), jnp.concatenate([other_links, links], axis=1)
    )
    depth = 2 * half_depth
    hits = link_hits(all_links, anchor, row_span)

    f32 = jnp.float32
    full = jax.ShapeDtypeStruct((n_members, slab_width, depth, row_span), f32)
    chunk = jax.ShapeDtypeStruct((flow_cycle, (FACE_ROWS + 1) * depth, row_span), f32)
    ghost = jax.ShapeDtypeStruct((5, depth, row_span), f32)
    rims = jax.ShapeDtypeStruct((2, depth, row_span), f32)
    own = jax.ShapeDtypeStruct((n_members, slab_width, half_depth, row_span), f32)
    density = jax.ShapeDtypeStruct((slab_width, half_depth, row_span), f32)

    chunks = _call(_first_kernel, 0, 2, chunk)(populations, other_states)
    relaxed = _call(_first_kernel, 0, 2, full)(populations, other_states)
    for section in range(STEPS):
        got = lax.all_to_all(chunks, "gy", 0, 0, tiled=True)
        low_send, high_send, rim_pair = _call(functools.partial(_window_kernel, section), 2, 1, (ghost, ghost, rims))(
            le_shift, le_frac, got
        )
        low_ghost = lax.ppermute(low_send, "gx", [(i, (i + 1) % slab_cycle) for i in range(slab_cycle)])
        high_ghost = lax.ppermute(high_send, "gx", [(i, (i - 1) % slab_cycle) for i in range(slab_cycle)])
        if section + 1 < STEPS:
            args = (relaxed, rim_pair, low_ghost, high_ghost, hits)
            chunks = _call(_middle_kernel, 0, 5, chunk)(*args)
            relaxed = _call(_middle_kernel, 0, 5, full)(*args)
        else:
            final, dens = _call(_last_kernel, 0, 5, (own, density))(relaxed, rim_pair, low_ghost, high_ghost, hits)
    return (final, dens)


def solution(mesh):
    in_specs = (P(None, "gx", "gz", "gy"), P(), P(), P("gx", "gz", "gy"))
    out_specs = (P(None, "gx", "gz", "gy"), P("gx", "gz", "gy"))
    return jax.shard_map(_per_device, mesh=mesh, in_specs=in_specs, out_specs=out_specs, check_vma=False)
```

```python
import functools

import jax
import jax.numpy as jnp
from jax import lax
from jax.sharding import PartitionSpec as P
from jax.experimental import pallas as pl
from jax.experimental.pallas import tpu as pltpu


STEPS = 2


velocity_table = (
    (0, 0, 0),
    (1, 0, 0),
    (-1, 0, 0),
    (0, 1, 0),
    (0, -1, 0),
    (0, 0, 1),
    (0, 0, -1),
    (1, 1, 0),
    (-1, -1, 0),
    (1, -1, 0),
    (-1, 1, 0),
    (1, 0, 1),
    (-1, 0, -1),
    (1, 0, -1),
    (-1, 0, 1),
    (0, 1, 1),
    (0, -1, -1),
    (0, 1, -1),
    (0, -1, 1),
)
weight_table = (1.0 / 3.0,) + (1.0 / 18.0,) * 6 + (1.0 / 36.0,) * 12
upward = (1, 7, 9, 11, 13)
downward = (2, 8, 10, 12, 14)
y_plus = tuple(m for m in range(19) if velocity_table[m][1] == 1)
y_minus = tuple(m for m in range(19) if velocity_table[m][1] == -1)
relax_rate = 1.25
plane_speed = 0.08


def total_density(states):
    density = states[0]
    for member in range(1, 19):
        density = density + states[member]
    return density


def moments(states):
    density = total_density(states)
    velocity = []
    for dim_index in range(3):
        momentum = None
        for member in range(19):
            sign_part = velocity_table[member][dim_index]
            if sign_part == 1:
                momentum = states[member] if momentum is None else momentum + states[member]
            elif sign_part == -1:
                momentum = momentum - states[member]
        velocity.append(momentum / density)
    return (density, velocity)


def speed_square(velocity):
    return velocity[0] * velocity[0] + velocity[1] * velocity[1] + velocity[2] * velocity[2]


def equilibrium(member, density, velocity, speed_sq):
    projected = None
    for dim_index in range(3):
        sign_part = velocity_table[member][dim_index]
        if sign_part != 0:
            summand = velocity[dim_index] if sign_part > 0 else -velocity[dim_index]
            projected = summand if projected is None else projected + summand
    if projected is None:
        return weight_table[member] * density * (1.0 - 1.5 * speed_sq)
    return (
        weight_table[member]
        * density
        * (1.0 + 3.0 * projected + 4.5 * projected * projected - 1.5 * speed_sq)
    )


def relax(states):
    density, velocity = moments(states)
    speed_sq = speed_square(velocity)
    return [
        states[member]
        + relax_rate * (equilibrium(member, density, velocity, speed_sq) - states[member])
        for member in range(19)
    ]


def corrected(plane, members, sign_part):
    density, velocity = moments(plane)
    speed_sq = speed_square(velocity)
    moved = [velocity[0], velocity[1] + sign_part * plane_speed, velocity[2]]
    moved_sq = speed_square(moved)
    return jnp.stack(
        [
            plane[member]
            + equilibrium(member, density, moved, moved_sq)
            - equilibrium(member, density, velocity, speed_sq)
            for member in members
        ]
    )


def link_hits(links, anchor, row_span):
    cell_y = links // 19 - anchor
    member = links % 19
    by_member = (member[:, :, None, :] == jnp.arange(19, dtype=jnp.int32)[:, None]).astype(jnp.bfloat16)
    by_cell = (cell_y[:, :, :, None] == jnp.arange(row_span, dtype=jnp.int32)).astype(jnp.bfloat16)
    counts = jnp.einsum("xzml,xzly->xzym", by_member, by_cell, preferred_element_type=jnp.float32)
    bits = jnp.left_shift(1, jnp.arange(19, dtype=jnp.int32))
    return jnp.sum(jnp.where(counts > 0.5, bits, 0), axis=-1, dtype=jnp.int32)


LANES = 128
FACE_ROWS = 2 * 5


def _roll(t, shift, axis):
    if isinstance(shift, int):
        shift = shift % t.shape[axis]
        if shift == 0:
            return t
    return pltpu.roll(t, shift, axis)


def _z_roll(t, step):
    half = t.shape[0] // 2
    a, b = t[:half], t[half:]
    row = lax.broadcasted_iota(jnp.int32, a.shape, 0)
    if step == 1:
        ra, rb = _roll(a, 1, 0), _roll(b, 1, 0)
        edge = row == 0
    else:
        ra, rb = _roll(a, half - 1, 0), _roll(b, half - 1, 0)
        edge = row == half - 1
    return jnp.concatenate([jnp.where(edge, rb, ra), jnp.where(edge, ra, rb)], axis=0)


def _positions():
    flow_cycle = lax.axis_size("gy")
    me_y = lax.axis_index("gy")
    return me_y, (me_y + 1) % flow_cycle, (me_y - 1 + flow_cycle) % flow_cycle, lax.axis_index("gz")


def _emit_relax(cells_of_x, slab_width, relaxed_ref, chunk_ref, depth, mix=None):
    lane = lax.broadcasted_iota(jnp.int32, (depth, LANES), 1)
    up_pack = jnp.zeros((depth, LANES), jnp.float32)
    down_pack = jnp.zeros((depth, LANES), jnp.float32)
    top = bottom = None
    for x in range(slab_width):
        r = relax(cells_of_x(x))
        if relaxed_ref is not None:
            for m in range(19):
                relaxed_ref[m, x] = r[m]
        if chunk_ref is None:
            continue
        if x == slab_width - 1:
            top = corrected(r, upward, -1.0)
        if x == 0:
            bottom = corrected(r, downward, 1.0)
        for i, m in enumerate(y_plus):
            k = i * slab_width + x
            up_pack = jnp.where(lane == k, _roll(r[m], k + 1, 1), up_pack)
        for i, m in enumerate(y_minus):
            k = i * slab_width + x
            down_pack = jnp.where(lane == k, _roll(r[m], k, 1), down_pack)
    if chunk_ref is None:
        return
    _write_shares(chunk_ref, top, bottom, up_pack, down_pack, mix, depth)


def _write_shares(chunk_ref, top, bottom, up_pack, down_pack, mix, depth):
    shift_ref, frac_ref, section = mix
    peers = chunk_ref.shape[0]
    flow_cells = peers * LANES
    me_y, after, before, _ = _positions()
    offset = shift_ref[section]
    shape = (depth, LANES)
    lane = lax.broadcasted_iota(jnp.int32, shape, 1)
    fraction = jnp.full(shape, frac_ref[section], jnp.int32).astype(jnp.float32) / 256.0
    keep = 1.0 - fraction
    here = jnp.full(shape, me_y, jnp.int32)

    def rolled(tile, rel):
        off = (rel + 2 * flow_cells) % LANES
        return pltpu.roll(tile, (LANES - off) % LANES, 1), off

    def share(r, off, rel, p):
        start = (p * LANES + rel + 2 * flow_cells) % flow_cells
        block = jnp.full(shape, start // LANES, jnp.int32)
        first = lane < LANES - off
        mine = jnp.where(first, block, (block + 1) % peers) == here
        return jnp.where(mine, r, 0.0)

    lows, highs = [], []
    for i, m in enumerate(upward):
        rel = -offset - velocity_table[m][1]
        lows.append((rolled(top[i], rel), rel, rolled(top[i], rel - 1), rel - 1))
    for i, m in enumerate(downward):
        rel = offset - velocity_table[m][1]
        highs.append((rolled(bottom[i], rel + 1), rel + 1, rolled(bottom[i], rel), rel))
    for p in range(peers):
        for i, ((ra, oa), a, (rb, ob), b) in enumerate(lows):
            chunk_ref[p, pl.ds(i * depth, depth)] = keep * share(ra, oa, a, p) + fraction * share(rb, ob, b, p)
        for i, ((rc, oc), c, (rd, od), d) in enumerate(highs):
            chunk_ref[p, pl.ds((5 + i) * depth, depth)] = fraction * share(rc, oc, c, p) + keep * share(rd, od, d, p)
        up = jnp.full(shape, after, jnp.int32) == p
        down = jnp.full(shape, before, jnp.int32) == p
        chunk_ref[p, pl.ds(FACE_ROWS * depth, depth)] = jnp.where(up, up_pack, 0.0)
        chunk_ref[p, pl.ds((FACE_ROWS + 1) * depth, depth)] = jnp.where(down, down_pack, 0.0)


def _streamed(x, slab_width, relaxed_ref, rims_ref, low_ref, high_ref, hits_ref, depth, own=None):
    rows = depth if own is None else depth // 2
    part = (lambda ref, *idx: ref[idx]) if own is None else (lambda ref, *idx: ref[idx + (pl.ds(own, rows),)])
    lower = None if own is None else jnp.full((rows, LANES), own, jnp.int32) == 0

    def source(n, full):
        step_x, step_y, _ = velocity_table[n]
        get = (lambda ref, *idx: ref[idx]) if full else part
        width = depth if full else rows
        lane = lax.broadcasted_iota(jnp.int32, (width, LANES), 1)
        xs = x - step_x
        if xs < 0:
            return get(low_ref, upward.index(n))
        if xs >= slab_width:
            return get(high_ref, downward.index(n))
        t = get(relaxed_ref, n, xs)
        if step_y == 1:
            k = y_plus.index(n) * slab_width + xs
            t = jnp.where(lane == 0, _roll(get(rims_ref, 0), LANES - k, 1), _roll(t, 1, 1))
        elif step_y == -1:
            k = y_minus.index(n) * slab_width + xs
            t = jnp.where(lane == LANES - 1, _roll(get(rims_ref, 1), LANES - 1 - k, 1), _roll(t, LANES - 1, 1))
        return t

    out = []
    for n in range(19):
        step_z = velocity_table[n][2]
        if step_z == 0:
            out.append(source(n, own is None))
            continue
        t = _z_roll(source(n, True), step_z)
        if own is not None:
            t = jnp.where(lower, t[:rows], t[rows:])
        out.append(t)
    result = [out[0]]
    for n in range(1, 19):
        src = n - 1 + 2 * (n % 2)
        hit = jnp.bitwise_and(jnp.right_shift(part(hits_ref, x), src), 1) != 0
        result.append(jnp.where(hit, part(relaxed_ref, src, x), out[n]))
    return result


def _first_kernel(section, shift_ref, frac_ref, mine_ref, other_ref, *outs):
    relaxed_ref, chunk_ref = (outs[0], None) if outs[0].shape[0] == 19 else (None, outs[0])
    slab_width, half = mine_ref.shape[1], mine_ref.shape[2]
    depth = 2 * half
    lower = jnp.full((half, LANES), _positions()[3], jnp.int32) == 0

    def cells(x):
        out = []
        for m in range(19):
            a, b = mine_ref[m, x], other_ref[m, x]
            out.append(jnp.concatenate([jnp.where(lower, a, b), jnp.where(lower, b, a)], axis=0))
        return out

    _emit_relax(cells, slab_width, relaxed_ref, chunk_ref, depth, mix=(shift_ref, frac_ref, section))


def _middle_kernel(section, shift_ref, frac_ref, relaxed_ref, rims_ref, low_ref, high_ref, hits_ref, *outs):
    next_ref, chunk_ref = (outs[0], None) if outs[0].shape[0] == 19 else (None, outs[0])
    slab_width, depth = relaxed_ref.shape[1], relaxed_ref.shape[2]
    cells = lambda x: _streamed(x, slab_width, relaxed_ref, rims_ref, low_ref, high_ref, hits_ref, depth)
    _emit_relax(cells, slab_width, next_ref, chunk_ref, depth, mix=(shift_ref, frac_ref, section))


def _last_kernel(relaxed_ref, rims_ref, low_ref, high_ref, hits_ref, out_ref, density_ref):
    slab_width, depth = relaxed_ref.shape[1], relaxed_ref.shape[2]
    half = depth // 2
    lower = jnp.full((half, LANES), _positions()[3], jnp.int32) == 0
    own = pl.multiple_of(_positions()[3] * half, half)
    for x in range(slab_width):
        mine = _streamed(x, slab_width, relaxed_ref, rims_ref, low_ref, high_ref, hits_ref, depth, own=own)
        for m in range(19):
            out_ref[m, x] = mine[m]
        density_ref[x] = total_density(mine)


def _vmem():
    return pl.BlockSpec(memory_space=pltpu.VMEM)


def _smem():
    return pl.BlockSpec(memory_space=pltpu.SMEM)


def _call(kernel, n_smem, n_vmem, out_shapes):
    return pl.pallas_call(
        kernel,
        out_shape=out_shapes,
        in_specs=[_smem()] * n_smem + [_vmem()] * n_vmem,
        out_specs=tuple(_vmem() for _ in out_shapes) if isinstance(out_shapes, tuple) else _vmem(),
    )


def _per_device(populations, le_shift, le_frac, links):
    n_members, slab_width, half_depth, row_span = populations.shape
    flow_cycle = lax.axis_size("gy")
    slab_cycle = lax.axis_size("gx")
    me_y = lax.axis_index("gy")
    me_z = lax.axis_index("gz")
    anchor = me_y * row_span

    other_states = lax.ppermute(populations, "gz", [(0, 1), (1, 0)])
    other_links = lax.ppermute(links, "gz", [(0, 1), (1, 0)])
    all_links = jnp.where(
        me_z == 0, jnp.concatenate([links, other_links], axis=1), jnp.concatenate([other_links, links], axis=1)
    )
    depth = 2 * half_depth
    hits = link_hits(all_links, anchor, row_span)

    f32 = jnp.float32
    full = jax.ShapeDtypeStruct((n_members, slab_width, depth, row_span), f32)
    chunk = jax.ShapeDtypeStruct((flow_cycle, (FACE_ROWS + 2) * depth, row_span), f32)
    own = jax.ShapeDtypeStruct((n_members, slab_width, half_depth, row_span), f32)
    density = jax.ShapeDtypeStruct((slab_width, half_depth, row_span), f32)

    first_kernel = functools.partial(_first_kernel, 0)
    chunks = _call(first_kernel, 2, 2, chunk)(le_shift, le_frac, populations, other_states)
    relaxed = _call(first_kernel, 2, 2, full)(le_shift, le_frac, populations, other_states)
    for section in range(STEPS):
        got = lax.all_to_all(chunks, "gy", 0, 0, tiled=True)
        total = jnp.sum(got, axis=0)
        face_rows = 5 * depth
        low_send = total[:face_rows].reshape(5, depth, row_span)
        high_send = total[face_rows : 2 * face_rows].reshape(5, depth, row_span)
        rim_pair = total[2 * face_rows :].reshape(2, depth, row_span)
        low_ghost = lax.ppermute(low_send, "gx", [(i, (i + 1) % slab_cycle) for i in range(slab_cycle)])
        high_ghost = lax.ppermute(high_send, "gx", [(i, (i - 1) % slab_cycle) for i in range(slab_cycle)])
        if section + 1 < STEPS:
            args = (le_shift, le_frac, relaxed, rim_pair, low_ghost, high_ghost, hits)
            middle_kernel = functools.partial(_middle_kernel, section + 1)
            chunks = _call(middle_kernel, 2, 5, chunk)(*args)
            relaxed = _call(middle_kernel, 2, 5, full)(*args)
        else:
            final, dens = _call(_last_kernel, 0, 5, (own, density))(relaxed, rim_pair, low_ghost, high_ghost, hits)
    return (final, dens)


def solution(mesh):
    in_specs = (P(None, "gx", "gz", "gy"), P(), P(), P("gx", "gz", "gy"))
    out_specs = (P(None, "gx", "gz", "gy"), P("gx", "gz", "gy"))
    return jax.shard_map(_per_device, mesh=mesh, in_specs=in_specs, out_specs=out_specs, check_vma=False)
```

```python
import functools

import jax
import jax.numpy as jnp
from jax import lax
from jax.sharding import PartitionSpec as P
from jax.experimental import pallas as pl
from jax.experimental.pallas import tpu as pltpu


STEPS = 2


velocity_table = (
    (0, 0, 0),
    (1, 0, 0),
    (-1, 0, 0),
    (0, 1, 0),
    (0, -1, 0),
    (0, 0, 1),
    (0, 0, -1),
    (1, 1, 0),
    (-1, -1, 0),
    (1, -1, 0),
    (-1, 1, 0),
    (1, 0, 1),
    (-1, 0, -1),
    (1, 0, -1),
    (-1, 0, 1),
    (0, 1, 1),
    (0, -1, -1),
    (0, 1, -1),
    (0, -1, 1),
)
weight_table = (1.0 / 3.0,) + (1.0 / 18.0,) * 6 + (1.0 / 36.0,) * 12
upward = (1, 7, 9, 11, 13)
downward = (2, 8, 10, 12, 14)
y_plus = tuple(m for m in range(19) if velocity_table[m][1] == 1)
y_minus = tuple(m for m in range(19) if velocity_table[m][1] == -1)
relax_rate = 1.25
plane_speed = 0.08


def total_density(states):
    density = states[0]
    for member in range(1, 19):
        density = density + states[member]
    return density


def moments(states):
    density = total_density(states)
    velocity = []
    for dim_index in range(3):
        momentum = None
        for member in range(19):
            sign_part = velocity_table[member][dim_index]
            if sign_part == 1:
                momentum = states[member] if momentum is None else momentum + states[member]
            elif sign_part == -1:
                momentum = momentum - states[member]
        velocity.append(momentum / density)
    return (density, velocity)


def speed_square(velocity):
    return velocity[0] * velocity[0] + velocity[1] * velocity[1] + velocity[2] * velocity[2]


def equilibrium(member, density, velocity, speed_sq):
    projected = None
    for dim_index in range(3):
        sign_part = velocity_table[member][dim_index]
        if sign_part != 0:
            summand = velocity[dim_index] if sign_part > 0 else -velocity[dim_index]
            projected = summand if projected is None else projected + summand
    if projected is None:
        return weight_table[member] * density * (1.0 - 1.5 * speed_sq)
    return (
        weight_table[member]
        * density
        * (1.0 + 3.0 * projected + 4.5 * projected * projected - 1.5 * speed_sq)
    )


def relax(states):
    density, velocity = moments(states)
    speed_sq = speed_square(velocity)
    return [
        states[member]
        + relax_rate * (equilibrium(member, density, velocity, speed_sq) - states[member])
        for member in range(19)
    ]


def corrected(plane, members, sign_part):
    density, velocity = moments(plane)
    speed_sq = speed_square(velocity)
    moved = [velocity[0], velocity[1] + sign_part * plane_speed, velocity[2]]
    moved_sq = speed_square(moved)
    return jnp.stack(
        [
            plane[member]
            + equilibrium(member, density, moved, moved_sq)
            - equilibrium(member, density, velocity, speed_sq)
            for member in members
        ]
    )


def link_hits(links, anchor, row_span):
    cell_y = links // 19 - anchor
    member = links % 19
    by_member = (member[:, :, None, :] == jnp.arange(19, dtype=jnp.int32)[:, None]).astype(jnp.bfloat16)
    by_cell = (cell_y[:, :, :, None] == jnp.arange(row_span, dtype=jnp.int32)).astype(jnp.bfloat16)
    counts = jnp.einsum("xzml,xzly->xzym", by_member, by_cell, preferred_element_type=jnp.float32)
    bits = jnp.left_shift(1, jnp.arange(19, dtype=jnp.int32))
    return jnp.sum(jnp.where(counts > 0.5, bits, 0), axis=-1, dtype=jnp.int32)


LANES = 128
FACE_ROWS = 2 * 5


def _roll(t, shift, axis):
    if isinstance(shift, int):
        shift = shift % t.shape[axis]
        if shift == 0:
            return t
    return pltpu.roll(t, shift, axis)


def _z_roll(t, step):
    half = t.shape[0] // 2
    a, b = t[:half], t[half:]
    row = lax.broadcasted_iota(jnp.int32, a.shape, 0)
    if step == 1:
        ra, rb = _roll(a, 1, 0), _roll(b, 1, 0)
        edge = row == 0
    else:
        ra, rb = _roll(a, half - 1, 0), _roll(b, half - 1, 0)
        edge = row == half - 1
    return jnp.concatenate([jnp.where(edge, rb, ra), jnp.where(edge, ra, rb)], axis=0)


def _positions():
    flow_cycle = lax.axis_size("gy")
    me_y = lax.axis_index("gy")
    return me_y, (me_y + 1) % flow_cycle, (me_y - 1 + flow_cycle) % flow_cycle, lax.axis_index("gz")


def _emit_relax(cells_of_x, slab_width, relaxed_ref, chunk_ref, depth, mix=None):
    lane = lax.broadcasted_iota(jnp.int32, (depth, LANES), 1)
    up_pack = jnp.zeros((depth, LANES), jnp.float32)
    down_pack = jnp.zeros((depth, LANES), jnp.float32)
    top = bottom = None
    for x in range(slab_width):
        r = relax(cells_of_x(x))
        if relaxed_ref is not None:
            for m in range(19):
                relaxed_ref[m, x] = r[m]
        if chunk_ref is None:
            continue
        if x == slab_width - 1:
            top = corrected(r, upward, -1.0)
        if x == 0:
            bottom = corrected(r, downward, 1.0)
        for i, m in enumerate(y_plus):
            k = i * slab_width + x
            up_pack = jnp.where(lane == k, _roll(r[m], k + 1, 1), up_pack)
        for i, m in enumerate(y_minus):
            k = i * slab_width + x
            down_pack = jnp.where(lane == k, _roll(r[m], k, 1), down_pack)
    if chunk_ref is None:
        return
    _write_shares(chunk_ref, top, bottom, up_pack, down_pack, mix, depth)


def _write_shares(chunk_ref, top, bottom, up_pack, down_pack, mix, depth):
    shift_ref, frac_ref, section = mix
    peers = chunk_ref.shape[0]
    flow_cells = peers * LANES
    me_y, after, before, _ = _positions()
    offset = shift_ref[section]
    shape = (depth, LANES)
    lane = lax.broadcasted_iota(jnp.int32, shape, 1)
    fraction = jnp.full(shape, frac_ref[section], jnp.int32).astype(jnp.float32) / 256.0
    keep = 1.0 - fraction
    here = jnp.full(shape, me_y, jnp.int32)

    def rolled(tile, rel):
        off = (rel + 2 * flow_cells) % LANES
        return pltpu.roll(tile, (LANES - off) % LANES, 1), off

    def share(r, off, rel, p):
        start = (p * LANES + rel + 2 * flow_cells) % flow_cells
        block = jnp.full(shape, start // LANES, jnp.int32)
        first = lane < LANES - off
        mine = jnp.where(first, block, (block + 1) % peers) == here
        return jnp.where(mine, r, 0.0)

    lows, highs = [], []
    for i, m in enumerate(upward):
        rel = -offset - velocity_table[m][1]
        lows.append((rolled(top[i], rel), rel, rolled(top[i], rel - 1), rel - 1))
    for i, m in enumerate(downward):
        rel = offset - velocity_table[m][1]
        highs.append((rolled(bottom[i], rel + 1), rel + 1, rolled(bottom[i], rel), rel))
    for p in range(peers):
        for i, ((ra, oa), a, (rb, ob), b) in enumerate(lows):
            chunk_ref[p, pl.ds(i * depth, depth)] = keep * share(ra, oa, a, p) + fraction * share(rb, ob, b, p)
        for i, ((rc, oc), c, (rd, od), d) in enumerate(highs):
            chunk_ref[p, pl.ds((5 + i) * depth, depth)] = fraction * share(rc, oc, c, p) + keep * share(rd, od, d, p)
        up = jnp.full(shape, after, jnp.int32) == p
        down = jnp.full(shape, before, jnp.int32) == p
        chunk_ref[p, pl.ds(FACE_ROWS * depth, depth)] = jnp.where(up, up_pack, jnp.where(down, down_pack, 0.0))


def _streamed(x, slab_width, relaxed_ref, rims_ref, low_ref, high_ref, hits_ref, depth, own=None):
    rows = depth if own is None else depth // 2
    part = (lambda ref, *idx: ref[idx]) if own is None else (lambda ref, *idx: ref[idx + (pl.ds(own, rows),)])
    lower = None if own is None else jnp.full((rows, LANES), own, jnp.int32) == 0

    def source(n, full):
        step_x, step_y, _ = velocity_table[n]
        get = (lambda ref, *idx: ref[idx]) if full else part
        width = depth if full else rows
        lane = lax.broadcasted_iota(jnp.int32, (width, LANES), 1)
        xs = x - step_x
        if xs < 0:
            return get(low_ref, upward.index(n))
        if xs >= slab_width:
            return get(high_ref, downward.index(n))
        t = get(relaxed_ref, n, xs)
        if step_y == 1:
            k = y_plus.index(n) * slab_width + xs
            t = jnp.where(lane == 0, _roll(get(rims_ref, 0), LANES - k, 1), _roll(t, 1, 1))
        elif step_y == -1:
            k = y_minus.index(n) * slab_width + xs
            t = jnp.where(lane == LANES - 1, _roll(get(rims_ref, 1), LANES - 1 - k, 1), _roll(t, LANES - 1, 1))
        return t

    out = []
    for n in range(19):
        step_z = velocity_table[n][2]
        if step_z == 0:
            out.append(source(n, own is None))
            continue
        t = _z_roll(source(n, True), step_z)
        if own is not None:
            t = jnp.where(lower, t[:rows], t[rows:])
        out.append(t)
    result = [out[0]]
    for n in range(1, 19):
        src = n - 1 + 2 * (n % 2)
        hit = jnp.bitwise_and(jnp.right_shift(part(hits_ref, x), src), 1) != 0
        result.append(jnp.where(hit, part(relaxed_ref, src, x), out[n]))
    return result


def _first_kernel(section, shift_ref, frac_ref, mine_ref, other_ref, *outs):
    relaxed_ref, chunk_ref = (outs[0], None) if outs[0].shape[0] == 19 else (None, outs[0])
    slab_width, half = mine_ref.shape[1], mine_ref.shape[2]
    depth = 2 * half
    lower = jnp.full((half, LANES), _positions()[3], jnp.int32) == 0

    def cells(x):
        out = []
        for m in range(19):
            a, b = mine_ref[m, x], other_ref[m, x]
            out.append(jnp.concatenate([jnp.where(lower, a, b), jnp.where(lower, b, a)], axis=0))
        return out

    _emit_relax(cells, slab_width, relaxed_ref, chunk_ref, depth, mix=(shift_ref, frac_ref, section))


def _middle_kernel(section, shift_ref, frac_ref, relaxed_ref, rims_ref, low_ref, high_ref, hits_ref, *outs):
    next_ref, chunk_ref = (outs[0], None) if outs[0].shape[0] == 19 else (None, outs[0])
    slab_width, depth = relaxed_ref.shape[1], relaxed_ref.shape[2]
    cells = lambda x: _streamed(x, slab_width, relaxed_ref, rims_ref, low_ref, high_ref, hits_ref, depth)
    _emit_relax(cells, slab_width, next_ref, chunk_ref, depth, mix=(shift_ref, frac_ref, section))


def _last_kernel(relaxed_ref, rims_ref, low_ref, high_ref, hits_ref, out_ref, density_ref):
    slab_width, depth = relaxed_ref.shape[1], relaxed_ref.shape[2]
    half = depth // 2
    lower = jnp.full((half, LANES), _positions()[3], jnp.int32) == 0
    own = pl.multiple_of(_positions()[3] * half, half)
    for x in range(slab_width):
        mine = _streamed(x, slab_width, relaxed_ref, rims_ref, low_ref, high_ref, hits_ref, depth, own=own)
        for m in range(19):
            out_ref[m, x] = mine[m]
        density_ref[x] = total_density(mine)


def _vmem():
    return pl.BlockSpec(memory_space=pltpu.VMEM)


def _smem():
    return pl.BlockSpec(memory_space=pltpu.SMEM)


def _call(kernel, n_smem, n_vmem, out_shapes):
    return pl.pallas_call(
        kernel,
        out_shape=out_shapes,
        in_specs=[_smem()] * n_smem + [_vmem()] * n_vmem,
        out_specs=tuple(_vmem() for _ in out_shapes) if isinstance(out_shapes, tuple) else _vmem(),
    )


def _per_device(populations, le_shift, le_frac, links):
    n_members, slab_width, half_depth, row_span = populations.shape
    flow_cycle = lax.axis_size("gy")
    slab_cycle = lax.axis_size("gx")
    me_y = lax.axis_index("gy")
    me_z = lax.axis_index("gz")
    anchor = me_y * row_span

    other_states = lax.ppermute(populations, "gz", [(0, 1), (1, 0)])
    other_links = lax.ppermute(links, "gz", [(0, 1), (1, 0)])
    all_links = jnp.where(
        me_z == 0, jnp.concatenate([links, other_links], axis=1), jnp.concatenate([other_links, links], axis=1)
    )
    depth = 2 * half_depth
    hits = link_hits(all_links, anchor, row_span)

    f32 = jnp.float32
    full = jax.ShapeDtypeStruct((n_members, slab_width, depth, row_span), f32)
    chunk = jax.ShapeDtypeStruct((flow_cycle, (FACE_ROWS + 1) * depth, row_span), f32)
    own = jax.ShapeDtypeStruct((n_members, slab_width, half_depth, row_span), f32)
    density = jax.ShapeDtypeStruct((slab_width, half_depth, row_span), f32)

    first_kernel = functools.partial(_first_kernel, 0)
    chunks = _call(first_kernel, 2, 2, chunk)(le_shift, le_frac, populations, other_states)
    relaxed = _call(first_kernel, 2, 2, full)(le_shift, le_frac, populations, other_states)
    for section in range(STEPS):
        got = lax.all_to_all(chunks, "gy", 0, 0, tiled=True)
        face_rows = 5 * depth
        total = jnp.sum(got[:, : 2 * face_rows], axis=0)
        low_send = total[:face_rows].reshape(5, depth, row_span)
        high_send = total[face_rows:].reshape(5, depth, row_span)
        rim_rows = got[:, 2 * face_rows :]
        rim_pair = jnp.stack(
            [
                lax.dynamic_index_in_dim(rim_rows, (me_y - 1 + flow_cycle) % flow_cycle, 0, keepdims=False),
                lax.dynamic_index_in_dim(rim_rows, (me_y + 1) % flow_cycle, 0, keepdims=False),
            ]
        )
        low_ghost = lax.ppermute(low_send, "gx", [(i, (i + 1) % slab_cycle) for i in range(slab_cycle)])
        high_ghost = lax.ppermute(high_send, "gx", [(i, (i - 1) % slab_cycle) for i in range(slab_cycle)])
        if section + 1 < STEPS:
            args = (le_shift, le_frac, relaxed, rim_pair, low_ghost, high_ghost, hits)
            middle_kernel = functools.partial(_middle_kernel, section + 1)
            chunks = _call(middle_kernel, 2, 5, chunk)(*args)
            relaxed = _call(middle_kernel, 2, 5, full)(*args)
        else:
            final, dens = _call(_last_kernel, 0, 5, (own, density))(relaxed, rim_pair, low_ghost, high_ghost, hits)
    return (final, dens)


def solution(mesh):
    in_specs = (P(None, "gx", "gz", "gy"), P(), P(), P("gx", "gz", "gy"))
    out_specs = (P(None, "gx", "gz", "gy"), P("gx", "gz", "gy"))
    return jax.shard_map(_per_device, mesh=mesh, in_specs=in_specs, out_specs=out_specs, check_vma=False)
```

```python
import functools

import jax
import jax.numpy as jnp
from jax import lax
from jax.sharding import PartitionSpec as P
from jax.experimental import pallas as pl
from jax.experimental.pallas import tpu as pltpu


STEPS = 2


velocity_table = (
    (0, 0, 0),
    (1, 0, 0),
    (-1, 0, 0),
    (0, 1, 0),
    (0, -1, 0),
    (0, 0, 1),
    (0, 0, -1),
    (1, 1, 0),
    (-1, -1, 0),
    (1, -1, 0),
    (-1, 1, 0),
    (1, 0, 1),
    (-1, 0, -1),
    (1, 0, -1),
    (-1, 0, 1),
    (0, 1, 1),
    (0, -1, -1),
    (0, 1, -1),
    (0, -1, 1),
)
weight_table = (1.0 / 3.0,) + (1.0 / 18.0,) * 6 + (1.0 / 36.0,) * 12
upward = (1, 7, 9, 11, 13)
downward = (2, 8, 10, 12, 14)
y_plus = tuple(m for m in range(19) if velocity_table[m][1] == 1)
y_minus = tuple(m for m in range(19) if velocity_table[m][1] == -1)
relax_rate = 1.25
plane_speed = 0.08


def total_density(states):
    density = states[0]
    for member in range(1, 19):
        density = density + states[member]
    return density


def moments(states):
    density = total_density(states)
    velocity = []
    for dim_index in range(3):
        momentum = None
        for member in range(19):
            sign_part = velocity_table[member][dim_index]
            if sign_part == 1:
                momentum = states[member] if momentum is None else momentum + states[member]
            elif sign_part == -1:
                momentum = momentum - states[member]
        velocity.append(momentum / density)
    return (density, velocity)


def speed_square(velocity):
    return velocity[0] * velocity[0] + velocity[1] * velocity[1] + velocity[2] * velocity[2]


def equilibrium(member, density, velocity, speed_sq):
    projected = None
    for dim_index in range(3):
        sign_part = velocity_table[member][dim_index]
        if sign_part != 0:
            summand = velocity[dim_index] if sign_part > 0 else -velocity[dim_index]
            projected = summand if projected is None else projected + summand
    if projected is None:
        return weight_table[member] * density * (1.0 - 1.5 * speed_sq)
    return (
        weight_table[member]
        * density
        * (1.0 + 3.0 * projected + 4.5 * projected * projected - 1.5 * speed_sq)
    )


def relax(states):
    density, velocity = moments(states)
    speed_sq = speed_square(velocity)
    return [
        states[member]
        + relax_rate * (equilibrium(member, density, velocity, speed_sq) - states[member])
        for member in range(19)
    ]


def corrected(plane, members, sign_part):
    density, velocity = moments(plane)
    speed_sq = speed_square(velocity)
    moved = [velocity[0], velocity[1] + sign_part * plane_speed, velocity[2]]
    moved_sq = speed_square(moved)
    return jnp.stack(
        [
            plane[member]
            + equilibrium(member, density, moved, moved_sq)
            - equilibrium(member, density, velocity, speed_sq)
            for member in members
        ]
    )


def link_hits(links, anchor, row_span):
    cell_y = links // 19 - anchor
    member = links % 19
    by_member = (member[:, :, None, :] == jnp.arange(19, dtype=jnp.int32)[:, None]).astype(jnp.bfloat16)
    by_cell = (cell_y[:, :, :, None] == jnp.arange(row_span, dtype=jnp.int32)).astype(jnp.bfloat16)
    counts = jnp.einsum("xzml,xzly->xzym", by_member, by_cell, preferred_element_type=jnp.float32)
    bits = jnp.left_shift(1, jnp.arange(19, dtype=jnp.int32))
    return jnp.sum(jnp.where(counts > 0.5, bits, 0), axis=-1, dtype=jnp.int32)


LANES = 128
FACE_ROWS = 2 * 5


def _roll(t, shift, axis):
    if isinstance(shift, int):
        shift = shift % t.shape[axis]
        if shift == 0:
            return t
    return pltpu.roll(t, shift, axis)


def _z_roll(t, step):
    half = t.shape[0] // 2
    a, b = t[:half], t[half:]
    row = lax.broadcasted_iota(jnp.int32, a.shape, 0)
    if step == 1:
        ra, rb = _roll(a, 1, 0), _roll(b, 1, 0)
        edge = row == 0
    else:
        ra, rb = _roll(a, half - 1, 0), _roll(b, half - 1, 0)
        edge = row == half - 1
    return jnp.concatenate([jnp.where(edge, rb, ra), jnp.where(edge, ra, rb)], axis=0)


def _positions():
    flow_cycle = lax.axis_size("gy")
    me_y = lax.axis_index("gy")
    return me_y, (me_y + 1) % flow_cycle, (me_y - 1 + flow_cycle) % flow_cycle, lax.axis_index("gz")


def _emit_relax(cells_of_x, slab_width, relaxed_ref, chunk_ref, depth, mix=None):
    lane = lax.broadcasted_iota(jnp.int32, (depth, LANES), 1)
    up_pack = jnp.zeros((depth, LANES), jnp.float32)
    down_pack = jnp.zeros((depth, LANES), jnp.float32)
    top = bottom = None
    edge_only = relaxed_ref is None and chunk_ref is not None
    edges = [jnp.zeros((depth, LANES), jnp.float32) for _ in range(19)]
    for x in range(slab_width):
        cells = cells_of_x(x)
        if edge_only and 0 < x < slab_width - 1:
            low_lane, high_lane = 2 * (x - 1), 2 * (x - 1) + 1
            for m in range(19):
                t = jnp.where(lane == low_lane, _roll(cells[m], low_lane, 1), edges[m])
                edges[m] = jnp.where(lane == high_lane, _roll(cells[m], high_lane + 1, 1), t)
            continue
        r = relax(cells)
        if relaxed_ref is not None:
            for m in range(19):
                relaxed_ref[m, x] = r[m]
        if chunk_ref is None:
            continue
        if x == slab_width - 1:
            top = corrected(r, upward, -1.0)
        if x == 0:
            bottom = corrected(r, downward, 1.0)
        for i, m in enumerate(y_plus):
            k = i * slab_width + x
            up_pack = jnp.where(lane == k, _roll(r[m], k + 1, 1), up_pack)
        for i, m in enumerate(y_minus):
            k = i * slab_width + x
            down_pack = jnp.where(lane == k, _roll(r[m], k, 1), down_pack)
    if chunk_ref is None:
        return
    if edge_only:
        packed = relax(edges)
        for x in range(1, slab_width - 1):
            low_lane, high_lane = 2 * (x - 1), 2 * (x - 1) + 1
            for i, m in enumerate(y_plus):
                k = i * slab_width + x
                up_pack = jnp.where(lane == k, _roll(packed[m], k - high_lane, 1), up_pack)
            for i, m in enumerate(y_minus):
                k = i * slab_width + x
                down_pack = jnp.where(lane == k, _roll(packed[m], k - low_lane, 1), down_pack)
    _write_shares(chunk_ref, top, bottom, up_pack, down_pack, mix, depth)


def _write_shares(chunk_ref, top, bottom, up_pack, down_pack, mix, depth):
    shift_ref, frac_ref, section = mix
    peers = chunk_ref.shape[0]
    flow_cells = peers * LANES
    me_y, after, before, _ = _positions()
    offset = shift_ref[section]
    shape = (depth, LANES)
    lane = lax.broadcasted_iota(jnp.int32, shape, 1)
    fraction = jnp.full(shape, frac_ref[section], jnp.int32).astype(jnp.float32) / 256.0
    keep = 1.0 - fraction
    here = jnp.full(shape, me_y, jnp.int32)

    def rolled(tile, rel):
        off = (rel + 2 * flow_cells) % LANES
        return pltpu.roll(tile, (LANES - off) % LANES, 1), off

    def share(r, off, rel, p):
        start = (p * LANES + rel + 2 * flow_cells) % flow_cells
        block = jnp.full(shape, start // LANES, jnp.int32)
        first = lane < LANES - off
        mine = jnp.where(first, block, (block + 1) % peers) == here
        return jnp.where(mine, r, 0.0)

    lows, highs = [], []
    for i, m in enumerate(upward):
        rel = -offset - velocity_table[m][1]
        lows.append((rolled(top[i], rel), rel, rolled(top[i], rel - 1), rel - 1))
    for i, m in enumerate(downward):
        rel = offset - velocity_table[m][1]
        highs.append((rolled(bottom[i], rel + 1), rel + 1, rolled(bottom[i], rel), rel))
    for p in range(peers):
        for i, ((ra, oa), a, (rb, ob), b) in enumerate(lows):
            chunk_ref[p, pl.ds(i * depth, depth)] = keep * share(ra, oa, a, p) + fraction * share(rb, ob, b, p)
        for i, ((rc, oc), c, (rd, od), d) in enumerate(highs):
            chunk_ref[p, pl.ds((5 + i) * depth, depth)] = fraction * share(rc, oc, c, p) + keep * share(rd, od, d, p)
        up = jnp.full(shape, after, jnp.int32) == p
        down = jnp.full(shape, before, jnp.int32) == p
        chunk_ref[p, pl.ds(FACE_ROWS * depth, depth)] = jnp.where(up, up_pack, jnp.where(down, down_pack, 0.0))


def _streamed(x, slab_width, relaxed_ref, rims_ref, low_ref, high_ref, hits_ref, depth, own=None):
    rows = depth if own is None else depth // 2
    part = (lambda ref, *idx: ref[idx]) if own is None else (lambda ref, *idx: ref[idx + (pl.ds(own, rows),)])
    lower = None if own is None else jnp.full((rows, LANES), own, jnp.int32) == 0

    def source(n, full):
        step_x, step_y, _ = velocity_table[n]
        get = (lambda ref, *idx: ref[idx]) if full else part
        width = depth if full else rows
        lane = lax.broadcasted_iota(jnp.int32, (width, LANES), 1)
        xs = x - step_x
        if xs < 0:
            return get(low_ref, upward.index(n))
        if xs >= slab_width:
            return get(high_ref, downward.index(n))
        t = get(relaxed_ref, n, xs)
        if step_y == 1:
            k = y_plus.index(n) * slab_width + xs
            t = jnp.where(lane == 0, _roll(get(rims_ref, 0), LANES - k, 1), _roll(t, 1, 1))
        elif step_y == -1:
            k = y_minus.index(n) * slab_width + xs
            t = jnp.where(lane == LANES - 1, _roll(get(rims_ref, 1), LANES - 1 - k, 1), _roll(t, LANES - 1, 1))
        return t

    out = []
    for n in range(19):
        step_z = velocity_table[n][2]
        if step_z == 0:
            out.append(source(n, own is None))
            continue
        t = _z_roll(source(n, True), step_z)
        if own is not None:
            t = jnp.where(lower, t[:rows], t[rows:])
        out.append(t)
    result = [out[0]]
    for n in range(1, 19):
        src = n - 1 + 2 * (n % 2)
        hit = jnp.bitwise_and(jnp.right_shift(part(hits_ref, x), src), 1) != 0
        result.append(jnp.where(hit, part(relaxed_ref, src, x), out[n]))
    return result


def _first_kernel(section, shift_ref, frac_ref, mine_ref, other_ref, *outs):
    relaxed_ref, chunk_ref = (outs[0], None) if outs[0].shape[0] == 19 else (None, outs[0])
    slab_width, half = mine_ref.shape[1], mine_ref.shape[2]
    depth = 2 * half
    lower = jnp.full((half, LANES), _positions()[3], jnp.int32) == 0

    def cells(x):
        out = []
        for m in range(19):
            a, b = mine_ref[m, x], other_ref[m, x]
            out.append(jnp.concatenate([jnp.where(lower, a, b), jnp.where(lower, b, a)], axis=0))
        return out

    _emit_relax(cells, slab_width, relaxed_ref, chunk_ref, depth, mix=(shift_ref, frac_ref, section))


def _middle_kernel(section, shift_ref, frac_ref, relaxed_ref, rims_ref, low_ref, high_ref, hits_ref, *outs):
    next_ref, chunk_ref = (outs[0], None) if outs[0].shape[0] == 19 else (None, outs[0])
    slab_width, depth = relaxed_ref.shape[1], relaxed_ref.shape[2]
    cells = lambda x: _streamed(x, slab_width, relaxed_ref, rims_ref, low_ref, high_ref, hits_ref, depth)
    _emit_relax(cells, slab_width, next_ref, chunk_ref, depth, mix=(shift_ref, frac_ref, section))


def _last_kernel(relaxed_ref, rims_ref, low_ref, high_ref, hits_ref, out_ref, density_ref):
    slab_width, depth = relaxed_ref.shape[1], relaxed_ref.shape[2]
    half = depth // 2
    lower = jnp.full((half, LANES), _positions()[3], jnp.int32) == 0
    own = pl.multiple_of(_positions()[3] * half, half)
    for x in range(slab_width):
        mine = _streamed(x, slab_width, relaxed_ref, rims_ref, low_ref, high_ref, hits_ref, depth, own=own)
        for m in range(19):
            out_ref[m, x] = mine[m]
        density_ref[x] = total_density(mine)


def _vmem():
    return pl.BlockSpec(memory_space=pltpu.VMEM)


def _smem():
    return pl.BlockSpec(memory_space=pltpu.SMEM)


def _call(kernel, n_smem, n_vmem, out_shapes):
    return pl.pallas_call(
        kernel,
        out_shape=out_shapes,
        in_specs=[_smem()] * n_smem + [_vmem()] * n_vmem,
        out_specs=tuple(_vmem() for _ in out_shapes) if isinstance(out_shapes, tuple) else _vmem(),
    )


def _per_device(populations, le_shift, le_frac, links):
    n_members, slab_width, half_depth, row_span = populations.shape
    flow_cycle = lax.axis_size("gy")
    slab_cycle = lax.axis_size("gx")
    me_y = lax.axis_index("gy")
    me_z = lax.axis_index("gz")
    anchor = me_y * row_span

    other_states = lax.ppermute(populations, "gz", [(0, 1), (1, 0)])
    other_links = lax.ppermute(links, "gz", [(0, 1), (1, 0)])
    all_links = jnp.where(
        me_z == 0, jnp.concatenate([links, other_links], axis=1), jnp.concatenate([other_links, links], axis=1)
    )
    depth = 2 * half_depth
    hits = link_hits(all_links, anchor, row_span)

    f32 = jnp.float32
    full = jax.ShapeDtypeStruct((n_members, slab_width, depth, row_span), f32)
    chunk = jax.ShapeDtypeStruct((flow_cycle, (FACE_ROWS + 1) * depth, row_span), f32)
    own = jax.ShapeDtypeStruct((n_members, slab_width, half_depth, row_span), f32)
    density = jax.ShapeDtypeStruct((slab_width, half_depth, row_span), f32)

    first_kernel = functools.partial(_first_kernel, 0)
    chunks = _call(first_kernel, 2, 2, chunk)(le_shift, le_frac, populations, other_states)
    relaxed = _call(first_kernel, 2, 2, full)(le_shift, le_frac, populations, other_states)
    for section in range(STEPS):
        got = lax.all_to_all(chunks, "gy", 0, 0, tiled=True)
        face_rows = 5 * depth
        total = jnp.sum(got[:, : 2 * face_rows], axis=0)
        low_send = total[:face_rows].reshape(5, depth, row_span)
        high_send = total[face_rows:].reshape(5, depth, row_span)
        rim_rows = got[:, 2 * face_rows :]
        rim_pair = jnp.stack(
            [
                lax.dynamic_index_in_dim(rim_rows, (me_y - 1 + flow_cycle) % flow_cycle, 0, keepdims=False),
                lax.dynamic_index_in_dim(rim_rows, (me_y + 1) % flow_cycle, 0, keepdims=False),
            ]
        )
        low_ghost = lax.ppermute(low_send, "gx", [(i, (i + 1) % slab_cycle) for i in range(slab_cycle)])
        high_ghost = lax.ppermute(high_send, "gx", [(i, (i - 1) % slab_cycle) for i in range(slab_cycle)])
        if section + 1 < STEPS:
            args = (le_shift, le_frac, relaxed, rim_pair, low_ghost, high_ghost, hits)
            middle_kernel = functools.partial(_middle_kernel, section + 1)
            chunks = _call(middle_kernel, 2, 5, chunk)(*args)
            relaxed = _call(middle_kernel, 2, 5, full)(*args)
        else:
            final, dens = _call(_last_kernel, 0, 5, (own, density))(relaxed, rim_pair, low_ghost, high_ghost, hits)
    return (final, dens)


def solution(mesh):
    in_specs = (P(None, "gx", "gz", "gy"), P(), P(), P("gx", "gz", "gy"))
    out_specs = (P(None, "gx", "gz", "gy"), P("gx", "gz", "gy"))
    return jax.shard_map(_per_device, mesh=mesh, in_specs=in_specs, out_specs=out_specs, check_vma=False)
```
